32 devices in a mesh: grp: 2 (over x), gx: 16 (over z, y, core).
Axes of the slice: x: 2, y: 2, z: 4, core: 2. Of those that a mesh axis runs over, the one named last changes fastest.
Arguments:
- volume: float32 [1024, 128, 128], P(('grp', 'gx')), parts along dimension 0, may hold values from -6 to 6
- level_set: float32 [1024, 128, 128], P(('grp', 'gx')), parts along dimension 0, may hold values from -6 to 6
Outputs:
- edge_map: float32 [1024, 128, 128], P(('grp', 'gx')), parts along dimension 0
- advanced: float32 [1024, 128, 128], P(('grp', 'gx')), parts along dimension 0
The draws below stay inside these ranges and needn't reach their ends.
There are 2 independent parts, one for each index of `grp`. The reference program is written for one: setup_inputs(seed, part) draws one part's arguments, and reference() takes and returns one part's arrays. A program takes and returns all parts, laid end to end along the dimension named above; each array names one. Nothing has to cross between parts.
All inputs are finite; a program needn't handle non-finite values.
Results may differ from the reference program's by a relative error of at most 0.00002.
Values sent between devices are 32-bit elements; how exact they have to be, the bound alone decides.
No kernel may reach another device: no remote copies, remote signals or barrier semaphores. Data moves between devices by JAX's collectives and lax.ppermute only.
A program may use at most 64 MiB of HBM per device.

```python
import math
import jax
import jax.numpy as jnp
from jax import lax

NY = 128
NZ = 128
RADIUS = 12
NX = 512


def levels(rng, dims, cuts, smallest, largest):
    loudness = 1.0
    for dim, blocks in cuts:
        steps = jax.random.uniform(jax.random.fold_in(jax.random.fold_in(rng, 6), dim), (blocks,), jnp.float32, smallest / len(cuts), largest / len(cuts))
        loudness = loudness * jnp.repeat(jnp.exp(steps), dims[dim] // blocks).reshape((-1,) + (1,) * (len(dims) - 1 - dim))
    return loudness


def scatter_about(rng, shape, scale, limit, split=(), held_as=jnp.bfloat16):
    values = jax.random.normal(rng, shape, jnp.float32) * scale
    if len(split) > 0:
        values = levels(rng, shape, split, -0.22, 0.18) * values
    return jnp.clip(values, min=-limit, max=limit).astype(held_as)


def setup_inputs(seed: int = 0, part: int = 0) -> dict:
    seeds = jax.random.split(jax.random.key(seed), 3)
    own_keys = jax.random.split(jax.random.fold_in(seeds[2], part), 3)
    volume = scatter_about(own_keys[0], (NX, NY, NZ), 1.0, 6.0, ((0, 16),), jnp.float32)
    level_set = scatter_about(own_keys[1], (NX, NY, NZ), 1.0, 6.0, ((0, 16),), jnp.float32)
    return {"volume": volume, "level_set": level_set}


def blur_taps():
    raw = [math.exp(-(offset * offset) / 18.0) for offset in range(-RADIUS, RADIUS + 1)]
    total = sum(raw)
    return [value / total for value in raw]


def pad_axis(array, axis, width):
    widths = [(0, 0), (0, 0), (0, 0)]
    widths[axis] = (width, width)
    return jnp.pad(array, widths)


def blur_padded(padded, axis, count):
    taps = blur_taps()
    result = taps[0] * lax.slice_in_dim(padded, 0, count, axis=axis)
    for offset in range(1, len(taps)):
        result = result + taps[offset] * lax.slice_in_dim(padded, offset, offset + count, axis=axis)
    return result


def central_grads(padded):
    inner = padded[1:-1]
    side = jnp.pad(inner, ((0, 0), (1, 1), (1, 1)))
    grad_x = (padded[2:] - padded[:-2]) * 0.5
    grad_y = (side[:, 2:, 1:-1] - side[:, :-2, 1:-1]) * 0.5
    grad_z = (side[:, 1:-1, 2:] - side[:, 1:-1, :-2]) * 0.5
    return grad_x, grad_y, grad_z


def edge_from(padded):
    grad_x, grad_y, grad_z = central_grads(padded)
    return 1.0 / (1.0 + 6000.0 * (grad_x * grad_x + grad_y * grad_y + grad_z * grad_z))


def weno(first, second, third, fourth, fifth):
    cand_one = (2.0 * first - 7.0 * second + 11.0 * third) / 6.0
    cand_two = (-second + 5.0 * third + 2.0 * fourth) / 6.0
    cand_three = (2.0 * third + 5.0 * fourth - fifth) / 6.0
    part_a = first - 2.0 * second + third
    part_b = first - 4.0 * second + 3.0 * third
    smooth_one = (13.0 / 12.0) * part_a * part_a + 0.25 * part_b * part_b
    part_a = second - 2.0 * third + fourth
    part_b = second - fourth
    smooth_two = (13.0 / 12.0) * part_a * part_a + 0.25 * part_b * part_b
    part_a = third - 2.0 * fourth + fifth
    part_b = 3.0 * third - 4.0 * fourth + fifth
    smooth_three = (13.0 / 12.0) * part_a * part_a + 0.25 * part_b * part_b
    denom_one = 1e-6 + smooth_one
    denom_two = 1e-6 + smooth_two
    denom_three = 1e-6 + smooth_three
    weight_one = 0.1 / (denom_one * denom_one)
    weight_two = 0.6 / (denom_two * denom_two)
    weight_three = 0.3 / (denom_three * denom_three)
    return (weight_one * cand_one + weight_two * cand_two + weight_three * cand_three) / (weight_one + weight_two + weight_three)


def upwind(padded, axis, count):
    diffs = lax.slice_in_dim(padded, 1, padded.shape[axis], axis=axis) - lax.slice_in_dim(padded, 0, padded.shape[axis] - 1, axis=axis)
    pieces = [lax.slice_in_dim(diffs, offset, offset + count, axis=axis) for offset in range(6)]
    minus = weno(pieces[0], pieces[1], pieces[2], pieces[3], pieces[4])
    plus = weno(pieces[5], pieces[4], pieces[3], pieces[2], pieces[1])
    return minus, plus


def rates(padded, edge, slope):
    count = padded.shape[0] - 6
    field = padded[3:-3]
    rows_y = field.shape[1]
    rows_z = field.shape[2]
    minus_x, plus_x = upwind(padded, 0, count)
    minus_y, plus_y = upwind(pad_axis(field, 1, 3), 1, rows_y)
    minus_z, plus_z = upwind(pad_axis(field, 2, 3), 2, rows_z)
    near = jnp.pad(padded[2:-2], ((0, 0), (1, 1), (1, 1)))

    def beside_all(step_x, step_y, step_z):
        return near[1 + step_x:1 + step_x + count, 1 + step_y:1 + step_y + rows_y, 1 + step_z:1 + step_z + rows_z]

    centre = beside_all(0, 0, 0)
    first_x = (beside_all(1, 0, 0) - beside_all(-1, 0, 0)) * 0.5
    first_y = (beside_all(0, 1, 0) - beside_all(0, -1, 0)) * 0.5
    first_z = (beside_all(0, 0, 1) - beside_all(0, 0, -1)) * 0.5
    second_xx = beside_all(1, 0, 0) - 2.0 * centre + beside_all(-1, 0, 0)
    second_yy = beside_all(0, 1, 0) - 2.0 * centre + beside_all(0, -1, 0)
    second_zz = beside_all(0, 0, 1) - 2.0 * centre + beside_all(0, 0, -1)
    mixed_xy = (beside_all(1, 1, 0) - beside_all(1, -1, 0) - beside_all(-1, 1, 0) + beside_all(-1, -1, 0)) * 0.25
    mixed_xz = (beside_all(1, 0, 1) - beside_all(1, 0, -1) - beside_all(-1, 0, 1) + beside_all(-1, 0, -1)) * 0.25
    mixed_yz = (beside_all(0, 1, 1) - beside_all(0, 1, -1) - beside_all(0, -1, 1) + beside_all(0, -1, -1)) * 0.25
    square_x = first_x * first_x
    square_y = first_y * first_y
    square_z = first_z * first_z
    numerator = second_xx * (square_y + square_z) + second_yy * (square_x + square_z) + second_zz * (square_x + square_y)
    numerator = numerator - 2.0 * (first_x * first_y * mixed_xy + first_x * first_z * mixed_xz + first_y * first_z * mixed_yz)
    curvature = numerator / (square_x + square_y + square_z + 1.0)
    speed_x = -slope[0]
    speed_y = -slope[1]
    speed_z = -slope[2]
    transport = jnp.maximum(speed_x, 0.0) * minus_x + jnp.minimum(speed_x, 0.0) * plus_x
    transport = transport + jnp.maximum(speed_y, 0.0) * minus_y + jnp.minimum(speed_y, 0.0) * plus_y
    transport = transport + jnp.maximum(speed_z, 0.0) * minus_z + jnp.minimum(speed_z, 0.0) * plus_z
    return edge * curvature - transport


def reference(volume, level_set):
    blurred = blur_padded(pad_axis(volume, 2, RADIUS), 2, volume.shape[2])
    blurred = blur_padded(pad_axis(blurred, 1, RADIUS), 1, volume.shape[1])
    blurred = blur_padded(pad_axis(blurred, 0, RADIUS), 0, volume.shape[0])
    edge = edge_from(pad_axis(blurred, 0, 1))
    slope = central_grads(pad_axis(edge, 0, 1))
    section_one = level_set + 0.1 * rates(pad_axis(level_set, 0, 3), edge, slope)
    section_two = 0.75 * level_set + 0.25 * (section_one + 0.1 * rates(pad_axis(section_one, 0, 3), edge, slope))
    advanced = (1.0 / 3.0) * level_set + (2.0 / 3.0) * (section_two + 0.1 * rates(pad_axis(section_two, 0, 3), edge, slope))
    return edge, advanced
```

```python
import math

import jax
import jax.numpy as jnp
from jax import lax
from jax.sharding import PartitionSpec as P

RADIUS = 12


def shifted(block, axis, distance):
    devices = range(lax.axis_size(axis))
    route = [(i - distance, i) for i in devices if i - distance in devices]
    return lax.ppermute(block, axis, route)


def extended_2(block, sides, width):
    for axis, dim in sides:
        count = lax.axis_size(axis)
        forward = [(i, i + 1) for i in range(count - 1)]
        backward = [(target, source) for source, target in forward]
        low = lax.ppermute(
            lax.slice_in_dim(block, block.shape[dim] - width, None, axis=dim), axis, forward
        )
        high = lax.ppermute(lax.slice_in_dim(block, 0, width, axis=dim), axis, backward)
        block = jnp.concatenate([low, block, high], axis=dim)
    return block


def blur_taps():
    raw = [math.exp(-(offset * offset) / 18.0) for offset in range(-RADIUS, RADIUS + 1)]
    total = sum(raw)
    return [value / total for value in raw]


def pad_axis(array, axis, width):
    widths = [(0, 0), (0, 0), (0, 0)]
    widths[axis] = (width, width)
    return jnp.pad(array, widths)


def blur_padded(padded, axis, count):
    taps = blur_taps()
    result = taps[0] * lax.slice_in_dim(padded, 0, count, axis=axis)
    for offset in range(1, len(taps)):
        result = result + taps[offset] * lax.slice_in_dim(padded, offset, offset + count, axis=axis)
    return result


def central_grads(padded):
    inner = padded[1:-1]
    side = jnp.pad(inner, ((0, 0), (1, 1), (1, 1)))
    grad_x = (padded[2:] - padded[:-2]) * 0.5
    grad_y = (side[:, 2:, 1:-1] - side[:, :-2, 1:-1]) * 0.5
    grad_z = (side[:, 1:-1, 2:] - side[:, 1:-1, :-2]) * 0.5
    return (grad_x, grad_y, grad_z)


def edge_from(padded):
    grad_x, grad_y, grad_z = central_grads(padded)
    return 1.0 / (1.0 + 6000.0 * (grad_x * grad_x + grad_y * grad_y + grad_z * grad_z))


def weno(first, second, third, fourth, fifth):
    cand_one = 2.0 * first - 7.0 * second + 11.0 * third
    cand_two = -second + 5.0 * third + 2.0 * fourth
    cand_three = 2.0 * third + 5.0 * fourth - fifth
    part_a = first - 2.0 * second + third
    part_b = first - 4.0 * second + 3.0 * third
    smooth_one = 13.0 / 12.0 * part_a * part_a + 0.25 * part_b * part_b
    part_a = second - 2.0 * third + fourth
    part_b = second - fourth
    smooth_two = 13.0 / 12.0 * part_a * part_a + 0.25 * part_b * part_b
    part_a = third - 2.0 * fourth + fifth
    part_b = 3.0 * third - 4.0 * fourth + fifth
    smooth_three = 13.0 / 12.0 * part_a * part_a + 0.25 * part_b * part_b
    denom_one = 1e-06 + smooth_one
    denom_two = 1e-06 + smooth_two
    denom_three = 1e-06 + smooth_three
    square_one = denom_one * denom_one
    square_two = denom_two * denom_two
    square_three = denom_three * denom_three
    weight_one = 0.1 * (square_two * square_three)
    weight_two = 0.6 * (square_one * square_three)
    weight_three = 0.3 * (square_one * square_two)
    return (weight_one * cand_one + weight_two * cand_two + weight_three * cand_three) / (
        6.0 * (weight_one + weight_two + weight_three)
    )


def upwind(padded, axis, count, speed):
    diffs = lax.slice_in_dim(padded, 1, padded.shape[axis], axis=axis) - lax.slice_in_dim(
        padded, 0, padded.shape[axis] - 1, axis=axis
    )
    pieces = [lax.slice_in_dim(diffs, offset, offset + count, axis=axis) for offset in range(6)]
    ahead = speed > 0.0
    chosen = [jnp.where(ahead, pieces[k], pieces[5 - k]) for k in range(5)]
    return speed * weno(*chosen)


def rates(padded, edge, slope):
    count = padded.shape[0] - 6
    field = padded[3:-3]
    rows_y = field.shape[1]
    rows_z = field.shape[2]
    speed_x = -slope[0]
    speed_y = -slope[1]
    speed_z = -slope[2]
    flow_x = upwind(padded, 0, count, speed_x)
    flow_y = upwind(pad_axis(field, 1, 3), 1, rows_y, speed_y)
    flow_z = upwind(pad_axis(field, 2, 3), 2, rows_z, speed_z)
    near = jnp.pad(padded[2:-2], ((0, 0), (1, 1), (1, 1)))

    def beside_all(step_x, step_y, step_z):
        return near[
            1 + step_x : 1 + step_x + count,
            1 + step_y : 1 + step_y + rows_y,
            1 + step_z : 1 + step_z + rows_z,
        ]

    centre = beside_all(0, 0, 0)
    first_x = (beside_all(1, 0, 0) - beside_all(-1, 0, 0)) * 0.5
    first_y = (beside_all(0, 1, 0) - beside_all(0, -1, 0)) * 0.5
    first_z = (beside_all(0, 0, 1) - beside_all(0, 0, -1)) * 0.5
    second_xx = beside_all(1, 0, 0) - 2.0 * centre + beside_all(-1, 0, 0)
    second_yy = beside_all(0, 1, 0) - 2.0 * centre + beside_all(0, -1, 0)
    second_zz = beside_all(0, 0, 1) - 2.0 * centre + beside_all(0, 0, -1)
    mixed_xy = (
        beside_all(1, 1, 0) - beside_all(1, -1, 0) - beside_all(-1, 1, 0) + beside_all(-1, -1, 0)
    ) * 0.25
    mixed_xz = (
        beside_all(1, 0, 1) - beside_all(1, 0, -1) - beside_all(-1, 0, 1) + beside_all(-1, 0, -1)
    ) * 0.25
    mixed_yz = (
        beside_all(0, 1, 1) - beside_all(0, 1, -1) - beside_all(0, -1, 1) + beside_all(0, -1, -1)
    ) * 0.25
    square_x = first_x * first_x
    square_y = first_y * first_y
    square_z = first_z * first_z
    numerator = (
        second_xx * (square_y + square_z)
        + second_yy * (square_x + square_z)
        + second_zz * (square_x + square_y)
    )
    numerator = numerator - 2.0 * (
        first_x * first_y * mixed_xy + first_x * first_z * mixed_xz + first_y * first_z * mixed_yz
    )
    curvature = numerator / (square_x + square_y + square_z + 1.0)
    transport = flow_x + flow_y + flow_z
    return edge * curvature - transport


def shards(volume, level_set):
    rows = volume.shape[0]
    blurred = blur_padded(pad_axis(volume, 2, RADIUS), 2, volume.shape[2])
    blurred = blur_padded(pad_axis(blurred, 1, RADIUS), 1, volume.shape[1])
    reach = -(-RADIUS // rows)
    jobs = []
    needed = min(rows, RADIUS)
    jobs.append((1, blurred[rows - needed :]))
    jobs.append((-1, blurred[:needed]))
    moved = [shifted(piece, "gx", signed_hops) for signed_hops, piece in jobs]
    below = [moved[2 * (reach - 1)]]
    above = [moved[1]]
    extended = jnp.concatenate(below + [blurred] + above, axis=0)
    blurred = blur_padded(extended, 0, rows)
    wider = extended_2(blurred, (("gx", 0),), 2)
    edge_wide = edge_from(wider)
    positions = lax.axis_index("gx") * rows - 1 + jnp.arange(rows + 2, dtype=jnp.int32)
    inside = (positions >= 0) & (positions < rows * lax.axis_size("gx"))
    edge_wide = jnp.where(inside[:, None, None], edge_wide, 0.0)
    edge = edge_wide[1:-1]
    slope = central_grads(edge_wide)

    def rate_of(field):
        padded = extended_2(field, (("gx", 0),), 3)
        return rates(padded, edge, slope)

    section_one = level_set + 0.1 * rate_of(level_set)
    section_two = 0.75 * level_set + 0.25 * (section_one + 0.1 * rate_of(section_one))
    advanced = 1.0 / 3.0 * level_set + 2.0 / 3.0 * (section_two + 0.1 * rate_of(section_two))
    return (edge, advanced)


def solution(mesh):
    return jax.shard_map(
        shards,
        mesh=mesh,
        in_specs=(P(("grp", "gx"), None, None), P(("grp", "gx"), None, None)),
        out_specs=(P(("grp", "gx"), None, None), P(("grp", "gx"), None, None)),
        check_vma=False,
    )
```

```python
import math

import numpy as np

import jax
import jax.numpy as jnp
from jax import lax
from jax.sharding import PartitionSpec as P

RADIUS = 12


def shifted(block, axis, distance):
    devices = range(lax.axis_size(axis))
    route = [(i - distance, i) for i in devices if i - distance in devices]
    return lax.ppermute(block, axis, route)


def extended_2(block, sides, width):
    for axis, dim in sides:
        count = lax.axis_size(axis)
        forward = [(i, i + 1) for i in range(count - 1)]
        backward = [(target, source) for source, target in forward]
        low = lax.ppermute(
            lax.slice_in_dim(block, block.shape[dim] - width, None, axis=dim), axis, forward
        )
        high = lax.ppermute(lax.slice_in_dim(block, 0, width, axis=dim), axis, backward)
        block = jnp.concatenate([low, block, high], axis=dim)
    return block


def blur_taps():
    raw = [math.exp(-(offset * offset) / 18.0) for offset in range(-RADIUS, RADIUS + 1)]
    total = sum(raw)
    return [value / total for value in raw]


def band(rows, cols, shift):
    taps = blur_taps()
    table = np.zeros((rows, cols), np.float32)
    for i in range(rows):
        for k in range(-RADIUS, RADIUS + 1):
            j = i + shift + k
            if 0 <= j < cols:
                table[i, j] = taps[k + RADIUS]
    return jnp.asarray(table)


def pad_axis(array, axis, width):
    widths = [(0, 0), (0, 0), (0, 0)]
    widths[axis] = (width, width)
    return jnp.pad(array, widths)


def blur_padded(padded, axis, count):
    taps = blur_taps()
    result = taps[0] * lax.slice_in_dim(padded, 0, count, axis=axis)
    for offset in range(1, len(taps)):
        result = result + taps[offset] * lax.slice_in_dim(padded, offset, offset + count, axis=axis)
    return result


def central_grads(padded):
    inner = padded[1:-1]
    side = jnp.pad(inner, ((0, 0), (1, 1), (1, 1)))
    grad_x = (padded[2:] - padded[:-2]) * 0.5
    grad_y = (side[:, 2:, 1:-1] - side[:, :-2, 1:-1]) * 0.5
    grad_z = (side[:, 1:-1, 2:] - side[:, 1:-1, :-2]) * 0.5
    return (grad_x, grad_y, grad_z)


def edge_from(padded):
    grad_x, grad_y, grad_z = central_grads(padded)
    return 1.0 / (1.0 + 6000.0 * (grad_x * grad_x + grad_y * grad_y + grad_z * grad_z))


def weno(first, second, third, fourth, fifth):
    cand_one = (2.0 * first - 7.0 * second + 11.0 * third) / 6.0
    cand_two = (-second + 5.0 * third + 2.0 * fourth) / 6.0
    cand_three = (2.0 * third + 5.0 * fourth - fifth) / 6.0
    part_a = first - 2.0 * second + third
    part_b = first - 4.0 * second + 3.0 * third
    smooth_one = 13.0 / 12.0 * part_a * part_a + 0.25 * part_b * part_b
    part_a = second - 2.0 * third + fourth
    part_b = second - fourth
    smooth_two = 13.0 / 12.0 * part_a * part_a + 0.25 * part_b * part_b
    part_a = third - 2.0 * fourth + fifth
    part_b = 3.0 * third - 4.0 * fourth + fifth
    smooth_three = 13.0 / 12.0 * part_a * part_a + 0.25 * part_b * part_b
    denom_one = 1e-06 + smooth_one
    denom_two = 1e-06 + smooth_two
    denom_three = 1e-06 + smooth_three
    weight_one = 0.1 / (denom_one * denom_one)
    weight_two = 0.6 / (denom_two * denom_two)
    weight_three = 0.3 / (denom_three * denom_three)
    return (weight_one * cand_one + weight_two * cand_two + weight_three * cand_three) / (
        weight_one + weight_two + weight_three
    )


def upwind(padded, axis, count):
    diffs = lax.slice_in_dim(padded, 1, padded.shape[axis], axis=axis) - lax.slice_in_dim(
        padded, 0, padded.shape[axis] - 1, axis=axis
    )
    pieces = [lax.slice_in_dim(diffs, offset, offset + count, axis=axis) for offset in range(6)]
    minus = weno(pieces[0], pieces[1], pieces[2], pieces[3], pieces[4])
    plus = weno(pieces[5], pieces[4], pieces[3], pieces[2], pieces[1])
    return (minus, plus)


def rates(padded, edge, slope):
    count = padded.shape[0] - 6
    field = padded[3:-3]
    rows_y = field.shape[1]
    rows_z = field.shape[2]
    minus_x, plus_x = upwind(padded, 0, count)
    minus_y, plus_y = upwind(pad_axis(field, 1, 3), 1, rows_y)
    minus_z, plus_z = upwind(pad_axis(field, 2, 3), 2, rows_z)
    near = jnp.pad(padded[2:-2], ((0, 0), (1, 1), (1, 1)))

    def beside_all(step_x, step_y, step_z):
        return near[
            1 + step_x : 1 + step_x + count,
            1 + step_y : 1 + step_y + rows_y,
            1 + step_z : 1 + step_z + rows_z,
        ]

    centre = beside_all(0, 0, 0)
    first_x = (beside_all(1, 0, 0) - beside_all(-1, 0, 0)) * 0.5
    first_y = (beside_all(0, 1, 0) - beside_all(0, -1, 0)) * 0.5
    first_z = (beside_all(0, 0, 1) - beside_all(0, 0, -1)) * 0.5
    second_xx = beside_all(1, 0, 0) - 2.0 * centre + beside_all(-1, 0, 0)
    second_yy = beside_all(0, 1, 0) - 2.0 * centre + beside_all(0, -1, 0)
    second_zz = beside_all(0, 0, 1) - 2.0 * centre + beside_all(0, 0, -1)
    mixed_xy = (
        beside_all(1, 1, 0) - beside_all(1, -1, 0) - beside_all(-1, 1, 0) + beside_all(-1, -1, 0)
    ) * 0.25
    mixed_xz = (
        beside_all(1, 0, 1) - beside_all(1, 0, -1) - beside_all(-1, 0, 1) + beside_all(-1, 0, -1)
    ) * 0.25
    mixed_yz = (
        beside_all(0, 1, 1) - beside_all(0, 1, -1) - beside_all(0, -1, 1) + beside_all(0, -1, -1)
    ) * 0.25
    square_x = first_x * first_x
    square_y = first_y * first_y
    square_z = first_z * first_z
    numerator = (
        second_xx * (square_y + square_z)
        + second_yy * (square_x + square_z)
        + second_zz * (square_x + square_y)
    )
    numerator = numerator - 2.0 * (
        first_x * first_y * mixed_xy + first_x * first_z * mixed_xz + first_y * first_z * mixed_yz
    )
    curvature = numerator / (square_x + square_y + square_z + 1.0)
    speed_x = -slope[0]
    speed_y = -slope[1]
    speed_z = -slope[2]
    transport = jnp.maximum(speed_x, 0.0) * minus_x + jnp.minimum(speed_x, 0.0) * plus_x
    transport = transport + jnp.maximum(speed_y, 0.0) * minus_y + jnp.minimum(speed_y, 0.0) * plus_y
    transport = transport + jnp.maximum(speed_z, 0.0) * minus_z + jnp.minimum(speed_z, 0.0) * plus_z
    return edge * curvature - transport


def shards(volume, level_set):
    rows, rows_y, rows_z = volume.shape
    exact = lax.Precision.HIGHEST
    blurred = jnp.dot(
        volume.reshape(rows * rows_y, rows_z), band(rows_z, rows_z, 0).T, precision=exact
    ).reshape(rows, rows_y, rows_z)
    blurred = jnp.einsum("yv,xvz->xyz", band(rows_y, rows_y, 0), blurred, precision=exact)
    reach = -(-RADIUS // rows)
    jobs = []
    needed = min(rows, RADIUS)
    jobs.append((1, blurred[rows - needed :]))
    jobs.append((-1, blurred[:needed]))
    moved = [shifted(piece, "gx", signed_hops) for signed_hops, piece in jobs]
    below = [moved[2 * (reach - 1)]]
    above = [moved[1]]
    extended = jnp.concatenate(below + [blurred] + above, axis=0)
    blurred = jnp.dot(
        band(rows, extended.shape[0], needed),
        extended.reshape(extended.shape[0], rows_y * rows_z),
        precision=exact,
    ).reshape(rows, rows_y, rows_z)
    wider = extended_2(blurred, (("gx", 0),), 2)
    edge_wide = edge_from(wider)
    positions = lax.axis_index("gx") * rows - 1 + jnp.arange(rows + 2, dtype=jnp.int32)
    inside = (positions >= 0) & (positions < rows * lax.axis_size("gx"))
    edge_wide = jnp.where(inside[:, None, None], edge_wide, 0.0)
    edge = edge_wide[1:-1]
    slope = central_grads(edge_wide)

    def rate_of(field):
        padded = extended_2(field, (("gx", 0),), 3)
        return rates(padded, edge, slope)

    section_one = level_set + 0.1 * rate_of(level_set)
    section_two = 0.75 * level_set + 0.25 * (section_one + 0.1 * rate_of(section_one))
    advanced = 1.0 / 3.0 * level_set + 2.0 / 3.0 * (section_two + 0.1 * rate_of(section_two))
    return (edge, advanced)


def solution(mesh):
    return jax.shard_map(
        shards,
        mesh=mesh,
        in_specs=(P(("grp", "gx"), None, None), P(("grp", "gx"), None, None)),
        out_specs=(P(("grp", "gx"), None, None), P(("grp", "gx"), None, None)),
        check_vma=False,
    )
```

```python
import math

import numpy as np

import jax
import jax.numpy as jnp
from jax import lax
from jax.experimental import pallas as pl
from jax.experimental.pallas import tpu as pltpu
from jax.sharding import PartitionSpec as P

RADIUS = 12


def shifted(block, axis, distance):
    devices = range(lax.axis_size(axis))
    route = [(i - distance, i) for i in devices if i - distance in devices]
    return lax.ppermute(block, axis, route)


def extended_2(block, sides, width):
    for axis, dim in sides:
        count = lax.axis_size(axis)
        forward = [(i, i + 1) for i in range(count - 1)]
        backward = [(target, source) for source, target in forward]
        low = lax.ppermute(
            lax.slice_in_dim(block, block.shape[dim] - width, None, axis=dim), axis, forward
        )
        high = lax.ppermute(lax.slice_in_dim(block, 0, width, axis=dim), axis, backward)
        block = jnp.concatenate([low, block, high], axis=dim)
    return block


def blur_taps():
    raw = [math.exp(-(offset * offset) / 18.0) for offset in range(-RADIUS, RADIUS + 1)]
    total = sum(raw)
    return [value / total for value in raw]


def band(rows, cols, shift):
    taps = blur_taps()
    table = np.zeros((rows, cols), np.float32)
    for i in range(rows):
        for k in range(-RADIUS, RADIUS + 1):
            j = i + shift + k
            if 0 <= j < cols:
                table[i, j] = taps[k + RADIUS]
    return jnp.asarray(table)


def pad_axis(array, axis, width):
    widths = [(0, 0), (0, 0), (0, 0)]
    widths[axis] = (width, width)
    return jnp.pad(array, widths)


def blur_padded(padded, axis, count):
    taps = blur_taps()
    result = taps[0] * lax.slice_in_dim(padded, 0, count, axis=axis)
    for offset in range(1, len(taps)):
        result = result + taps[offset] * lax.slice_in_dim(padded, offset, offset + count, axis=axis)
    return result


def central_grads(padded):
    inner = padded[1:-1]
    side = jnp.pad(inner, ((0, 0), (1, 1), (1, 1)))
    grad_x = (padded[2:] - padded[:-2]) * 0.5
    grad_y = (side[:, 2:, 1:-1] - side[:, :-2, 1:-1]) * 0.5
    grad_z = (side[:, 1:-1, 2:] - side[:, 1:-1, :-2]) * 0.5
    return (grad_x, grad_y, grad_z)


def edge_from(padded):
    grad_x, grad_y, grad_z = central_grads(padded)
    return 1.0 / (1.0 + 6000.0 * (grad_x * grad_x + grad_y * grad_y + grad_z * grad_z))


def weno(first, second, third, fourth, fifth):
    cand_one = 2.0 * first - 7.0 * second + 11.0 * third
    cand_two = -second + 5.0 * third + 2.0 * fourth
    cand_three = 2.0 * third + 5.0 * fourth - fifth
    part_a = first - 2.0 * second + third
    part_b = first - 4.0 * second + 3.0 * third
    smooth_one = 13.0 / 12.0 * part_a * part_a + 0.25 * part_b * part_b
    part_a = second - 2.0 * third + fourth
    part_b = second - fourth
    smooth_two = 13.0 / 12.0 * part_a * part_a + 0.25 * part_b * part_b
    part_a = third - 2.0 * fourth + fifth
    part_b = 3.0 * third - 4.0 * fourth + fifth
    smooth_three = 13.0 / 12.0 * part_a * part_a + 0.25 * part_b * part_b
    denom_one = 1e-06 + smooth_one
    denom_two = 1e-06 + smooth_two
    denom_three = 1e-06 + smooth_three
    square_one = denom_one * denom_one
    square_two = denom_two * denom_two
    square_three = denom_three * denom_three
    weight_one = 0.1 * (square_two * square_three)
    weight_two = 0.6 * (square_one * square_three)
    weight_three = 0.3 * (square_one * square_two)
    return (weight_one * cand_one + weight_two * cand_two + weight_three * cand_three) / (
        6.0 * (weight_one + weight_two + weight_three)
    )


def upwind(values, speed):
    diffs = [values[k + 1] - values[k] for k in range(6)]
    ahead = speed > 0.0
    chosen = [jnp.where(ahead, diffs[k], diffs[5 - k]) for k in range(5)]
    return speed * weno(*chosen)


SUB = 8
HALO = 3


def stage_kernel(scale_level, scale_step, rows_block):
    def kernel(p_ref, edge_ref, sx_ref, sy_ref, sz_ref, ls_ref, out_ref):
        rows_y = out_ref.shape[1]
        rows_z = out_ref.shape[2]
        block = pl.program_id(0)
        lane = lax.broadcasted_iota(jnp.int32, (SUB, rows_z), 1)

        def along_z(tile, step):
            moved = pltpu.roll(tile, (-step) % rows_z, 1)
            keep = (lane + step >= 0) & (lane + step < rows_z)
            return jnp.where(keep, moved, 0.0)

        def row(r, carry):
            centre_row = block * rows_block + r + HALO
            for chunk in range(rows_y // SUB):
                top = SUB + chunk * SUB

                def at(step_x, step_y):
                    return p_ref[centre_row + step_x, pl.ds(top + step_y, SUB), :]

                centre = at(0, 0)
                line_x = [at(k, 0) for k in range(-HALO, HALO + 1)]
                line_y = [at(0, k) for k in range(-HALO, HALO + 1)]
                line_z = [along_z(centre, k) for k in range(-HALO, HALO + 1)]
                here = pl.ds(chunk * SUB, SUB)
                speed_x = -sx_ref[r, here, :]
                speed_y = -sy_ref[r, here, :]
                speed_z = -sz_ref[r, here, :]
                flow_x = upwind(line_x, speed_x)
                flow_y = upwind(line_y, speed_y)
                flow_z = upwind(line_z, speed_z)
                up_x = line_x[HALO + 1]
                down_x = line_x[HALO - 1]
                up_y = line_y[HALO + 1]
                down_y = line_y[HALO - 1]
                up_z = line_z[HALO + 1]
                down_z = line_z[HALO - 1]
                first_x = (up_x - down_x) * 0.5
                first_y = (up_y - down_y) * 0.5
                first_z = (up_z - down_z) * 0.5
                second_xx = up_x - 2.0 * centre + down_x
                second_yy = up_y - 2.0 * centre + down_y
                second_zz = up_z - 2.0 * centre + down_z
                mixed_xy = (at(1, 1) - at(1, -1) - at(-1, 1) + at(-1, -1)) * 0.25
                mixed_xz = (
                    along_z(up_x, 1) - along_z(up_x, -1) - along_z(down_x, 1) + along_z(down_x, -1)
                ) * 0.25
                mixed_yz = (
                    along_z(up_y, 1) - along_z(up_y, -1) - along_z(down_y, 1) + along_z(down_y, -1)
                ) * 0.25
                square_x = first_x * first_x
                square_y = first_y * first_y
                square_z = first_z * first_z
                numerator = (
                    second_xx * (square_y + square_z)
                    + second_yy * (square_x + square_z)
                    + second_zz * (square_x + square_y)
                )
                numerator = numerator - 2.0 * (
                    first_x * first_y * mixed_xy
                    + first_x * first_z * mixed_xz
                    + first_y * first_z * mixed_yz
                )
                curvature = numerator / (square_x + square_y + square_z + 1.0)
                transport = flow_x + flow_y + flow_z
                rate = edge_ref[r, here, :] * curvature - transport
                moved = centre + 0.1 * rate
                if scale_level is None:
                    out_ref[r, here, :] = moved
                else:
                    out_ref[r, here, :] = scale_level * ls_ref[r, here, :] + scale_step * moved
            return carry

        lax.fori_loop(0, rows_block, row, 0)

    return kernel


def stage(padded, edge, slope, level_set, scale_level, scale_step):
    rows, rows_y, rows_z = level_set.shape
    rows_block = SUB if rows % SUB == 0 else rows
    whole = pl.BlockSpec(padded.shape, lambda i: (0, 0, 0))
    part = pl.BlockSpec((rows_block, rows_y, rows_z), lambda i: (i, 0, 0))
    return pl.pallas_call(
        stage_kernel(scale_level, scale_step, rows_block),
        grid=(rows // rows_block,),
        in_specs=[whole, part, part, part, part, part],
        out_specs=part,
        out_shape=jax.ShapeDtypeStruct(level_set.shape, level_set.dtype),
    )(padded, edge, slope[0], slope[1], slope[2], level_set)


def shards(volume, level_set):
    rows, rows_y, rows_z = volume.shape
    exact = lax.Precision.HIGHEST
    blurred = jnp.dot(
        volume.reshape(rows * rows_y, rows_z), band(rows_z, rows_z, 0).T, precision=exact
    ).reshape(rows, rows_y, rows_z)
    blurred = jnp.einsum("yv,xvz->xyz", band(rows_y, rows_y, 0), blurred, precision=exact)
    reach = -(-RADIUS // rows)
    jobs = []
    needed = min(rows, RADIUS)
    jobs.append((1, blurred[rows - needed :]))
    jobs.append((-1, blurred[:needed]))
    moved = [shifted(piece, "gx", signed_hops) for signed_hops, piece in jobs]
    below = [moved[2 * (reach - 1)]]
    above = [moved[1]]
    extended = jnp.concatenate(below + [blurred] + above, axis=0)
    blurred = jnp.dot(
        band(rows, extended.shape[0], needed),
        extended.reshape(extended.shape[0], rows_y * rows_z),
        precision=exact,
    ).reshape(rows, rows_y, rows_z)
    wider = extended_2(blurred, (("gx", 0),), 2)
    edge_wide = edge_from(wider)
    positions = lax.axis_index("gx") * rows - 1 + jnp.arange(rows + 2, dtype=jnp.int32)
    inside = (positions >= 0) & (positions < rows * lax.axis_size("gx"))
    edge_wide = jnp.where(inside[:, None, None], edge_wide, 0.0)
    edge = edge_wide[1:-1]
    slope = central_grads(edge_wide)

    def step(field, scale_level, scale_step):
        padded = extended_2(field, (("gx", 0),), HALO)
        padded = jnp.pad(padded, ((0, 0), (SUB, SUB), (0, 0)))
        return stage(padded, edge, slope, level_set, scale_level, scale_step)

    section_one = step(level_set, None, None)
    section_two = step(section_one, 0.75, 0.25)
    advanced = step(section_two, 1.0 / 3.0, 2.0 / 3.0)
    return (edge, advanced)


def solution(mesh):
    return jax.shard_map(
        shards,
        mesh=mesh,
        in_specs=(P(("grp", "gx"), None, None), P(("grp", "gx"), None, None)),
        out_specs=(P(("grp", "gx"), None, None), P(("grp", "gx"), None, None)),
        check_vma=False,
    )
```

```python
import math

import numpy as np

import jax
import jax.numpy as jnp
from jax import lax
from jax.experimental import pallas as pl
from jax.experimental.pallas import tpu as pltpu
from jax.sharding import PartitionSpec as P

RADIUS = 12


def shifted(block, axis, distance):
    devices = range(lax.axis_size(axis))
    route = [(i - distance, i) for i in devices if i - distance in devices]
    return lax.ppermute(block, axis, route)


def extended_2(block, sides, width):
    for axis, dim in sides:
        count = lax.axis_size(axis)
        forward = [(i, i + 1) for i in range(count - 1)]
        backward = [(target, source) for source, target in forward]
        low = lax.ppermute(
            lax.slice_in_dim(block, block.shape[dim] - width, None, axis=dim), axis, forward
        )
        high = lax.ppermute(lax.slice_in_dim(block, 0, width, axis=dim), axis, backward)
        block = jnp.concatenate([low, block, high], axis=dim)
    return block


def blur_taps():
    raw = [math.exp(-(offset * offset) / 18.0) for offset in range(-RADIUS, RADIUS + 1)]
    total = sum(raw)
    return [value / total for value in raw]


def band(rows, cols, shift):
    taps = blur_taps()
    table = np.zeros((rows, cols), np.float32)
    for i in range(rows):
        for k in range(-RADIUS, RADIUS + 1):
            j = i + shift + k
            if 0 <= j < cols:
                table[i, j] = taps[k + RADIUS]
    return jnp.asarray(table)


def pad_axis(array, axis, width):
    widths = [(0, 0), (0, 0), (0, 0)]
    widths[axis] = (width, width)
    return jnp.pad(array, widths)


def blur_padded(padded, axis, count):
    taps = blur_taps()
    result = taps[0] * lax.slice_in_dim(padded, 0, count, axis=axis)
    for offset in range(1, len(taps)):
        result = result + taps[offset] * lax.slice_in_dim(padded, offset, offset + count, axis=axis)
    return result


def central_grads(padded):
    inner = padded[1:-1]
    side = jnp.pad(inner, ((0, 0), (1, 1), (1, 1)))
    grad_x = (padded[2:] - padded[:-2]) * 0.5
    grad_y = (side[:, 2:, 1:-1] - side[:, :-2, 1:-1]) * 0.5
    grad_z = (side[:, 1:-1, 2:] - side[:, 1:-1, :-2]) * 0.5
    return (grad_x, grad_y, grad_z)


def edge_from(padded):
    grad_x, grad_y, grad_z = central_grads(padded)
    return 1.0 / (1.0 + 6000.0 * (grad_x * grad_x + grad_y * grad_y + grad_z * grad_z))


def weno(first, second, third, fourth, fifth):
    cand_one = 2.0 * first - 7.0 * second + 11.0 * third
    cand_two = -second + 5.0 * third + 2.0 * fourth
    cand_three = 2.0 * third + 5.0 * fourth - fifth
    part_a = first - 2.0 * second + third
    part_b = first - 4.0 * second + 3.0 * third
    smooth_one = 13.0 / 12.0 * part_a * part_a + 0.25 * part_b * part_b
    part_a = second - 2.0 * third + fourth
    part_b = second - fourth
    smooth_two = 13.0 / 12.0 * part_a * part_a + 0.25 * part_b * part_b
    part_a = third - 2.0 * fourth + fifth
    part_b = 3.0 * third - 4.0 * fourth + fifth
    smooth_three = 13.0 / 12.0 * part_a * part_a + 0.25 * part_b * part_b
    denom_one = 1e-06 + smooth_one
    denom_two = 1e-06 + smooth_two
    denom_three = 1e-06 + smooth_three
    square_one = denom_one * denom_one
    square_two = denom_two * denom_two
    square_three = denom_three * denom_three
    weight_one = 0.1 * (square_two * square_three)
    weight_two = 0.6 * (square_one * square_three)
    weight_three = 0.3 * (square_one * square_two)
    return (weight_one * cand_one + weight_two * cand_two + weight_three * cand_three) / (
        6.0 * (weight_one + weight_two + weight_three)
    )


def upwind(values, speed):
    diffs = [values[k + 1] - values[k] for k in range(6)]
    ahead = speed > 0.0
    chosen = [jnp.where(ahead, diffs[k], diffs[5 - k]) for k in range(5)]
    return speed * weno(*chosen)


SUB = 8
HALO = 3


def stage_kernel(scale_level, scale_step, rows_block):
    def kernel(p_ref, edge_ref, sx_ref, sy_ref, sz_ref, ls_ref, out_ref):
        rows_y = out_ref.shape[1]
        rows_z = out_ref.shape[2]
        block = pl.program_id(0)
        lane = lax.broadcasted_iota(jnp.int32, (SUB, rows_z), 1)

        def along_z(tile, step):
            moved = pltpu.roll(tile, (-step) % rows_z, 1)
            keep = (lane + step >= 0) & (lane + step < rows_z)
            return jnp.where(keep, moved, 0.0)

        def row(r, carry):
            centre_row = block * rows_block + r + HALO
            for chunk in range(rows_y // SUB):
                top = SUB + chunk * SUB

                def at(step_x, step_y):
                    return p_ref[centre_row + step_x, pl.ds(top + step_y, SUB), :]

                centre = at(0, 0)
                line_x = [at(k, 0) for k in range(-HALO, HALO + 1)]
                line_y = [at(0, k) for k in range(-HALO, HALO + 1)]
                line_z = [along_z(centre, k) for k in range(-HALO, HALO + 1)]
                here = pl.ds(chunk * SUB, SUB)
                speed_x = -sx_ref[r, here, :]
                speed_y = -sy_ref[r, here, :]
                speed_z = -sz_ref[r, here, :]
                flow_x = upwind(line_x, speed_x)
                flow_y = upwind(line_y, speed_y)
                flow_z = upwind(line_z, speed_z)
                up_x = line_x[HALO + 1]
                down_x = line_x[HALO - 1]
                up_y = line_y[HALO + 1]
                down_y = line_y[HALO - 1]
                up_z = line_z[HALO + 1]
                down_z = line_z[HALO - 1]
                first_x = (up_x - down_x) * 0.5
                first_y = (up_y - down_y) * 0.5
                first_z = (up_z - down_z) * 0.5
                second_xx = up_x - 2.0 * centre + down_x
                second_yy = up_y - 2.0 * centre + down_y
                second_zz = up_z - 2.0 * centre + down_z
                mixed_xy = (at(1, 1) - at(1, -1) - at(-1, 1) + at(-1, -1)) * 0.25
                mixed_xz = (
                    along_z(up_x, 1) - along_z(up_x, -1) - along_z(down_x, 1) + along_z(down_x, -1)
                ) * 0.25
                mixed_yz = (
                    along_z(up_y, 1) - along_z(up_y, -1) - along_z(down_y, 1) + along_z(down_y, -1)
                ) * 0.25
                square_x = first_x * first_x
                square_y = first_y * first_y
                square_z = first_z * first_z
                numerator = (
                    second_xx * (square_y + square_z)
                    + second_yy * (square_x + square_z)
                    + second_zz * (square_x + square_y)
                )
                numerator = numerator - 2.0 * (
                    first_x * first_y * mixed_xy
                    + first_x * first_z * mixed_xz
                    + first_y * first_z * mixed_yz
                )
                curvature = numerator / (square_x + square_y + square_z + 1.0)
                transport = flow_x + flow_y + flow_z
                rate = edge_ref[r, here, :] * curvature - transport
                moved = centre + 0.1 * rate
                if scale_level is None:
                    out_ref[r, here, :] = moved
                else:
                    out_ref[r, here, :] = scale_level * ls_ref[r, here, :] + scale_step * moved
            return carry

        lax.fori_loop(0, rows_block, row, 0)

    return kernel


def stage(padded, edge, slope, level_set, scale_level, scale_step):
    rows, rows_y, rows_z = level_set.shape
    rows_block = SUB if rows % SUB == 0 else rows
    whole = pl.BlockSpec(padded.shape, lambda i: (0, 0, 0))
    part = pl.BlockSpec((rows_block, rows_y, rows_z), lambda i: (i, 0, 0))
    return pl.pallas_call(
        stage_kernel(scale_level, scale_step, rows_block),
        grid=(rows // rows_block,),
        in_specs=[whole, part, part, part, part, part],
        out_specs=part,
        out_shape=jax.ShapeDtypeStruct(level_set.shape, level_set.dtype),
    )(padded, edge, slope[0], slope[1], slope[2], level_set)


def shards(volume, level_set):
    rows, rows_y, rows_z = volume.shape
    exact = lax.Precision.HIGHEST
    halo = min(rows, RADIUS + 2)
    low = shifted(volume[rows - halo :], "gx", 1)
    high = shifted(volume[:halo], "gx", -1)
    extended = jnp.concatenate([low, volume, high], axis=0)
    wide = rows + 4
    blurred = jnp.dot(
        band(wide, extended.shape[0], halo - 2),
        extended.reshape(extended.shape[0], rows_y * rows_z),
        precision=exact,
    )
    blurred = jnp.dot(
        blurred.reshape(wide * rows_y, rows_z), band(rows_z, rows_z, 0).T, precision=exact
    ).reshape(wide, rows_y, rows_z)
    blurred = jnp.einsum("yv,xvz->xyz", band(rows_y, rows_y, 0), blurred, precision=exact)
    positions = lax.axis_index("gx") * rows - 2 + jnp.arange(wide, dtype=jnp.int32)
    inside = (positions >= 0) & (positions < rows * lax.axis_size("gx"))
    blurred = jnp.where(inside[:, None, None], blurred, 0.0)
    edge_wide = edge_from(blurred)
    edge_wide = jnp.where(inside[1:-1, None, None], edge_wide, 0.0)
    edge = edge_wide[1:-1]
    slope = central_grads(edge_wide)

    def step(field, scale_level, scale_step):
        padded = extended_2(field, (("gx", 0),), HALO)
        padded = jnp.pad(padded, ((0, 0), (SUB, SUB), (0, 0)))
        return stage(padded, edge, slope, level_set, scale_level, scale_step)

    section_one = step(level_set, None, None)
    section_two = step(section_one, 0.75, 0.25)
    advanced = step(section_two, 1.0 / 3.0, 2.0 / 3.0)
    return (edge, advanced)


def solution(mesh):
    return jax.shard_map(
        shards,
        mesh=mesh,
        in_specs=(P(("grp", "gx"), None, None), P(("grp", "gx"), None, None)),
        out_specs=(P(("grp", "gx"), None, None), P(("grp", "gx"), None, None)),
        check_vma=False,
    )
```

```python
import math

import numpy as np

import jax
import jax.numpy as jnp
from jax import lax
from jax.experimental import pallas as pl
from jax.experimental.pallas import tpu as pltpu
from jax.sharding import PartitionSpec as P

RADIUS = 12


def shifted(block, axis, distance):
    devices = range(lax.axis_size(axis))
    route = [(i - distance, i) for i in devices if i - distance in devices]
    return lax.ppermute(block, axis, route)


def extended_2(block, sides, width):
    for axis, dim in sides:
        count = lax.axis_size(axis)
        forward = [(i, i + 1) for i in range(count - 1)]
        backward = [(target, source) for source, target in forward]
        low = lax.ppermute(
            lax.slice_in_dim(block, block.shape[dim] - width, None, axis=dim), axis, forward
        )
        high = lax.ppermute(lax.slice_in_dim(block, 0, width, axis=dim), axis, backward)
        block = jnp.concatenate([low, block, high], axis=dim)
    return block


def blur_taps():
    raw = [math.exp(-(offset * offset) / 18.0) for offset in range(-RADIUS, RADIUS + 1)]
    total = sum(raw)
    return [value / total for value in raw]


def band(rows, cols, shift):
    taps = blur_taps()
    table = np.zeros((rows, cols), np.float32)
    for i in range(rows):
        for k in range(-RADIUS, RADIUS + 1):
            j = i + shift + k
            if 0 <= j < cols:
                table[i, j] = taps[k + RADIUS]
    return jnp.asarray(table)


def pad_axis(array, axis, width):
    widths = [(0, 0), (0, 0), (0, 0)]
    widths[axis] = (width, width)
    return jnp.pad(array, widths)


def blur_padded(padded, axis, count):
    taps = blur_taps()
    result = taps[0] * lax.slice_in_dim(padded, 0, count, axis=axis)
    for offset in range(1, len(taps)):
        result = result + taps[offset] * lax.slice_in_dim(padded, offset, offset + count, axis=axis)
    return result


def central_grads(padded):
    inner = padded[1:-1]
    side = jnp.pad(inner, ((0, 0), (1, 1), (1, 1)))
    grad_x = (padded[2:] - padded[:-2]) * 0.5
    grad_y = (side[:, 2:, 1:-1] - side[:, :-2, 1:-1]) * 0.5
    grad_z = (side[:, 1:-1, 2:] - side[:, 1:-1, :-2]) * 0.5
    return (grad_x, grad_y, grad_z)


def edge_from(padded):
    grad_x, grad_y, grad_z = central_grads(padded)
    return 1.0 / (1.0 + 6000.0 * (grad_x * grad_x + grad_y * grad_y + grad_z * grad_z))


def weno(first, second, third, fourth, fifth):
    cand_one = 2.0 * first - 7.0 * second + 11.0 * third
    cand_two = -second + 5.0 * third + 2.0 * fourth
    cand_three = 2.0 * third + 5.0 * fourth - fifth
    part_a = first - 2.0 * second + third
    part_b = first - 4.0 * second + 3.0 * third
    smooth_one = 13.0 / 12.0 * part_a * part_a + 0.25 * part_b * part_b
    part_a = second - 2.0 * third + fourth
    part_b = second - fourth
    smooth_two = 13.0 / 12.0 * part_a * part_a + 0.25 * part_b * part_b
    part_a = third - 2.0 * fourth + fifth
    part_b = 3.0 * third - 4.0 * fourth + fifth
    smooth_three = 13.0 / 12.0 * part_a * part_a + 0.25 * part_b * part_b
    denom_one = 1e-06 + smooth_one
    denom_two = 1e-06 + smooth_two
    denom_three = 1e-06 + smooth_three
    square_one = denom_one * denom_one
    square_two = denom_two * denom_two
    square_three = denom_three * denom_three
    weight_one = 0.1 * (square_two * square_three)
    weight_two = 0.6 * (square_one * square_three)
    weight_three = 0.3 * (square_one * square_two)
    return (weight_one * cand_one + weight_two * cand_two + weight_three * cand_three) / (
        6.0 * (weight_one + weight_two + weight_three)
    )


def upwind(values, speed):
    diffs = [values[k + 1] - values[k] for k in range(6)]
    ahead = speed > 0.0
    chosen = [jnp.where(ahead, diffs[k], diffs[5 - k]) for k in range(5)]
    return speed * weno(*chosen)


SUB = 8
HALO = 3


def stage_kernel(scale_level, scale_step, rows_block):
    def kernel(p_ref, edge_ref, sx_ref, sy_ref, sz_ref, ls_ref, out_ref):
        rows_y = out_ref.shape[1]
        rows_z = out_ref.shape[2]
        block = pl.program_id(0)
        lane = lax.broadcasted_iota(jnp.int32, (SUB, rows_z), 1)
        keeps = {
            step: (lane + step >= 0) & (lane + step < rows_z)
            for step in range(-HALO, HALO + 1)
            if step != 0
        }

        def along_z(tile, step):
            if step == 0:
                return tile
            return jnp.where(keeps[step], pltpu.roll(tile, (-step) % rows_z, 1), 0.0)

        def row(r, carry):
            centre_row = block * rows_block + r + HALO
            for chunk in range(rows_y // SUB):
                top = SUB + chunk * SUB

                def at(step_x, step_y):
                    return p_ref[centre_row + step_x, pl.ds(top + step_y, SUB), :]

                centre = at(0, 0)
                line_x = [at(k, 0) for k in range(-HALO, HALO + 1)]
                line_y = [at(0, k) for k in range(-HALO, HALO + 1)]
                line_z = [along_z(centre, k) for k in range(-HALO, HALO + 1)]
                here = pl.ds(chunk * SUB, SUB)
                speed_x = -sx_ref[r, here, :]
                speed_y = -sy_ref[r, here, :]
                speed_z = -sz_ref[r, here, :]
                flow_x = upwind(line_x, speed_x)
                flow_y = upwind(line_y, speed_y)
                flow_z = upwind(line_z, speed_z)
                up_x = line_x[HALO + 1]
                down_x = line_x[HALO - 1]
                up_y = line_y[HALO + 1]
                down_y = line_y[HALO - 1]
                up_z = line_z[HALO + 1]
                down_z = line_z[HALO - 1]
                first_x = (up_x - down_x) * 0.5
                first_y = (up_y - down_y) * 0.5
                first_z = (up_z - down_z) * 0.5
                second_xx = up_x - 2.0 * centre + down_x
                second_yy = up_y - 2.0 * centre + down_y
                second_zz = up_z - 2.0 * centre + down_z
                mixed_xy = (at(1, 1) - at(1, -1) - at(-1, 1) + at(-1, -1)) * 0.25
                mixed_xz = (
                    along_z(up_x, 1) - along_z(up_x, -1) - along_z(down_x, 1) + along_z(down_x, -1)
                ) * 0.25
                mixed_yz = (
                    along_z(up_y, 1) - along_z(up_y, -1) - along_z(down_y, 1) + along_z(down_y, -1)
                ) * 0.25
                square_x = first_x * first_x
                square_y = first_y * first_y
                square_z = first_z * first_z
                numerator = (
                    second_xx * (square_y + square_z)
                    + second_yy * (square_x + square_z)
                    + second_zz * (square_x + square_y)
                )
                numerator = numerator - 2.0 * (
                    first_x * first_y * mixed_xy
                    + first_x * first_z * mixed_xz
                    + first_y * first_z * mixed_yz
                )
                curvature = numerator / (square_x + square_y + square_z + 1.0)
                transport = flow_x + flow_y + flow_z
                rate = edge_ref[r, here, :] * curvature - transport
                moved = centre + 0.1 * rate
                if scale_level is None:
                    out_ref[r, here, :] = moved
                else:
                    out_ref[r, here, :] = scale_level * ls_ref[r, here, :] + scale_step * moved
            return carry

        lax.fori_loop(0, rows_block, row, 0)

    return kernel


def stage(padded, edge, slope, level_set, scale_level, scale_step):
    rows, rows_y, rows_z = level_set.shape
    rows_block = SUB if rows % SUB == 0 else rows
    whole = pl.BlockSpec(padded.shape, lambda i: (0, 0, 0))
    part = pl.BlockSpec((rows_block, rows_y, rows_z), lambda i: (i, 0, 0))
    return pl.pallas_call(
        stage_kernel(scale_level, scale_step, rows_block),
        grid=(rows // rows_block,),
        in_specs=[whole, part, part, part, part, part],
        out_specs=part,
        out_shape=jax.ShapeDtypeStruct(level_set.shape, level_set.dtype),
    )(padded, edge, slope[0], slope[1], slope[2], level_set)


def shards(volume, level_set):
    rows, rows_y, rows_z = volume.shape
    exact = lax.Precision.HIGHEST
    halo = min(rows, RADIUS + 2)
    low = shifted(volume[rows - halo :], "gx", 1)
    high = shifted(volume[:halo], "gx", -1)

    def across(block):
        count = block.shape[0]
        flat = jnp.dot(
            block.reshape(count * rows_y, rows_z), band(rows_z, rows_z, 0).T, precision=exact
        ).reshape(count, rows_y, rows_z)
        return jnp.einsum("yv,xvz->xyz", band(rows_y, rows_y, 0), flat, precision=exact)

    wide = rows + 4

    def along_x(block, shift):
        count = block.shape[0]
        return jnp.dot(
            band(wide, count, shift), block.reshape(count, rows_y * rows_z), precision=exact
        ).reshape(wide, rows_y, rows_z)

    blurred = along_x(across(volume), -2)
    blurred = blurred + along_x(across(low), halo - 2) + along_x(across(high), -(rows + 2))
    positions = lax.axis_index("gx") * rows - 2 + jnp.arange(wide, dtype=jnp.int32)
    inside = (positions >= 0) & (positions < rows * lax.axis_size("gx"))
    blurred = jnp.where(inside[:, None, None], blurred, 0.0)
    edge_wide = edge_from(blurred)
    edge_wide = jnp.where(inside[1:-1, None, None], edge_wide, 0.0)
    edge = edge_wide[1:-1]
    slope = central_grads(edge_wide)

    def step(field, scale_level, scale_step):
        padded = extended_2(field, (("gx", 0),), HALO)
        padded = jnp.pad(padded, ((0, 0), (SUB, SUB), (0, 0)))
        return stage(padded, edge, slope, level_set, scale_level, scale_step)

    section_one = step(level_set, None, None)
    section_two = step(section_one, 0.75, 0.25)
    advanced = step(section_two, 1.0 / 3.0, 2.0 / 3.0)
    return (edge, advanced)


def solution(mesh):
    return jax.shard_map(
        shards,
        mesh=mesh,
        in_specs=(P(("grp", "gx"), None, None), P(("grp", "gx"), None, None)),
        out_specs=(P(("grp", "gx"), None, None), P(("grp", "gx"), None, None)),
        check_vma=False,
    )
```

```python
import math

import numpy as np

import jax
import jax.numpy as jnp
from jax import lax
from jax.experimental import pallas as pl
from jax.experimental.pallas import tpu as pltpu
from jax.sharding import PartitionSpec as P

RADIUS = 12


def shifted(block, axis, distance):
    devices = range(lax.axis_size(axis))
    route = [(i - distance, i) for i in devices if i - distance in devices]
    return lax.ppermute(block, axis, route)


def extended_2(block, sides, width):
    for axis, dim in sides:
        count = lax.axis_size(axis)
        forward = [(i, i + 1) for i in range(count - 1)]
        backward = [(target, source) for source, target in forward]
        low = lax.ppermute(
            lax.slice_in_dim(block, block.shape[dim] - width, None, axis=dim), axis, forward
        )
        high = lax.ppermute(lax.slice_in_dim(block, 0, width, axis=dim), axis, backward)
        block = jnp.concatenate([low, block, high], axis=dim)
    return block


def blur_taps():
    raw = [math.exp(-(offset * offset) / 18.0) for offset in range(-RADIUS, RADIUS + 1)]
    total = sum(raw)
    return [value / total for value in raw]


def band(rows, cols, shift):
    taps = blur_taps()
    table = np.zeros((rows, cols), np.float32)
    for i in range(rows):
        for k in range(-RADIUS, RADIUS + 1):
            j = i + shift + k
            if 0 <= j < cols:
                table[i, j] = taps[k + RADIUS]
    return jnp.asarray(table)


def pad_axis(array, axis, width):
    widths = [(0, 0), (0, 0), (0, 0)]
    widths[axis] = (width, width)
    return jnp.pad(array, widths)


def blur_padded(padded, axis, count):
    taps = blur_taps()
    result = taps[0] * lax.slice_in_dim(padded, 0, count, axis=axis)
    for offset in range(1, len(taps)):
        result = result + taps[offset] * lax.slice_in_dim(padded, offset, offset + count, axis=axis)
    return result


def central_grads(padded):
    inner = padded[1:-1]
    side = jnp.pad(inner, ((0, 0), (1, 1), (1, 1)))
    grad_x = (padded[2:] - padded[:-2]) * 0.5
    grad_y = (side[:, 2:, 1:-1] - side[:, :-2, 1:-1]) * 0.5
    grad_z = (side[:, 1:-1, 2:] - side[:, 1:-1, :-2]) * 0.5
    return (grad_x, grad_y, grad_z)


def edge_from(padded):
    grad_x, grad_y, grad_z = central_grads(padded)
    return 1.0 / (1.0 + 6000.0 * (grad_x * grad_x + grad_y * grad_y + grad_z * grad_z))


def weno(first, second, third, fourth, fifth):
    cand_one = 2.0 * first - 7.0 * second + 11.0 * third
    cand_two = -second + 5.0 * third + 2.0 * fourth
    cand_three = 2.0 * third + 5.0 * fourth - fifth
    part_a = first - 2.0 * second + third
    part_b = first - 4.0 * second + 3.0 * third
    smooth_one = 13.0 / 12.0 * part_a * part_a + 0.25 * part_b * part_b
    part_a = second - 2.0 * third + fourth
    part_b = second - fourth
    smooth_two = 13.0 / 12.0 * part_a * part_a + 0.25 * part_b * part_b
    part_a = third - 2.0 * fourth + fifth
    part_b = 3.0 * third - 4.0 * fourth + fifth
    smooth_three = 13.0 / 12.0 * part_a * part_a + 0.25 * part_b * part_b
    denom_one = 1e-06 + smooth_one
    denom_two = 1e-06 + smooth_two
    denom_three = 1e-06 + smooth_three
    square_one = denom_one * denom_one
    square_two = denom_two * denom_two
    square_three = denom_three * denom_three
    weight_one = 0.1 * (square_two * square_three)
    weight_two = 0.6 * (square_one * square_three)
    weight_three = 0.3 * (square_one * square_two)
    return (weight_one * cand_one + weight_two * cand_two + weight_three * cand_three) / (
        6.0 * (weight_one + weight_two + weight_three)
    )


def upwind(values, speed):
    diffs = [values[k + 1] - values[k] for k in range(6)]
    ahead = speed > 0.0
    chosen = [jnp.where(ahead, diffs[k], diffs[5 - k]) for k in range(5)]
    return speed * weno(*chosen)


SUB = 8
HALO = 3


def stage_kernel(scale_level, scale_step, rows_block):
    def kernel(
        low_ref, main_ref, high_ref, edge_ref, sx_ref, sy_ref, sz_ref, ls_ref, out_ref, p_ref, sems
    ):
        rows = main_ref.shape[0]
        rows_y = out_ref.shape[1]
        rows_z = out_ref.shape[2]
        block = pl.program_id(0)

        @pl.when(block == 0)
        def _():
            inner = pl.ds(SUB, rows_y)
            copies = [
                pltpu.make_async_copy(low_ref, p_ref.at[pl.ds(0, HALO), inner, :], sems.at[0]),
                pltpu.make_async_copy(main_ref, p_ref.at[pl.ds(HALO, rows), inner, :], sems.at[1]),
                pltpu.make_async_copy(
                    high_ref, p_ref.at[pl.ds(HALO + rows, HALO), inner, :], sems.at[2]
                ),
            ]
            for copy in copies:
                copy.start()
            zeros = jnp.zeros((SUB, rows_z), jnp.float32)

            def clear(x, carry):
                p_ref[x, pl.ds(0, SUB), :] = zeros
                p_ref[x, pl.ds(SUB + rows_y, SUB), :] = zeros
                return carry

            lax.fori_loop(0, rows + 2 * HALO, clear, 0)
            for copy in copies:
                copy.wait()
        lane = lax.broadcasted_iota(jnp.int32, (SUB, rows_z), 1)

        def along_z(tile, step):
            moved = pltpu.roll(tile, (-step) % rows_z, 1)
            keep = (lane + step >= 0) & (lane + step < rows_z)
            return jnp.where(keep, moved, 0.0)

        def row(r, carry):
            centre_row = block * rows_block + r + HALO
            for chunk in range(rows_y // SUB):
                top = SUB + chunk * SUB

                def at(step_x, step_y):
                    return p_ref[centre_row + step_x, pl.ds(top + step_y, SUB), :]

                centre = at(0, 0)
                line_x = [at(k, 0) for k in range(-HALO, HALO + 1)]
                line_y = [at(0, k) for k in range(-HALO, HALO + 1)]
                line_z = [along_z(centre, k) for k in range(-HALO, HALO + 1)]
                here = pl.ds(chunk * SUB, SUB)
                speed_x = -sx_ref[r, here, :]
                speed_y = -sy_ref[r, here, :]
                speed_z = -sz_ref[r, here, :]
                flow_x = upwind(line_x, speed_x)
                flow_y = upwind(line_y, speed_y)
                flow_z = upwind(line_z, speed_z)
                up_x = line_x[HALO + 1]
                down_x = line_x[HALO - 1]
                up_y = line_y[HALO + 1]
                down_y = line_y[HALO - 1]
                up_z = line_z[HALO + 1]
                down_z = line_z[HALO - 1]
                first_x = (up_x - down_x) * 0.5
                first_y = (up_y - down_y) * 0.5
                first_z = (up_z - down_z) * 0.5
                second_xx = up_x - 2.0 * centre + down_x
                second_yy = up_y - 2.0 * centre + down_y
                second_zz = up_z - 2.0 * centre + down_z
                mixed_xy = (at(1, 1) - at(1, -1) - at(-1, 1) + at(-1, -1)) * 0.25
                mixed_xz = (
                    along_z(up_x, 1) - along_z(up_x, -1) - along_z(down_x, 1) + along_z(down_x, -1)
                ) * 0.25
                mixed_yz = (
                    along_z(up_y, 1) - along_z(up_y, -1) - along_z(down_y, 1) + along_z(down_y, -1)
                ) * 0.25
                square_x = first_x * first_x
                square_y = first_y * first_y
                square_z = first_z * first_z
                numerator = (
                    second_xx * (square_y + square_z)
                    + second_yy * (square_x + square_z)
                    + second_zz * (square_x + square_y)
                )
                numerator = numerator - 2.0 * (
                    first_x * first_y * mixed_xy
                    + first_x * first_z * mixed_xz
                    + first_y * first_z * mixed_yz
                )
                curvature = numerator / (square_x + square_y + square_z + 1.0)
                transport = flow_x + flow_y + flow_z
                rate = edge_ref[r, here, :] * curvature - transport
                moved = centre + 0.1 * rate
                if scale_level is None:
                    out_ref[r, here, :] = moved
                else:
                    out_ref[r, here, :] = scale_level * ls_ref[r, here, :] + scale_step * moved
            return carry

        lax.fori_loop(0, rows_block, row, 0)

    return kernel


def stage(low, field, high, edge, slope, level_set, scale_level, scale_step):
    rows, rows_y, rows_z = level_set.shape
    rows_block = SUB if rows % SUB == 0 else rows
    raw = pl.BlockSpec(memory_space=pl.ANY)
    part = pl.BlockSpec((rows_block, rows_y, rows_z), lambda i: (i, 0, 0))
    return pl.pallas_call(
        stage_kernel(scale_level, scale_step, rows_block),
        grid=(rows // rows_block,),
        in_specs=[raw, raw, raw, part, part, part, part, part],
        out_specs=part,
        out_shape=jax.ShapeDtypeStruct(level_set.shape, level_set.dtype),
        scratch_shapes=[
            pltpu.VMEM((rows + 2 * HALO, rows_y + 2 * SUB, rows_z), jnp.float32),
            pltpu.SemaphoreType.DMA((3,)),
        ],
        compiler_params=pltpu.CompilerParams(dimension_semantics=("arbitrary",)),
    )(low, field, high, edge, slope[0], slope[1], slope[2], level_set)


def shards(volume, level_set):
    rows, rows_y, rows_z = volume.shape
    exact = lax.Precision.HIGHEST
    halo = min(rows, RADIUS + 2)
    low = shifted(volume[rows - halo :], "gx", 1)
    high = shifted(volume[:halo], "gx", -1)
    extended = jnp.concatenate([low, volume, high], axis=0)
    wide = rows + 4
    blurred = jnp.dot(
        band(wide, extended.shape[0], halo - 2),
        extended.reshape(extended.shape[0], rows_y * rows_z),
        precision=exact,
    )
    blurred = jnp.dot(
        blurred.reshape(wide * rows_y, rows_z), band(rows_z, rows_z, 0).T, precision=exact
    ).reshape(wide, rows_y, rows_z)
    blurred = jnp.einsum("yv,xvz->xyz", band(rows_y, rows_y, 0), blurred, precision=exact)
    positions = lax.axis_index("gx") * rows - 2 + jnp.arange(wide, dtype=jnp.int32)
    inside = (positions >= 0) & (positions < rows * lax.axis_size("gx"))
    blurred = jnp.where(inside[:, None, None], blurred, 0.0)
    edge_wide = edge_from(blurred)
    edge_wide = jnp.where(inside[1:-1, None, None], edge_wide, 0.0)
    edge = edge_wide[1:-1]
    slope = central_grads(edge_wide)

    def step(field, scale_level, scale_step):
        low = shifted(field[rows - HALO :], "gx", 1)
        high = shifted(field[:HALO], "gx", -1)
        return stage(low, field, high, edge, slope, level_set, scale_level, scale_step)

    section_one = step(level_set, None, None)
    section_two = step(section_one, 0.75, 0.25)
    advanced = step(section_two, 1.0 / 3.0, 2.0 / 3.0)
    return (edge, advanced)


def solution(mesh):
    return jax.shard_map(
        shards,
        mesh=mesh,
        in_specs=(P(("grp", "gx"), None, None), P(("grp", "gx"), None, None)),
        out_specs=(P(("grp", "gx"), None, None), P(("grp", "gx"), None, None)),
        check_vma=False,
    )
```

```python
import math

import numpy as np

import jax
import jax.numpy as jnp
from jax import lax
from jax.experimental import pallas as pl
from jax.experimental.pallas import tpu as pltpu
from jax.sharding import PartitionSpec as P

RADIUS = 12


def shifted(block, axis, distance):
    devices = range(lax.axis_size(axis))
    route = [(i - distance, i) for i in devices if i - distance in devices]
    return lax.ppermute(block, axis, route)


def extended_2(block, sides, width):
    for axis, dim in sides:
        count = lax.axis_size(axis)
        forward = [(i, i + 1) for i in range(count - 1)]
        backward = [(target, source) for source, target in forward]
        low = lax.ppermute(
            lax.slice_in_dim(block, block.shape[dim] - width, None, axis=dim), axis, forward
        )
        high = lax.ppermute(lax.slice_in_dim(block, 0, width, axis=dim), axis, backward)
        block = jnp.concatenate([low, block, high], axis=dim)
    return block


def blur_taps():
    raw = [math.exp(-(offset * offset) / 18.0) for offset in range(-RADIUS, RADIUS + 1)]
    total = sum(raw)
    return [value / total for value in raw]


def band(rows, cols, shift):
    taps = blur_taps()
    table = np.zeros((rows, cols), np.float32)
    for i in range(rows):
        for k in range(-RADIUS, RADIUS + 1):
            j = i + shift + k
            if 0 <= j < cols:
                table[i, j] = taps[k + RADIUS]
    return jnp.asarray(table)


def pad_axis(array, axis, width):
    widths = [(0, 0), (0, 0), (0, 0)]
    widths[axis] = (width, width)
    return jnp.pad(array, widths)


def blur_padded(padded, axis, count):
    taps = blur_taps()
    result = taps[0] * lax.slice_in_dim(padded, 0, count, axis=axis)
    for offset in range(1, len(taps)):
        result = result + taps[offset] * lax.slice_in_dim(padded, offset, offset + count, axis=axis)
    return result


def central_grads(padded):
    inner = padded[1:-1]
    side = jnp.pad(inner, ((0, 0), (1, 1), (1, 1)))
    grad_x = (padded[2:] - padded[:-2]) * 0.5
    grad_y = (side[:, 2:, 1:-1] - side[:, :-2, 1:-1]) * 0.5
    grad_z = (side[:, 1:-1, 2:] - side[:, 1:-1, :-2]) * 0.5
    return (grad_x, grad_y, grad_z)


def edge_from(padded):
    grad_x, grad_y, grad_z = central_grads(padded)
    return 1.0 / (1.0 + 6000.0 * (grad_x * grad_x + grad_y * grad_y + grad_z * grad_z))


def weno(first, second, third, fourth, fifth):
    cand_one = 2.0 * first - 7.0 * second + 11.0 * third
    cand_two = -second + 5.0 * third + 2.0 * fourth
    cand_three = 2.0 * third + 5.0 * fourth - fifth
    part_a = first - 2.0 * second + third
    part_b = first - 4.0 * second + 3.0 * third
    smooth_one = 13.0 / 12.0 * part_a * part_a + 0.25 * part_b * part_b
    part_a = second - 2.0 * third + fourth
    part_b = second - fourth
    smooth_two = 13.0 / 12.0 * part_a * part_a + 0.25 * part_b * part_b
    part_a = third - 2.0 * fourth + fifth
    part_b = 3.0 * third - 4.0 * fourth + fifth
    smooth_three = 13.0 / 12.0 * part_a * part_a + 0.25 * part_b * part_b
    denom_one = 1e-06 + smooth_one
    denom_two = 1e-06 + smooth_two
    denom_three = 1e-06 + smooth_three
    square_one = denom_one * denom_one
    square_two = denom_two * denom_two
    square_three = denom_three * denom_three
    weight_one = 0.1 * (square_two * square_three)
    weight_two = 0.6 * (square_one * square_three)
    weight_three = 0.3 * (square_one * square_two)
    return (weight_one * cand_one + weight_two * cand_two + weight_three * cand_three) / (
        6.0 * (weight_one + weight_two + weight_three)
    )


def upwind(values, speed):
    diffs = [values[k + 1] - values[k] for k in range(6)]
    ahead = speed > 0.0
    chosen = [jnp.where(ahead, diffs[k], diffs[5 - k]) for k in range(5)]
    return speed * weno(*chosen)


SUB = 8
HALO = 3


def stage_kernel(scale_level, scale_step, rows_block, block_of, edges):
    def kernel(*refs):
        if edges:
            low_ref, main_ref, high_ref = refs[:3]
            rest = refs[3:]
        else:
            main_ref = refs[0]
            rest = refs[1:]
        edge_ref, sx_ref, sy_ref, sz_ref, ls_ref = rest[:5]
        out_ref, p_ref, sems = rest[-3:]
        rows = main_ref.shape[0]
        rows_y = out_ref.shape[1]
        rows_z = out_ref.shape[2]
        block = pl.program_id(0)

        @pl.when(block == 0)
        def _():
            inner = pl.ds(SUB, rows_y)
            copies = [
                pltpu.make_async_copy(main_ref, p_ref.at[pl.ds(HALO, rows), inner, :], sems.at[1])
            ]
            if edges:
                copies.append(
                    pltpu.make_async_copy(low_ref, p_ref.at[pl.ds(0, HALO), inner, :], sems.at[0])
                )
                copies.append(
                    pltpu.make_async_copy(
                        high_ref, p_ref.at[pl.ds(HALO + rows, HALO), inner, :], sems.at[2]
                    )
                )
            for copy in copies:
                copy.start()
            zeros = jnp.zeros((SUB, rows_z), jnp.float32)

            def clear(x, carry):
                p_ref[x, pl.ds(0, SUB), :] = zeros
                p_ref[x, pl.ds(SUB + rows_y, SUB), :] = zeros
                return carry

            lax.fori_loop(0, rows + 2 * HALO, clear, 0)
            for copy in copies:
                copy.wait()

        lane = lax.broadcasted_iota(jnp.int32, (SUB, rows_z), 1)

        def along_z(tile, step):
            moved = pltpu.roll(tile, (-step) % rows_z, 1)
            keep = (lane + step >= 0) & (lane + step < rows_z)
            return jnp.where(keep, moved, 0.0)

        def row(r, carry):
            centre_row = block_of(block) * rows_block + r + HALO
            for chunk in range(rows_y // SUB):
                top = SUB + chunk * SUB

                def at(step_x, step_y):
                    return p_ref[centre_row + step_x, pl.ds(top + step_y, SUB), :]

                centre = at(0, 0)
                line_x = [at(k, 0) for k in range(-HALO, HALO + 1)]
                line_y = [at(0, k) for k in range(-HALO, HALO + 1)]
                line_z = [along_z(centre, k) for k in range(-HALO, HALO + 1)]
                here = pl.ds(chunk * SUB, SUB)
                speed_x = -sx_ref[r, here, :]
                speed_y = -sy_ref[r, here, :]
                speed_z = -sz_ref[r, here, :]
                flow_x = upwind(line_x, speed_x)
                flow_y = upwind(line_y, speed_y)
                flow_z = upwind(line_z, speed_z)
                up_x = line_x[HALO + 1]
                down_x = line_x[HALO - 1]
                up_y = line_y[HALO + 1]
                down_y = line_y[HALO - 1]
                up_z = line_z[HALO + 1]
                down_z = line_z[HALO - 1]
                first_x = (up_x - down_x) * 0.5
                first_y = (up_y - down_y) * 0.5
                first_z = (up_z - down_z) * 0.5
                second_xx = up_x - 2.0 * centre + down_x
                second_yy = up_y - 2.0 * centre + down_y
                second_zz = up_z - 2.0 * centre + down_z
                mixed_xy = (at(1, 1) - at(1, -1) - at(-1, 1) + at(-1, -1)) * 0.25
                mixed_xz = (
                    along_z(up_x, 1) - along_z(up_x, -1) - along_z(down_x, 1) + along_z(down_x, -1)
                ) * 0.25
                mixed_yz = (
                    along_z(up_y, 1) - along_z(up_y, -1) - along_z(down_y, 1) + along_z(down_y, -1)
                ) * 0.25
                square_x = first_x * first_x
                square_y = first_y * first_y
                square_z = first_z * first_z
                numerator = (
                    second_xx * (square_y + square_z)
                    + second_yy * (square_x + square_z)
                    + second_zz * (square_x + square_y)
                )
                numerator = numerator - 2.0 * (
                    first_x * first_y * mixed_xy
                    + first_x * first_z * mixed_xz
                    + first_y * first_z * mixed_yz
                )
                curvature = numerator / (square_x + square_y + square_z + 1.0)
                transport = flow_x + flow_y + flow_z
                rate = edge_ref[r, here, :] * curvature - transport
                moved = centre + 0.1 * rate
                if scale_level is None:
                    out_ref[r, here, :] = moved
                else:
                    out_ref[r, here, :] = scale_level * ls_ref[r, here, :] + scale_step * moved
            return carry

        lax.fori_loop(0, rows_block, row, 0)

    return kernel


def stage_call(inputs, prior, level_set, scale_level, scale_step, blocks, block_of, edges):
    rows, rows_y, rows_z = level_set.shape
    rows_block = SUB if rows % SUB == 0 else rows
    raw = pl.BlockSpec(memory_space=pl.ANY)
    part = pl.BlockSpec((rows_block, rows_y, rows_z), lambda i: (block_of(i), 0, 0))
    count = len(inputs)
    specs = [raw] * count + [part] * 5
    operands = list(inputs)
    aliases = {}
    if prior is not None:
        specs.append(raw)
        aliases = {count + 5: 0}
    return pl.pallas_call(
        stage_kernel(scale_level, scale_step, rows_block, block_of, edges),
        grid=(blocks,),
        in_specs=specs,
        out_specs=part,
        out_shape=jax.ShapeDtypeStruct(level_set.shape, level_set.dtype),
        scratch_shapes=[
            pltpu.VMEM((rows + 2 * HALO, rows_y + 2 * SUB, rows_z), jnp.float32),
            pltpu.SemaphoreType.DMA((3,)),
        ],
        input_output_aliases=aliases,
        compiler_params=pltpu.CompilerParams(dimension_semantics=("arbitrary",)),
    ), operands


def stage(low, field, high, edge, slope, level_set, scale_level, scale_step):
    rows = level_set.shape[0]
    blocks = rows // SUB
    extras = (edge, slope[0], slope[1], slope[2], level_set)
    if rows % SUB != 0 or blocks < 3 or HALO > SUB:
        call, operands = stage_call(
            (low, field, high), None, level_set, scale_level, scale_step, 1, lambda i: 0, True
        )
        return call(*operands, *extras)
    call, operands = stage_call(
        (field,), None, level_set, scale_level, scale_step, blocks - 2, lambda i: i + 1, False
    )
    middle = call(*operands, *extras)
    call, operands = stage_call(
        (low, field, high),
        middle,
        level_set,
        scale_level,
        scale_step,
        2,
        lambda i: i * (blocks - 1),
        True,
    )
    return call(*operands, *extras, middle)


def shards(volume, level_set):
    rows, rows_y, rows_z = volume.shape
    exact = lax.Precision.HIGHEST
    halo = min(rows, RADIUS + 2)
    low = shifted(volume[rows - halo :], "gx", 1)
    high = shifted(volume[:halo], "gx", -1)
    extended = jnp.concatenate([low, volume, high], axis=0)
    wide = rows + 4
    blurred = jnp.dot(
        band(wide, extended.shape[0], halo - 2),
        extended.reshape(extended.shape[0], rows_y * rows_z),
        precision=exact,
    )
    blurred = jnp.dot(
        blurred.reshape(wide * rows_y, rows_z), band(rows_z, rows_z, 0).T, precision=exact
    ).reshape(wide, rows_y, rows_z)
    blurred = jnp.einsum("yv,xvz->xyz", band(rows_y, rows_y, 0), blurred, precision=exact)
    positions = lax.axis_index("gx") * rows - 2 + jnp.arange(wide, dtype=jnp.int32)
    inside = (positions >= 0) & (positions < rows * lax.axis_size("gx"))
    blurred = jnp.where(inside[:, None, None], blurred, 0.0)
    edge_wide = edge_from(blurred)
    edge_wide = jnp.where(inside[1:-1, None, None], edge_wide, 0.0)
    edge = edge_wide[1:-1]
    slope = central_grads(edge_wide)

    def step(field, scale_level, scale_step):
        low = shifted(field[rows - HALO :], "gx", 1)
        high = shifted(field[:HALO], "gx", -1)
        return stage(low, field, high, edge, slope, level_set, scale_level, scale_step)

    section_one = step(level_set, None, None)
    section_two = step(section_one, 0.75, 0.25)
    advanced = step(section_two, 1.0 / 3.0, 2.0 / 3.0)
    return (edge, advanced)


def solution(mesh):
    return jax.shard_map(
        shards,
        mesh=mesh,
        in_specs=(P(("grp", "gx"), None, None), P(("grp", "gx"), None, None)),
        out_specs=(P(("grp", "gx"), None, None), P(("grp", "gx"), None, None)),
        check_vma=False,
    )
```

```python
import math

import numpy as np

import jax
import jax.numpy as jnp
from jax import lax
from jax.experimental import pallas as pl
from jax.experimental.pallas import tpu as pltpu
from jax.sharding import PartitionSpec as P

RADIUS = 12


def shifted(block, axis, distance):
    devices = range(lax.axis_size(axis))
    route = [(i - distance, i) for i in devices if i - distance in devices]
    return lax.ppermute(block, axis, route)


def extended_2(block, sides, width):
    for axis, dim in sides:
        count = lax.axis_size(axis)
        forward = [(i, i + 1) for i in range(count - 1)]
        backward = [(target, source) for source, target in forward]
        low = lax.ppermute(
            lax.slice_in_dim(block, block.shape[dim] - width, None, axis=dim), axis, forward
        )
        high = lax.ppermute(lax.slice_in_dim(block, 0, width, axis=dim), axis, backward)
        block = jnp.concatenate([low, block, high], axis=dim)
    return block


def blur_taps():
    raw = [math.exp(-(offset * offset) / 18.0) for offset in range(-RADIUS, RADIUS + 1)]
    total = sum(raw)
    return [value / total for value in raw]


def band(rows, cols, shift):
    taps = blur_taps()
    table = np.zeros((rows, cols), np.float32)
    for i in range(rows):
        for k in range(-RADIUS, RADIUS + 1):
            j = i + shift + k
            if 0 <= j < cols:
                table[i, j] = taps[k + RADIUS]
    return jnp.asarray(table)


def pad_axis(array, axis, width):
    widths = [(0, 0), (0, 0), (0, 0)]
    widths[axis] = (width, width)
    return jnp.pad(array, widths)


def blur_padded(padded, axis, count):
    taps = blur_taps()
    result = taps[0] * lax.slice_in_dim(padded, 0, count, axis=axis)
    for offset in range(1, len(taps)):
        result = result + taps[offset] * lax.slice_in_dim(padded, offset, offset + count, axis=axis)
    return result


def central_grads(padded):
    inner = padded[1:-1]
    side = jnp.pad(inner, ((0, 0), (1, 1), (1, 1)))
    grad_x = (padded[2:] - padded[:-2]) * 0.5
    grad_y = (side[:, 2:, 1:-1] - side[:, :-2, 1:-1]) * 0.5
    grad_z = (side[:, 1:-1, 2:] - side[:, 1:-1, :-2]) * 0.5
    return (grad_x, grad_y, grad_z)


def edge_from(padded):
    grad_x, grad_y, grad_z = central_grads(padded)
    return 1.0 / (1.0 + 6000.0 * (grad_x * grad_x + grad_y * grad_y + grad_z * grad_z))


def weno(first, second, third, fourth, fifth):
    step_one = second - first
    step_two = third - second
    step_three = fourth - third
    step_four = fifth - fourth
    cand_one = 2.0 * first - 7.0 * second + 11.0 * third
    cand_two = -second + 5.0 * third + 2.0 * fourth
    cand_three = 2.0 * third + 5.0 * fourth - fifth
    part_a = step_two - step_one
    part_b = 3.0 * step_two - step_one
    smooth_one = 13.0 / 12.0 * part_a * part_a + 0.25 * part_b * part_b
    part_a = step_three - step_two
    part_b = step_two + step_three
    smooth_two = 13.0 / 12.0 * part_a * part_a + 0.25 * part_b * part_b
    part_a = step_four - step_three
    part_b = step_four - 3.0 * step_three
    smooth_three = 13.0 / 12.0 * part_a * part_a + 0.25 * part_b * part_b
    denom_one = 1e-06 + smooth_one
    denom_two = 1e-06 + smooth_two
    denom_three = 1e-06 + smooth_three
    square_one = denom_one * denom_one
    square_two = denom_two * denom_two
    square_three = denom_three * denom_three
    weight_one = 0.1 * (square_two * square_three)
    weight_two = 0.6 * (square_one * square_three)
    weight_three = 0.3 * (square_one * square_two)
    return (weight_one * cand_one + weight_two * cand_two + weight_three * cand_three) / (
        6.0 * (weight_one + weight_two + weight_three)
    )


def upwind(values, slope):
    diffs = [values[k + 1] - values[k] for k in range(6)]
    ahead = slope < 0.0
    chosen = [jnp.where(ahead, diffs[k], diffs[5 - k]) for k in range(5)]
    return slope * weno(*chosen)


SUB = 8
HALO = 3


def stage_kernel(scale_level, scale_step, rows_block):
    def kernel(
        low_ref, main_ref, high_ref, edge_ref, sx_ref, sy_ref, sz_ref, ls_ref, out_ref, p_ref, sems
    ):
        rows = main_ref.shape[0]
        rows_y = out_ref.shape[1]
        rows_z = out_ref.shape[2]
        block = pl.program_id(0)

        @pl.when(block == 0)
        def _():
            inner = pl.ds(SUB, rows_y)
            copies = [
                pltpu.make_async_copy(low_ref, p_ref.at[pl.ds(0, HALO), inner, :], sems.at[0]),
                pltpu.make_async_copy(main_ref, p_ref.at[pl.ds(HALO, rows), inner, :], sems.at[1]),
                pltpu.make_async_copy(
                    high_ref, p_ref.at[pl.ds(HALO + rows, HALO), inner, :], sems.at[2]
                ),
            ]
            for copy in copies:
                copy.start()
            zeros = jnp.zeros((SUB, rows_z), jnp.float32)

            def clear(x, carry):
                p_ref[x, pl.ds(0, SUB), :] = zeros
                p_ref[x, pl.ds(SUB + rows_y, SUB), :] = zeros
                return carry

            lax.fori_loop(0, rows + 2 * HALO, clear, 0)
            for copy in copies:
                copy.wait()
        lane = lax.broadcasted_iota(jnp.int32, (SUB, rows_z), 1)

        def along_z(tile, step):
            moved = pltpu.roll(tile, (-step) % rows_z, 1)
            keep = lane < rows_z - step if step > 0 else lane >= -step
            return jnp.where(keep, moved, 0.0)

        def row(r, carry):
            centre_row = block * rows_block + r + HALO
            for chunk in range(rows_y // SUB):
                top = SUB + chunk * SUB

                def at(step_x, step_y):
                    return p_ref[centre_row + step_x, pl.ds(top + step_y, SUB), :]

                centre = at(0, 0)
                line_x = [at(k, 0) for k in range(-HALO, HALO + 1)]
                line_y = [at(0, k) for k in range(-HALO, HALO + 1)]
                line_z = [along_z(centre, k) for k in range(-HALO, HALO + 1)]
                here = pl.ds(chunk * SUB, SUB)
                flow_x = upwind(line_x, sx_ref[r, here, :])
                flow_y = upwind(line_y, sy_ref[r, here, :])
                flow_z = upwind(line_z, sz_ref[r, here, :])
                up_x = line_x[HALO + 1]
                down_x = line_x[HALO - 1]
                up_y = line_y[HALO + 1]
                down_y = line_y[HALO - 1]
                up_z = line_z[HALO + 1]
                down_z = line_z[HALO - 1]
                first_x = (up_x - down_x) * 0.5
                first_y = (up_y - down_y) * 0.5
                first_z = (up_z - down_z) * 0.5
                second_xx = up_x - 2.0 * centre + down_x
                second_yy = up_y - 2.0 * centre + down_y
                second_zz = up_z - 2.0 * centre + down_z
                mixed_xy = (at(1, 1) - at(1, -1) - at(-1, 1) + at(-1, -1)) * 0.25
                across_x = up_x - down_x
                across_y = up_y - down_y
                mixed_xz = (along_z(across_x, 1) - along_z(across_x, -1)) * 0.25
                mixed_yz = (along_z(across_y, 1) - along_z(across_y, -1)) * 0.25
                square_x = first_x * first_x
                square_y = first_y * first_y
                square_z = first_z * first_z
                numerator = (
                    second_xx * (square_y + square_z)
                    + second_yy * (square_x + square_z)
                    + second_zz * (square_x + square_y)
                )
                numerator = numerator - 2.0 * (
                    first_x * first_y * mixed_xy
                    + first_x * first_z * mixed_xz
                    + first_y * first_z * mixed_yz
                )
                curvature = numerator / (square_x + square_y + square_z + 1.0)
                rate = edge_ref[r, here, :] * curvature + (flow_x + flow_y + flow_z)
                moved = centre + 0.1 * rate
                if scale_level is None:
                    out_ref[r, here, :] = moved
                else:
                    out_ref[r, here, :] = scale_level * ls_ref[r, here, :] + scale_step * moved
            return carry

        lax.fori_loop(0, rows_block, row, 0)

    return kernel


def stage(low, field, high, edge, slope, level_set, scale_level, scale_step):
    rows, rows_y, rows_z = level_set.shape
    rows_block = SUB if rows % SUB == 0 else rows
    raw = pl.BlockSpec(memory_space=pl.ANY)
    part = pl.BlockSpec((rows_block, rows_y, rows_z), lambda i: (i, 0, 0))
    return pl.pallas_call(
        stage_kernel(scale_level, scale_step, rows_block),
        grid=(rows // rows_block,),
        in_specs=[raw, raw, raw, part, part, part, part, part],
        out_specs=part,
        out_shape=jax.ShapeDtypeStruct(level_set.shape, level_set.dtype),
        scratch_shapes=[
            pltpu.VMEM((rows + 2 * HALO, rows_y + 2 * SUB, rows_z), jnp.float32),
            pltpu.SemaphoreType.DMA((3,)),
        ],
        compiler_params=pltpu.CompilerParams(dimension_semantics=("arbitrary",)),
    )(low, field, high, edge, slope[0], slope[1], slope[2], level_set)


def shards(volume, level_set):
    rows, rows_y, rows_z = volume.shape
    exact = lax.Precision.HIGHEST
    halo = min(rows, RADIUS + 2)
    low = shifted(volume[rows - halo :], "gx", 1)
    high = shifted(volume[:halo], "gx", -1)
    extended = jnp.concatenate([low, volume, high], axis=0)
    wide = rows + 4
    blurred = jnp.dot(
        band(wide, extended.shape[0], halo - 2),
        extended.reshape(extended.shape[0], rows_y * rows_z),
        precision=exact,
    )
    blurred = jnp.dot(
        blurred.reshape(wide * rows_y, rows_z), band(rows_z, rows_z, 0).T, precision=exact
    ).reshape(wide, rows_y, rows_z)
    blurred = jnp.einsum("yv,xvz->xyz", band(rows_y, rows_y, 0), blurred, precision=exact)
    positions = lax.axis_index("gx") * rows - 2 + jnp.arange(wide, dtype=jnp.int32)
    inside = (positions >= 0) & (positions < rows * lax.axis_size("gx"))
    blurred = jnp.where(inside[:, None, None], blurred, 0.0)
    edge_wide = edge_from(blurred)
    edge_wide = jnp.where(inside[1:-1, None, None], edge_wide, 0.0)
    edge = edge_wide[1:-1]
    slope = central_grads(edge_wide)

    def step(field, scale_level, scale_step):
        low = shifted(field[rows - HALO :], "gx", 1)
        high = shifted(field[:HALO], "gx", -1)
        return stage(low, field, high, edge, slope, level_set, scale_level, scale_step)

    section_one = step(level_set, None, None)
    section_two = step(section_one, 0.75, 0.25)
    advanced = step(section_two, 1.0 / 3.0, 2.0 / 3.0)
    return (edge, advanced)


def solution(mesh):
    return jax.shard_map(
        shards,
        mesh=mesh,
        in_specs=(P(("grp", "gx"), None, None), P(("grp", "gx"), None, None)),
        out_specs=(P(("grp", "gx"), None, None), P(("grp", "gx"), None, None)),
        check_vma=False,
    )
```

```python
import math

import numpy as np

import jax
import jax.numpy as jnp
from jax import lax
from jax.experimental import pallas as pl
from jax.experimental.pallas import tpu as pltpu
from jax.sharding import PartitionSpec as P

RADIUS = 12


def shifted(block, axis, distance):
    devices = range(lax.axis_size(axis))
    route = [(i - distance, i) for i in devices if i - distance in devices]
    return lax.ppermute(block, axis, route)


def extended_2(block, sides, width):
    for axis, dim in sides:
        count = lax.axis_size(axis)
        forward = [(i, i + 1) for i in range(count - 1)]
        backward = [(target, source) for source, target in forward]
        low = lax.ppermute(
            lax.slice_in_dim(block, block.shape[dim] - width, None, axis=dim), axis, forward
        )
        high = lax.ppermute(lax.slice_in_dim(block, 0, width, axis=dim), axis, backward)
        block = jnp.concatenate([low, block, high], axis=dim)
    return block


def blur_taps():
    raw = [math.exp(-(offset * offset) / 18.0) for offset in range(-RADIUS, RADIUS + 1)]
    total = sum(raw)
    return [value / total for value in raw]


def band(rows, cols, shift):
    taps = blur_taps()
    table = np.zeros((rows, cols), np.float32)
    for i in range(rows):
        for k in range(-RADIUS, RADIUS + 1):
            j = i + shift + k
            if 0 <= j < cols:
                table[i, j] = taps[k + RADIUS]
    return jnp.asarray(table)


def pad_axis(array, axis, width):
    widths = [(0, 0), (0, 0), (0, 0)]
    widths[axis] = (width, width)
    return jnp.pad(array, widths)


def blur_padded(padded, axis, count):
    taps = blur_taps()
    result = taps[0] * lax.slice_in_dim(padded, 0, count, axis=axis)
    for offset in range(1, len(taps)):
        result = result + taps[offset] * lax.slice_in_dim(padded, offset, offset + count, axis=axis)
    return result


def central_grads(padded):
    inner = padded[1:-1]
    side = jnp.pad(inner, ((0, 0), (1, 1), (1, 1)))
    grad_x = (padded[2:] - padded[:-2]) * 0.5
    grad_y = (side[:, 2:, 1:-1] - side[:, :-2, 1:-1]) * 0.5
    grad_z = (side[:, 1:-1, 2:] - side[:, 1:-1, :-2]) * 0.5
    return (grad_x, grad_y, grad_z)


def edge_from(padded):
    grad_x, grad_y, grad_z = central_grads(padded)
    return 1.0 / (1.0 + 6000.0 * (grad_x * grad_x + grad_y * grad_y + grad_z * grad_z))


def weno(first, second, third, fourth, fifth):
    step_one = second - first
    step_two = third - second
    step_three = fourth - third
    step_four = fifth - fourth
    cand_one = 5.0 * step_two - 2.0 * step_one
    cand_two = step_two + 2.0 * step_three
    cand_three = 4.0 * step_three - step_four
    part_a = step_two - step_one
    part_b = 3.0 * step_two - step_one
    smooth_one = 13.0 / 12.0 * part_a * part_a + 0.25 * part_b * part_b
    part_a = step_three - step_two
    part_b = step_two + step_three
    smooth_two = 13.0 / 12.0 * part_a * part_a + 0.25 * part_b * part_b
    part_a = step_four - step_three
    part_b = step_four - 3.0 * step_three
    smooth_three = 13.0 / 12.0 * part_a * part_a + 0.25 * part_b * part_b
    denom_one = 1e-06 + smooth_one
    denom_two = 1e-06 + smooth_two
    denom_three = 1e-06 + smooth_three
    square_one = denom_one * denom_one
    square_two = denom_two * denom_two
    square_three = denom_three * denom_three
    weight_one = 0.1 * (square_two * square_three)
    weight_two = 0.6 * (square_one * square_three)
    weight_three = 0.3 * (square_one * square_two)
    return third + (weight_one * cand_one + weight_two * cand_two + weight_three * cand_three) / (
        6.0 * (weight_one + weight_two + weight_three)
    )


def upwind(values, slope):
    diffs = [values[k + 1] - values[k] for k in range(6)]
    ahead = slope < 0.0
    chosen = [jnp.where(ahead, diffs[k], diffs[5 - k]) for k in range(5)]
    return slope * weno(*chosen)


SUB = 8
HALO = 3


def stage_kernel(scale_level, scale_step, rows_block):
    def kernel(
        low_ref, main_ref, high_ref, edge_ref, sx_ref, sy_ref, sz_ref, ls_ref, out_ref, p_ref, sems
    ):
        rows = main_ref.shape[0]
        rows_y = out_ref.shape[1]
        rows_z = out_ref.shape[2]
        block = pl.program_id(0)

        @pl.when(block == 0)
        def _():
            inner = pl.ds(SUB, rows_y)
            copies = [
                pltpu.make_async_copy(low_ref, p_ref.at[pl.ds(0, HALO), inner, :], sems.at[0]),
                pltpu.make_async_copy(main_ref, p_ref.at[pl.ds(HALO, rows), inner, :], sems.at[1]),
                pltpu.make_async_copy(
                    high_ref, p_ref.at[pl.ds(HALO + rows, HALO), inner, :], sems.at[2]
                ),
            ]
            for copy in copies:
                copy.start()
            zeros = jnp.zeros((SUB, rows_z), jnp.float32)

            def clear(x, carry):
                p_ref[x, pl.ds(0, SUB), :] = zeros
                p_ref[x, pl.ds(SUB + rows_y, SUB), :] = zeros
                return carry

            lax.fori_loop(0, rows + 2 * HALO, clear, 0)
            for copy in copies:
                copy.wait()
        lane = lax.broadcasted_iota(jnp.int32, (SUB, rows_z), 1)

        def along_z(tile, step):
            moved = pltpu.roll(tile, (-step) % rows_z, 1)
            keep = lane < rows_z - step if step > 0 else lane >= -step
            return jnp.where(keep, moved, 0.0)

        def row(r, carry):
            centre_row = block * rows_block + r + HALO
            for chunk in range(rows_y // SUB):
                top = SUB + chunk * SUB

                def at(step_x, step_y):
                    return p_ref[centre_row + step_x, pl.ds(top + step_y, SUB), :]

                centre = at(0, 0)
                line_x = [at(k, 0) for k in range(-HALO, HALO + 1)]
                line_y = [at(0, k) for k in range(-HALO, HALO + 1)]
                line_z = [along_z(centre, k) for k in range(-HALO, HALO + 1)]
                here = pl.ds(chunk * SUB, SUB)
                flow_x = upwind(line_x, sx_ref[r, here, :])
                flow_y = upwind(line_y, sy_ref[r, here, :])
                flow_z = upwind(line_z, sz_ref[r, here, :])
                up_x = line_x[HALO + 1]
                down_x = line_x[HALO - 1]
                up_y = line_y[HALO + 1]
                down_y = line_y[HALO - 1]
                up_z = line_z[HALO + 1]
                down_z = line_z[HALO - 1]
                first_x = up_x - down_x
                first_y = up_y - down_y
                first_z = up_z - down_z
                second_xx = up_x - 2.0 * centre + down_x
                second_yy = up_y - 2.0 * centre + down_y
                second_zz = up_z - 2.0 * centre + down_z
                mixed_xy = at(1, 1) - at(1, -1) - at(-1, 1) + at(-1, -1)
                mixed_xz = along_z(first_x, 1) - along_z(first_x, -1)
                mixed_yz = along_z(first_y, 1) - along_z(first_y, -1)
                square_x = first_x * first_x
                square_y = first_y * first_y
                square_z = first_z * first_z
                numerator = (
                    second_xx * (square_y + square_z)
                    + second_yy * (square_x + square_z)
                    + second_zz * (square_x + square_y)
                )
                numerator = numerator - 0.5 * (
                    first_x * first_y * mixed_xy
                    + first_x * first_z * mixed_xz
                    + first_y * first_z * mixed_yz
                )
                curvature = numerator / (square_x + square_y + square_z + 4.0)
                rate = edge_ref[r, here, :] * curvature + (flow_x + flow_y + flow_z)
                moved = centre + 0.1 * rate
                if scale_level is None:
                    out_ref[r, here, :] = moved
                else:
                    out_ref[r, here, :] = scale_level * ls_ref[r, here, :] + scale_step * moved
            return carry

        lax.fori_loop(0, rows_block, row, 0)

    return kernel


def stage(low, field, high, edge, slope, level_set, scale_level, scale_step):
    rows, rows_y, rows_z = level_set.shape
    rows_block = SUB if rows % SUB == 0 else rows
    raw = pl.BlockSpec(memory_space=pl.ANY)
    part = pl.BlockSpec((rows_block, rows_y, rows_z), lambda i: (i, 0, 0))
    return pl.pallas_call(
        stage_kernel(scale_level, scale_step, rows_block),
        grid=(rows // rows_block,),
        in_specs=[raw, raw, raw, part, part, part, part, part],
        out_specs=part,
        out_shape=jax.ShapeDtypeStruct(level_set.shape, level_set.dtype),
        scratch_shapes=[
            pltpu.VMEM((rows + 2 * HALO, rows_y + 2 * SUB, rows_z), jnp.float32),
            pltpu.SemaphoreType.DMA((3,)),
        ],
        compiler_params=pltpu.CompilerParams(dimension_semantics=("arbitrary",)),
    )(low, field, high, edge, slope[0], slope[1], slope[2], level_set)


def shards(volume, level_set):
    rows, rows_y, rows_z = volume.shape
    exact = lax.Precision.HIGHEST
    halo = min(rows, RADIUS + 2)
    low = shifted(volume[rows - halo :], "gx", 1)
    high = shifted(volume[:halo], "gx", -1)
    extended = jnp.concatenate([low, volume, high], axis=0)
    wide = rows + 4
    blurred = jnp.dot(
        band(wide, extended.shape[0], halo - 2),
        extended.reshape(extended.shape[0], rows_y * rows_z),
        precision=exact,
    )
    blurred = jnp.dot(
        blurred.reshape(wide * rows_y, rows_z), band(rows_z, rows_z, 0).T, precision=exact
    ).reshape(wide, rows_y, rows_z)
    blurred = jnp.einsum("yv,xvz->xyz", band(rows_y, rows_y, 0), blurred, precision=exact)
    positions = lax.axis_index("gx") * rows - 2 + jnp.arange(wide, dtype=jnp.int32)
    inside = (positions >= 0) & (positions < rows * lax.axis_size("gx"))
    blurred = jnp.where(inside[:, None, None], blurred, 0.0)
    edge_wide = edge_from(blurred)
    edge_wide = jnp.where(inside[1:-1, None, None], edge_wide, 0.0)
    edge = edge_wide[1:-1]
    slope = central_grads(edge_wide)

    def step(field, scale_level, scale_step):
        low = shifted(field[rows - HALO :], "gx", 1)
        high = shifted(field[:HALO], "gx", -1)
        return stage(low, field, high, edge, slope, level_set, scale_level, scale_step)

    section_one = step(level_set, None, None)
    section_two = step(section_one, 0.75, 0.25)
    advanced = step(section_two, 1.0 / 3.0, 2.0 / 3.0)
    return (edge, advanced)


def solution(mesh):
    return jax.shard_map(
        shards,
        mesh=mesh,
        in_specs=(P(("grp", "gx"), None, None), P(("grp", "gx"), None, None)),
        out_specs=(P(("grp", "gx"), None, None), P(("grp", "gx"), None, None)),
        check_vma=False,
    )
```

```python
import math

import numpy as np

import jax
import jax.numpy as jnp
from jax import lax
from jax.experimental import pallas as pl
from jax.experimental.pallas import tpu as pltpu
from jax.sharding import PartitionSpec as P

RADIUS = 12


def shifted(block, axis, distance):
    devices = range(lax.axis_size(axis))
    route = [(i - distance, i) for i in devices if i - distance in devices]
    return lax.ppermute(block, axis, route)


def extended_2(block, sides, width):
    for axis, dim in sides:
        count = lax.axis_size(axis)
        forward = [(i, i + 1) for i in range(count - 1)]
        backward = [(target, source) for source, target in forward]
        low = lax.ppermute(
            lax.slice_in_dim(block, block.shape[dim] - width, None, axis=dim), axis, forward
        )
        high = lax.ppermute(lax.slice_in_dim(block, 0, width, axis=dim), axis, backward)
        block = jnp.concatenate([low, block, high], axis=dim)
    return block


def blur_taps():
    raw = [math.exp(-(offset * offset) / 18.0) for offset in range(-RADIUS, RADIUS + 1)]
    total = sum(raw)
    return [value / total for value in raw]


def band(rows, cols, shift):
    taps = blur_taps()
    table = np.zeros((rows, cols), np.float32)
    for i in range(rows):
        for k in range(-RADIUS, RADIUS + 1):
            j = i + shift + k
            if 0 <= j < cols:
                table[i, j] = taps[k + RADIUS]
    return jnp.asarray(table)


def pad_axis(array, axis, width):
    widths = [(0, 0), (0, 0), (0, 0)]
    widths[axis] = (width, width)
    return jnp.pad(array, widths)


def blur_padded(padded, axis, count):
    taps = blur_taps()
    result = taps[0] * lax.slice_in_dim(padded, 0, count, axis=axis)
    for offset in range(1, len(taps)):
        result = result + taps[offset] * lax.slice_in_dim(padded, offset, offset + count, axis=axis)
    return result


def central_grads(padded):
    inner = padded[1:-1]
    side = jnp.pad(inner, ((0, 0), (1, 1), (1, 1)))
    grad_x = (padded[2:] - padded[:-2]) * 0.5
    grad_y = (side[:, 2:, 1:-1] - side[:, :-2, 1:-1]) * 0.5
    grad_z = (side[:, 1:-1, 2:] - side[:, 1:-1, :-2]) * 0.5
    return (grad_x, grad_y, grad_z)


def edge_from(padded):
    grad_x, grad_y, grad_z = central_grads(padded)
    return 1.0 / (1.0 + 6000.0 * (grad_x * grad_x + grad_y * grad_y + grad_z * grad_z))


def weno(first, second, third, fourth, fifth):
    step_one = second - first
    step_two = third - second
    step_three = fourth - third
    step_four = fifth - fourth
    cand_one = 5.0 * step_two - 2.0 * step_one
    cand_two = step_two + 2.0 * step_three
    cand_three = 4.0 * step_three - step_four
    part_a = step_two - step_one
    part_b = 3.0 * step_two - step_one
    smooth_one = 13.0 / 12.0 * part_a * part_a + 0.25 * part_b * part_b
    part_a = step_three - step_two
    part_b = step_two + step_three
    smooth_two = 13.0 / 12.0 * part_a * part_a + 0.25 * part_b * part_b
    part_a = step_four - step_three
    part_b = step_four - 3.0 * step_three
    smooth_three = 13.0 / 12.0 * part_a * part_a + 0.25 * part_b * part_b
    denom_one = 1e-06 + smooth_one
    denom_two = 1e-06 + smooth_two
    denom_three = 1e-06 + smooth_three
    square_one = denom_one * denom_one
    square_two = denom_two * denom_two
    square_three = denom_three * denom_three
    weight_one = 0.1 * (square_two * square_three)
    weight_two = 0.6 * (square_one * square_three)
    weight_three = 0.3 * (square_one * square_two)
    return third + (weight_one * cand_one + weight_two * cand_two + weight_three * cand_three) / (
        6.0 * (weight_one + weight_two + weight_three)
    )


def upwind(values, slope):
    diffs = [values[k + 1] - values[k] for k in range(6)]
    ahead = slope < 0.0
    chosen = [jnp.where(ahead, diffs[k], diffs[5 - k]) for k in range(5)]
    return slope * weno(*chosen)


SUB = 8
HALO = 3


def stage_kernel(scale_level, scale_step, rows_block):
    def kernel(
        low_ref, main_ref, high_ref, edge_ref, sx_ref, sy_ref, sz_ref, ls_ref, out_ref, p_ref, sems
    ):
        rows = main_ref.shape[0]
        rows_y = out_ref.shape[1]
        rows_z = out_ref.shape[2]
        block = pl.program_id(0)

        @pl.when(block == 0)
        def _():
            inner = pl.ds(SUB, rows_y)
            copies = [
                pltpu.make_async_copy(low_ref, p_ref.at[pl.ds(0, HALO), inner, :], sems.at[0]),
                pltpu.make_async_copy(main_ref, p_ref.at[pl.ds(HALO, rows), inner, :], sems.at[1]),
                pltpu.make_async_copy(
                    high_ref, p_ref.at[pl.ds(HALO + rows, HALO), inner, :], sems.at[2]
                ),
            ]
            for copy in copies:
                copy.start()
            zeros = jnp.zeros((SUB, rows_z), jnp.float32)

            def clear(x, carry):
                p_ref[x, pl.ds(0, SUB), :] = zeros
                p_ref[x, pl.ds(SUB + rows_y, SUB), :] = zeros
                return carry

            lax.fori_loop(0, rows + 2 * HALO, clear, 0)
            for copy in copies:
                copy.wait()
        lane = lax.broadcasted_iota(jnp.int32, (SUB, rows_z), 1)

        def along_z(tile, step):
            moved = pltpu.roll(tile, (-step) % rows_z, 1)
            keep = lane < rows_z - step if step > 0 else lane >= -step
            return jnp.where(keep, moved, 0.0)

        def row(r, carry):
            centre_row = block * rows_block + r + HALO
            for chunk in range(rows_y // SUB):
                top = SUB + chunk * SUB

                def at(step_x, step_y):
                    return p_ref[centre_row + step_x, pl.ds(top + step_y, SUB), :]

                centre = at(0, 0)
                line_x = [at(k, 0) for k in range(-HALO, HALO + 1)]
                line_y = [at(0, k) for k in range(-HALO, HALO + 1)]
                line_z = [along_z(centre, k) for k in range(-HALO, HALO + 1)]
                here = pl.ds(chunk * SUB, SUB)
                flow_x = upwind(line_x, sx_ref[r, here, :])
                flow_y = upwind(line_y, sy_ref[r, here, :])
                flow_z = upwind(line_z, sz_ref[r, here, :])
                up_x = line_x[HALO + 1]
                down_x = line_x[HALO - 1]
                up_y = line_y[HALO + 1]
                down_y = line_y[HALO - 1]
                up_z = line_z[HALO + 1]
                down_z = line_z[HALO - 1]
                first_x = up_x - down_x
                first_y = up_y - down_y
                first_z = up_z - down_z
                second_xx = up_x - 2.0 * centre + down_x
                second_yy = up_y - 2.0 * centre + down_y
                second_zz = up_z - 2.0 * centre + down_z
                mixed_xy = at(1, 1) - at(1, -1) - at(-1, 1) + at(-1, -1)
                mixed_xz = along_z(first_x, 1) - along_z(first_x, -1)
                mixed_yz = along_z(first_y, 1) - along_z(first_y, -1)
                square_x = first_x * first_x
                square_y = first_y * first_y
                square_z = first_z * first_z
                numerator = (
                    second_xx * (square_y + square_z)
                    + second_yy * (square_x + square_z)
                    + second_zz * (square_x + square_y)
                )
                numerator = numerator - 0.5 * (
                    first_x * first_y * mixed_xy
                    + first_x * first_z * mixed_xz
                    + first_y * first_z * mixed_yz
                )
                curvature = numerator / (square_x + square_y + square_z + 4.0)
                rate = edge_ref[r, here, :] * curvature + (flow_x + flow_y + flow_z)
                moved = centre + 0.1 * rate
                if scale_level is None:
                    out_ref[r, here, :] = moved
                else:
                    out_ref[r, here, :] = scale_level * ls_ref[r, here, :] + scale_step * moved
            return carry

        lax.fori_loop(0, rows_block, row, 0)

    return kernel


def stage(low, field, high, edge, slope, level_set, scale_level, scale_step):
    rows, rows_y, rows_z = level_set.shape
    rows_block = SUB if rows % SUB == 0 else rows
    raw = pl.BlockSpec(memory_space=pl.ANY)
    part = pl.BlockSpec((rows_block, rows_y, rows_z), lambda i: (i, 0, 0))
    return pl.pallas_call(
        stage_kernel(scale_level, scale_step, rows_block),
        grid=(rows // rows_block,),
        in_specs=[raw, raw, raw, part, part, part, part, part],
        out_specs=part,
        out_shape=jax.ShapeDtypeStruct(level_set.shape, level_set.dtype),
        scratch_shapes=[
            pltpu.VMEM((rows + 2 * HALO, rows_y + 2 * SUB, rows_z), jnp.float32),
            pltpu.SemaphoreType.DMA((3,)),
        ],
        compiler_params=pltpu.CompilerParams(dimension_semantics=("arbitrary",)),
    )(low, field, high, edge, slope[0], slope[1], slope[2], level_set)


def shards(volume, level_set):
    rows, rows_y, rows_z = volume.shape
    exact = lax.Precision.HIGHEST
    halo = min(rows, RADIUS + 2)
    low_all = shifted(
        jnp.concatenate([volume[rows - halo :], level_set[rows - HALO :]], axis=0), "gx", 1
    )
    high_all = shifted(jnp.concatenate([volume[:halo], level_set[:HALO]], axis=0), "gx", -1)
    low = low_all[:halo]
    high = high_all[:halo]
    extended = jnp.concatenate([low, volume, high], axis=0)
    wide = rows + 4
    blurred = jnp.dot(
        band(wide, extended.shape[0], halo - 2),
        extended.reshape(extended.shape[0], rows_y * rows_z),
        precision=exact,
    )
    blurred = jnp.dot(
        blurred.reshape(wide * rows_y, rows_z), band(rows_z, rows_z, 0).T, precision=exact
    ).reshape(wide, rows_y, rows_z)
    blurred = jnp.einsum("yv,xvz->xyz", band(rows_y, rows_y, 0), blurred, precision=exact)
    positions = lax.axis_index("gx") * rows - 2 + jnp.arange(wide, dtype=jnp.int32)
    inside = (positions >= 0) & (positions < rows * lax.axis_size("gx"))
    blurred = jnp.where(inside[:, None, None], blurred, 0.0)
    edge_wide = edge_from(blurred)
    edge_wide = jnp.where(inside[1:-1, None, None], edge_wide, 0.0)
    edge = edge_wide[1:-1]
    slope = central_grads(edge_wide)

    def step(field, scale_level, scale_step, low=None, high=None):
        if low is None:
            low = shifted(field[rows - HALO :], "gx", 1)
            high = shifted(field[:HALO], "gx", -1)
        return stage(low, field, high, edge, slope, level_set, scale_level, scale_step)

    section_one = step(level_set, None, None, low_all[halo:], high_all[halo:])
    section_two = step(section_one, 0.75, 0.25)
    advanced = step(section_two, 1.0 / 3.0, 2.0 / 3.0)
    return (edge, advanced)


def solution(mesh):
    return jax.shard_map(
        shards,
        mesh=mesh,
        in_specs=(P(("grp", "gx"), None, None), P(("grp", "gx"), None, None)),
        out_specs=(P(("grp", "gx"), None, None), P(("grp", "gx"), None, None)),
        check_vma=False,
    )
```

```python
import math

import numpy as np

import jax
import jax.numpy as jnp
from jax import lax
from jax.experimental import pallas as pl
from jax.experimental.pallas import tpu as pltpu
from jax.sharding import PartitionSpec as P

RADIUS = 12


def shifted(block, axis, distance):
    devices = range(lax.axis_size(axis))
    route = [(i - distance, i) for i in devices if i - distance in devices]
    return lax.ppermute(block, axis, route)


def extended_2(block, sides, width):
    for axis, dim in sides:
        count = lax.axis_size(axis)
        forward = [(i, i + 1) for i in range(count - 1)]
        backward = [(target, source) for source, target in forward]
        low = lax.ppermute(
            lax.slice_in_dim(block, block.shape[dim] - width, None, axis=dim), axis, forward
        )
        high = lax.ppermute(lax.slice_in_dim(block, 0, width, axis=dim), axis, backward)
        block = jnp.concatenate([low, block, high], axis=dim)
    return block


def blur_taps():
    raw = [math.exp(-(offset * offset) / 18.0) for offset in range(-RADIUS, RADIUS + 1)]
    total = sum(raw)
    return [value / total for value in raw]


def band(rows, cols, shift):
    taps = blur_taps()
    table = np.zeros((rows, cols), np.float32)
    for i in range(rows):
        for k in range(-RADIUS, RADIUS + 1):
            j = i + shift + k
            if 0 <= j < cols:
                table[i, j] = taps[k + RADIUS]
    return jnp.asarray(table)


def pad_axis(array, axis, width):
    widths = [(0, 0), (0, 0), (0, 0)]
    widths[axis] = (width, width)
    return jnp.pad(array, widths)


def blur_padded(padded, axis, count):
    taps = blur_taps()
    result = taps[0] * lax.slice_in_dim(padded, 0, count, axis=axis)
    for offset in range(1, len(taps)):
        result = result + taps[offset] * lax.slice_in_dim(padded, offset, offset + count, axis=axis)
    return result


def central_grads(padded):
    inner = padded[1:-1]
    side = jnp.pad(inner, ((0, 0), (1, 1), (1, 1)))
    grad_x = (padded[2:] - padded[:-2]) * 0.5
    grad_y = (side[:, 2:, 1:-1] - side[:, :-2, 1:-1]) * 0.5
    grad_z = (side[:, 1:-1, 2:] - side[:, 1:-1, :-2]) * 0.5
    return (grad_x, grad_y, grad_z)


def edge_from(padded):
    grad_x, grad_y, grad_z = central_grads(padded)
    return 1.0 / (1.0 + 6000.0 * (grad_x * grad_x + grad_y * grad_y + grad_z * grad_z))


def weno(first, second, third, fourth, fifth):
    step_one = second - first
    step_two = third - second
    step_three = fourth - third
    step_four = fifth - fourth
    cand_one = 5.0 * step_two - 2.0 * step_one
    cand_two = step_two + 2.0 * step_three
    cand_three = 4.0 * step_three - step_four
    part_a = step_two - step_one
    part_b = 3.0 * step_two - step_one
    smooth_one = 13.0 / 12.0 * part_a * part_a + 0.25 * part_b * part_b
    part_a = step_three - step_two
    part_b = step_two + step_three
    smooth_two = 13.0 / 12.0 * part_a * part_a + 0.25 * part_b * part_b
    part_a = step_four - step_three
    part_b = step_four - 3.0 * step_three
    smooth_three = 13.0 / 12.0 * part_a * part_a + 0.25 * part_b * part_b
    denom_one = 1e-06 + smooth_one
    denom_two = 1e-06 + smooth_two
    denom_three = 1e-06 + smooth_three
    square_one = denom_one * denom_one
    square_two = denom_two * denom_two
    square_three = denom_three * denom_three
    weight_one = 0.1 * (square_two * square_three)
    weight_two = 0.6 * (square_one * square_three)
    weight_three = 0.3 * (square_one * square_two)
    return third + (weight_one * cand_one + weight_two * cand_two + weight_three * cand_three) / (
        6.0 * (weight_one + weight_two + weight_three)
    )


def upwind(values, slope):
    diffs = [values[k + 1] - values[k] for k in range(6)]
    ahead = slope < 0.0
    chosen = [jnp.where(ahead, diffs[k], diffs[5 - k]) for k in range(5)]
    return slope * weno(*chosen)


SUB = 8
HALO = 3


def stage_kernel(scale_level, scale_step, rows_block):
    def kernel(low_ref, main_ref, high_ref, edge_ref, sx_ref, sy_ref, sz_ref, ls_ref, *rest):
        out_ref = rest[0]
        p_ref, sems = rest[-2:]
        rows = main_ref.shape[0]
        rows_y = out_ref.shape[1]
        rows_z = out_ref.shape[2]
        block = pl.program_id(0)
        last = pl.num_programs(0) - 1
        inner = pl.ds(SUB, rows_y)

        @pl.when(block == 0)
        def _():
            copy = pltpu.make_async_copy(main_ref, p_ref.at[pl.ds(HALO, rows), inner, :], sems.at[0])
            copy.start()
            zeros = jnp.zeros((SUB, rows_z), jnp.float32)

            def clear(x, carry):
                p_ref[x, pl.ds(0, SUB), :] = zeros
                p_ref[x, pl.ds(SUB + rows_y, SUB), :] = zeros
                return carry

            lax.fori_loop(0, rows + 2 * HALO, clear, 0)
            p_ref[pl.ds(0, HALO), inner, :] = low_ref[...]
            p_ref[pl.ds(HALO + rows, HALO), inner, :] = high_ref[...]
            copy.wait()

        lane = lax.broadcasted_iota(jnp.int32, (SUB, rows_z), 1)

        def along_z(tile, step):
            moved = pltpu.roll(tile, (-step) % rows_z, 1)
            keep = lane < rows_z - step if step > 0 else lane >= -step
            return jnp.where(keep, moved, 0.0)

        def row(r, carry):
            centre_row = block * rows_block + r + HALO
            for chunk in range(rows_y // SUB):
                top = SUB + chunk * SUB

                def at(step_x, step_y):
                    return p_ref[centre_row + step_x, pl.ds(top + step_y, SUB), :]

                centre = at(0, 0)
                line_x = [at(k, 0) for k in range(-HALO, HALO + 1)]
                line_y = [at(0, k) for k in range(-HALO, HALO + 1)]
                line_z = [along_z(centre, k) for k in range(-HALO, HALO + 1)]
                here = pl.ds(chunk * SUB, SUB)
                flow_x = upwind(line_x, sx_ref[r, here, :])
                flow_y = upwind(line_y, sy_ref[r, here, :])
                flow_z = upwind(line_z, sz_ref[r, here, :])
                up_x = line_x[HALO + 1]
                down_x = line_x[HALO - 1]
                up_y = line_y[HALO + 1]
                down_y = line_y[HALO - 1]
                up_z = line_z[HALO + 1]
                down_z = line_z[HALO - 1]
                first_x = up_x - down_x
                first_y = up_y - down_y
                first_z = up_z - down_z
                second_xx = up_x - 2.0 * centre + down_x
                second_yy = up_y - 2.0 * centre + down_y
                second_zz = up_z - 2.0 * centre + down_z
                mixed_xy = at(1, 1) - at(1, -1) - at(-1, 1) + at(-1, -1)
                mixed_xz = along_z(first_x, 1) - along_z(first_x, -1)
                mixed_yz = along_z(first_y, 1) - along_z(first_y, -1)
                square_x = first_x * first_x
                square_y = first_y * first_y
                square_z = first_z * first_z
                numerator = (
                    second_xx * (square_y + square_z)
                    + second_yy * (square_x + square_z)
                    + second_zz * (square_x + square_y)
                )
                numerator = numerator - 0.5 * (
                    first_x * first_y * mixed_xy
                    + first_x * first_z * mixed_xz
                    + first_y * first_z * mixed_yz
                )
                curvature = numerator / (square_x + square_y + square_z + 4.0)
                rate = edge_ref[r, here, :] * curvature + (flow_x + flow_y + flow_z)
                moved = centre + 0.1 * rate
                if scale_level is None:
                    out_ref[r, here, :] = moved
                else:
                    out_ref[r, here, :] = scale_level * ls_ref[r, here, :] + scale_step * moved
            return carry

        lax.fori_loop(0, rows_block, row, 0)
        if len(rest) > 3:
            top_ref, bottom_ref = rest[1], rest[2]

            @pl.when(block == 0)
            def _():
                top_ref[...] = out_ref[pl.ds(0, HALO)]

            @pl.when(block == last)
            def _():
                bottom_ref[...] = out_ref[pl.ds(rows_block - HALO, HALO)]

    return kernel


def stage(low, field, high, edge, slope, level_set, scale_level, scale_step, sides):
    rows, rows_y, rows_z = level_set.shape
    rows_block = SUB if rows % SUB == 0 else rows
    raw = pl.BlockSpec(memory_space=pl.ANY)
    part = pl.BlockSpec((rows_block, rows_y, rows_z), lambda i: (i, 0, 0))
    side = pl.BlockSpec((HALO, rows_y, rows_z), lambda i: (0, 0, 0))
    result = jax.ShapeDtypeStruct(level_set.shape, level_set.dtype)
    edge_rows = jax.ShapeDtypeStruct((HALO, rows_y, rows_z), level_set.dtype)
    return pl.pallas_call(
        stage_kernel(scale_level, scale_step, rows_block),
        grid=(rows // rows_block,),
        in_specs=[side, raw, side, part, part, part, part, part],
        out_specs=[part, side, side] if sides else part,
        out_shape=[result, edge_rows, edge_rows] if sides else result,
        scratch_shapes=[
            pltpu.VMEM((rows + 2 * HALO, rows_y + 2 * SUB, rows_z), jnp.float32),
            pltpu.SemaphoreType.DMA((1,)),
        ],
        compiler_params=pltpu.CompilerParams(dimension_semantics=("arbitrary",)),
    )(low, field, high, edge, slope[0], slope[1], slope[2], level_set)


def shards(volume, level_set):
    rows, rows_y, rows_z = volume.shape
    exact = lax.Precision.HIGHEST
    halo = min(rows, RADIUS + 2)
    low = shifted(volume[rows - halo :], "gx", 1)
    high = shifted(volume[:halo], "gx", -1)
    extended = jnp.concatenate([low, volume, high], axis=0)
    wide = rows + 4
    blurred = jnp.dot(
        band(wide, extended.shape[0], halo - 2),
        extended.reshape(extended.shape[0], rows_y * rows_z),
        precision=exact,
    )
    blurred = jnp.dot(
        blurred.reshape(wide * rows_y, rows_z), band(rows_z, rows_z, 0).T, precision=exact
    ).reshape(wide, rows_y, rows_z)
    blurred = jnp.einsum("yv,xvz->xyz", band(rows_y, rows_y, 0), blurred, precision=exact)
    positions = lax.axis_index("gx") * rows - 2 + jnp.arange(wide, dtype=jnp.int32)
    inside = (positions >= 0) & (positions < rows * lax.axis_size("gx"))
    blurred = jnp.where(inside[:, None, None], blurred, 0.0)
    edge_wide = edge_from(blurred)
    edge_wide = jnp.where(inside[1:-1, None, None], edge_wide, 0.0)
    edge = edge_wide[1:-1]
    slope = central_grads(edge_wide)

    def step(field, top, bottom, scale_level, scale_step, sides=True):
        low = shifted(bottom, "gx", 1)
        high = shifted(top, "gx", -1)
        return stage(low, field, high, edge, slope, level_set, scale_level, scale_step, sides)

    section_one, top, bottom = step(level_set, level_set[:HALO], level_set[rows - HALO :], None, None)
    section_two, top, bottom = step(section_one, top, bottom, 0.75, 0.25)
    advanced = step(section_two, top, bottom, 1.0 / 3.0, 2.0 / 3.0, sides=False)
    return (edge, advanced)


def solution(mesh):
    return jax.shard_map(
        shards,
        mesh=mesh,
        in_specs=(P(("grp", "gx"), None, None), P(("grp", "gx"), None, None)),
        out_specs=(P(("grp", "gx"), None, None), P(("grp", "gx"), None, None)),
        check_vma=False,
    )
```

```python
import math

import numpy as np

import jax
import jax.numpy as jnp
from jax import lax
from jax.experimental import pallas as pl
from jax.experimental.pallas import tpu as pltpu
from jax.sharding import PartitionSpec as P

RADIUS = 12


def shifted(block, axis, distance):
    devices = range(lax.axis_size(axis))
    route = [(i - distance, i) for i in devices if i - distance in devices]
    return lax.ppermute(block, axis, route)


def extended_2(block, sides, width):
    for axis, dim in sides:
        count = lax.axis_size(axis)
        forward = [(i, i + 1) for i in range(count - 1)]
        backward = [(target, source) for source, target in forward]
        low = lax.ppermute(
            lax.slice_in_dim(block, block.shape[dim] - width, None, axis=dim), axis, forward
        )
        high = lax.ppermute(lax.slice_in_dim(block, 0, width, axis=dim), axis, backward)
        block = jnp.concatenate([low, block, high], axis=dim)
    return block


def blur_taps():
    raw = [math.exp(-(offset * offset) / 18.0) for offset in range(-RADIUS, RADIUS + 1)]
    total = sum(raw)
    return [value / total for value in raw]


def band(rows, cols, shift):
    taps = blur_taps()
    table = np.zeros((rows, cols), np.float32)
    for i in range(rows):
        for k in range(-RADIUS, RADIUS + 1):
            j = i + shift + k
            if 0 <= j < cols:
                table[i, j] = taps[k + RADIUS]
    return jnp.asarray(table)


def pad_axis(array, axis, width):
    widths = [(0, 0), (0, 0), (0, 0)]
    widths[axis] = (width, width)
    return jnp.pad(array, widths)


def blur_padded(padded, axis, count):
    taps = blur_taps()
    result = taps[0] * lax.slice_in_dim(padded, 0, count, axis=axis)
    for offset in range(1, len(taps)):
        result = result + taps[offset] * lax.slice_in_dim(padded, offset, offset + count, axis=axis)
    return result


def central_grads(padded):
    inner = padded[1:-1]
    side = jnp.pad(inner, ((0, 0), (1, 1), (1, 1)))
    grad_x = (padded[2:] - padded[:-2]) * 0.5
    grad_y = (side[:, 2:, 1:-1] - side[:, :-2, 1:-1]) * 0.5
    grad_z = (side[:, 1:-1, 2:] - side[:, 1:-1, :-2]) * 0.5
    return (grad_x, grad_y, grad_z)


def edge_from(padded):
    grad_x, grad_y, grad_z = central_grads(padded)
    return 1.0 / (1.0 + 6000.0 * (grad_x * grad_x + grad_y * grad_y + grad_z * grad_z))


def weno(first, second, third, fourth, fifth):
    step_one = second - first
    step_two = third - second
    step_three = fourth - third
    step_four = fifth - fourth
    cand_one = 5.0 * step_two - 2.0 * step_one
    cand_two = step_two + 2.0 * step_three
    cand_three = 4.0 * step_three - step_four
    part_a = step_two - step_one
    part_b = 3.0 * step_two - step_one
    smooth_one = 13.0 / 12.0 * part_a * part_a + 0.25 * part_b * part_b
    part_a = step_three - step_two
    part_b = step_two + step_three
    smooth_two = 13.0 / 12.0 * part_a * part_a + 0.25 * part_b * part_b
    part_a = step_four - step_three
    part_b = step_four - 3.0 * step_three
    smooth_three = 13.0 / 12.0 * part_a * part_a + 0.25 * part_b * part_b
    denom_one = 1e-06 + smooth_one
    denom_two = 1e-06 + smooth_two
    denom_three = 1e-06 + smooth_three
    square_one = denom_one * denom_one
    square_two = denom_two * denom_two
    square_three = denom_three * denom_three
    weight_one = 0.1 * (square_two * square_three)
    weight_two = 0.6 * (square_one * square_three)
    weight_three = 0.3 * (square_one * square_two)
    return third + (weight_one * cand_one + weight_two * cand_two + weight_three * cand_three) / (
        6.0 * (weight_one + weight_two + weight_three)
    )


def upwind(values, slope):
    diffs = [values[k + 1] - values[k] for k in range(6)]
    ahead = slope < 0.0
    chosen = [jnp.where(ahead, diffs[k], diffs[5 - k]) for k in range(5)]
    return slope * weno(*chosen)


SUB = 8
HALO = 3


def stage_kernel(scale_level, scale_step, rows_block, first):
    def kernel(*refs):
        if first:
            low_ref, main_ref, high_ref, wide_ref, ls_ref = refs[:5]
            out_ref, top_ref, bottom_ref, edge_ref, sx_ref, sy_ref, sz_ref = refs[5:12]
            p_ref, e_ref, sems = refs[12:]
            rest = (out_ref, top_ref, bottom_ref, p_ref, sems)
        else:
            low_ref, main_ref, high_ref, edge_ref, sx_ref, sy_ref, sz_ref, ls_ref = refs[:8]
            rest = refs[8:]
            out_ref = rest[0]
            p_ref, sems = rest[-2:]
        rows = main_ref.shape[0]
        rows_y = out_ref.shape[1]
        rows_z = out_ref.shape[2]
        block = pl.program_id(0)
        last = pl.num_programs(0) - 1
        inner = pl.ds(SUB, rows_y)

        @pl.when(block == 0)
        def _():
            copy = pltpu.make_async_copy(main_ref, p_ref.at[pl.ds(HALO, rows), inner, :], sems.at[0])
            copy.start()
            zeros = jnp.zeros((SUB, rows_z), jnp.float32)

            def clear(x, carry):
                p_ref[x, pl.ds(0, SUB), :] = zeros
                p_ref[x, pl.ds(SUB + rows_y, SUB), :] = zeros
                return carry

            lax.fori_loop(0, rows + 2 * HALO, clear, 0)
            p_ref[pl.ds(0, HALO), inner, :] = low_ref[...]
            p_ref[pl.ds(HALO + rows, HALO), inner, :] = high_ref[...]
            if first:
                spread = pltpu.make_async_copy(
                    wide_ref, e_ref.at[pl.ds(0, rows + 2), inner, :], sems.at[1]
                )
                spread.start()

                def clear_edge(x, carry):
                    e_ref[x, pl.ds(0, SUB), :] = zeros
                    e_ref[x, pl.ds(SUB + rows_y, SUB), :] = zeros
                    return carry

                lax.fori_loop(0, rows + 2, clear_edge, 0)
                spread.wait()
            copy.wait()

        lane = lax.broadcasted_iota(jnp.int32, (SUB, rows_z), 1)

        def along_z(tile, step):
            moved = pltpu.roll(tile, (-step) % rows_z, 1)
            keep = lane < rows_z - step if step > 0 else lane >= -step
            return jnp.where(keep, moved, 0.0)

        def row(r, carry):
            centre_row = block * rows_block + r + HALO
            for chunk in range(rows_y // SUB):
                top = SUB + chunk * SUB

                def at(step_x, step_y):
                    return p_ref[centre_row + step_x, pl.ds(top + step_y, SUB), :]

                centre = at(0, 0)
                line_x = [at(k, 0) for k in range(-HALO, HALO + 1)]
                line_y = [at(0, k) for k in range(-HALO, HALO + 1)]
                line_z = [along_z(centre, k) for k in range(-HALO, HALO + 1)]
                here = pl.ds(chunk * SUB, SUB)
                if first:
                    edge_row = block * rows_block + r + 1

                    def near(step_x, step_y):
                        return e_ref[edge_row + step_x, pl.ds(top + step_y, SUB), :]

                    edge_here = near(0, 0)
                    slope_x = (near(1, 0) - near(-1, 0)) * 0.5
                    slope_y = (near(0, 1) - near(0, -1)) * 0.5
                    slope_z = (along_z(edge_here, 1) - along_z(edge_here, -1)) * 0.5
                    edge_ref[r, here, :] = edge_here
                    sx_ref[r, here, :] = slope_x
                    sy_ref[r, here, :] = slope_y
                    sz_ref[r, here, :] = slope_z
                else:
                    edge_here = edge_ref[r, here, :]
                    slope_x = sx_ref[r, here, :]
                    slope_y = sy_ref[r, here, :]
                    slope_z = sz_ref[r, here, :]
                flow_x = upwind(line_x, slope_x)
                flow_y = upwind(line_y, slope_y)
                flow_z = upwind(line_z, slope_z)
                up_x = line_x[HALO + 1]
                down_x = line_x[HALO - 1]
                up_y = line_y[HALO + 1]
                down_y = line_y[HALO - 1]
                up_z = line_z[HALO + 1]
                down_z = line_z[HALO - 1]
                first_x = up_x - down_x
                first_y = up_y - down_y
                first_z = up_z - down_z
                second_xx = up_x - 2.0 * centre + down_x
                second_yy = up_y - 2.0 * centre + down_y
                second_zz = up_z - 2.0 * centre + down_z
                mixed_xy = at(1, 1) - at(1, -1) - at(-1, 1) + at(-1, -1)
                mixed_xz = along_z(first_x, 1) - along_z(first_x, -1)
                mixed_yz = along_z(first_y, 1) - along_z(first_y, -1)
                square_x = first_x * first_x
                square_y = first_y * first_y
                square_z = first_z * first_z
                numerator = (
                    second_xx * (square_y + square_z)
                    + second_yy * (square_x + square_z)
                    + second_zz * (square_x + square_y)
                )
                numerator = numerator - 0.5 * (
                    first_x * first_y * mixed_xy
                    + first_x * first_z * mixed_xz
                    + first_y * first_z * mixed_yz
                )
                curvature = numerator / (square_x + square_y + square_z + 4.0)
                rate = edge_here * curvature + (flow_x + flow_y + flow_z)
                moved = centre + 0.1 * rate
                if scale_level is None:
                    out_ref[r, here, :] = moved
                else:
                    out_ref[r, here, :] = scale_level * ls_ref[r, here, :] + scale_step * moved
            return carry

        lax.fori_loop(0, rows_block, row, 0)
        if len(rest) > 3:
            top_ref, bottom_ref = rest[1], rest[2]

            @pl.when(block == 0)
            def _():
                top_ref[...] = out_ref[pl.ds(0, HALO)]

            @pl.when(block == last)
            def _():
                bottom_ref[...] = out_ref[pl.ds(rows_block - HALO, HALO)]

    return kernel


def stage(low, field, high, edge, slope, level_set, scale_level, scale_step, sides):
    rows, rows_y, rows_z = level_set.shape
    rows_block = SUB if rows % SUB == 0 else rows
    raw = pl.BlockSpec(memory_space=pl.ANY)
    part = pl.BlockSpec((rows_block, rows_y, rows_z), lambda i: (i, 0, 0))
    side = pl.BlockSpec((HALO, rows_y, rows_z), lambda i: (0, 0, 0))
    result = jax.ShapeDtypeStruct(level_set.shape, level_set.dtype)
    edge_rows = jax.ShapeDtypeStruct((HALO, rows_y, rows_z), level_set.dtype)
    first = slope is None
    scratch = [pltpu.VMEM((rows + 2 * HALO, rows_y + 2 * SUB, rows_z), jnp.float32)]
    if first:
        scratch.append(pltpu.VMEM((rows + 2, rows_y + 2 * SUB, rows_z), jnp.float32))
        in_specs = [side, raw, side, raw, part]
        operands = (low, field, high, edge, level_set)
        out_specs = [part, side, side, part, part, part, part]
        out_shape = [result, edge_rows, edge_rows, result, result, result, result]
    else:
        in_specs = [side, raw, side, part, part, part, part, part]
        operands = (low, field, high, edge, slope[0], slope[1], slope[2], level_set)
        out_specs = [part, side, side] if sides else part
        out_shape = [result, edge_rows, edge_rows] if sides else result
    return pl.pallas_call(
        stage_kernel(scale_level, scale_step, rows_block, first),
        grid=(rows // rows_block,),
        in_specs=in_specs,
        out_specs=out_specs,
        out_shape=out_shape,
        scratch_shapes=scratch + [pltpu.SemaphoreType.DMA((2,))],
        compiler_params=pltpu.CompilerParams(dimension_semantics=("arbitrary",)),
    )(*operands)


def shards(volume, level_set):
    rows, rows_y, rows_z = volume.shape
    exact = lax.Precision.HIGHEST
    halo = min(rows, RADIUS + 2)
    low = shifted(volume[rows - halo :], "gx", 1)
    high = shifted(volume[:halo], "gx", -1)
    extended = jnp.concatenate([low, volume, high], axis=0)
    wide = rows + 4
    blurred = jnp.dot(
        band(wide, extended.shape[0], halo - 2),
        extended.reshape(extended.shape[0], rows_y * rows_z),
        precision=exact,
    )
    blurred = jnp.dot(
        blurred.reshape(wide * rows_y, rows_z), band(rows_z, rows_z, 0).T, precision=exact
    ).reshape(wide, rows_y, rows_z)
    blurred = jnp.einsum("yv,xvz->xyz", band(rows_y, rows_y, 0), blurred, precision=exact)
    positions = lax.axis_index("gx") * rows - 2 + jnp.arange(wide, dtype=jnp.int32)
    inside = (positions >= 0) & (positions < rows * lax.axis_size("gx"))
    blurred = jnp.where(inside[:, None, None], blurred, 0.0)
    edge_wide = edge_from(blurred)
    edge_wide = jnp.where(inside[1:-1, None, None], edge_wide, 0.0)

    def step(field, top, bottom, scale_level, scale_step, sides=True):
        low = shifted(bottom, "gx", 1)
        high = shifted(top, "gx", -1)
        return stage(low, field, high, edge, slope, level_set, scale_level, scale_step, sides)

    low = shifted(level_set[rows - HALO :], "gx", 1)
    high = shifted(level_set[:HALO], "gx", -1)
    section_one, top, bottom, edge, *slope = stage(
        low, level_set, high, edge_wide, None, level_set, None, None, True
    )
    section_two, top, bottom = step(section_one, top, bottom, 0.75, 0.25)
    advanced = step(section_two, top, bottom, 1.0 / 3.0, 2.0 / 3.0, sides=False)
    return (edge, advanced)


def solution(mesh):
    return jax.shard_map(
        shards,
        mesh=mesh,
        in_specs=(P(("grp", "gx"), None, None), P(("grp", "gx"), None, None)),
        out_specs=(P(("grp", "gx"), None, None), P(("grp", "gx"), None, None)),
        check_vma=False,
    )
```

```python
import math

import numpy as np

import jax
import jax.numpy as jnp
from jax import lax
from jax.experimental import pallas as pl
from jax.experimental.pallas import tpu as pltpu
from jax.sharding import PartitionSpec as P

RADIUS = 12


def shifted(block, axis, distance):
    devices = range(lax.axis_size(axis))
    route = [(i - distance, i) for i in devices if i - distance in devices]
    return lax.ppermute(block, axis, route)


def extended_2(block, sides, width):
    for axis, dim in sides:
        count = lax.axis_size(axis)
        forward = [(i, i + 1) for i in range(count - 1)]
        backward = [(target, source) for source, target in forward]
        low = lax.ppermute(
            lax.slice_in_dim(block, block.shape[dim] - width, None, axis=dim), axis, forward
        )
        high = lax.ppermute(lax.slice_in_dim(block, 0, width, axis=dim), axis, backward)
        block = jnp.concatenate([low, block, high], axis=dim)
    return block


def blur_taps():
    raw = [math.exp(-(offset * offset) / 18.0) for offset in range(-RADIUS, RADIUS + 1)]
    total = sum(raw)
    return [value / total for value in raw]


def band(rows, cols, shift):
    taps = blur_taps()
    table = np.zeros((rows, cols), np.float32)
    for i in range(rows):
        for k in range(-RADIUS, RADIUS + 1):
            j = i + shift + k
            if 0 <= j < cols:
                table[i, j] = taps[k + RADIUS]
    return jnp.asarray(table)


def pad_axis(array, axis, width):
    widths = [(0, 0), (0, 0), (0, 0)]
    widths[axis] = (width, width)
    return jnp.pad(array, widths)


def blur_padded(padded, axis, count):
    taps = blur_taps()
    result = taps[0] * lax.slice_in_dim(padded, 0, count, axis=axis)
    for offset in range(1, len(taps)):
        result = result + taps[offset] * lax.slice_in_dim(padded, offset, offset + count, axis=axis)
    return result


def central_grads(padded):
    inner = padded[1:-1]
    side = jnp.pad(inner, ((0, 0), (1, 1), (1, 1)))
    grad_x = (padded[2:] - padded[:-2]) * 0.5
    grad_y = (side[:, 2:, 1:-1] - side[:, :-2, 1:-1]) * 0.5
    grad_z = (side[:, 1:-1, 2:] - side[:, 1:-1, :-2]) * 0.5
    return (grad_x, grad_y, grad_z)


def edge_from(padded):
    grad_x, grad_y, grad_z = central_grads(padded)
    return 1.0 / (1.0 + 6000.0 * (grad_x * grad_x + grad_y * grad_y + grad_z * grad_z))


def weno(first, second, third, fourth, fifth):
    step_one = second - first
    step_two = third - second
    step_three = fourth - third
    step_four = fifth - fourth
    cand_one = 5.0 * step_two - 2.0 * step_one
    cand_two = step_two + 2.0 * step_three
    cand_three = 4.0 * step_three - step_four
    part_a = step_two - step_one
    part_b = 3.0 * step_two - step_one
    smooth_one = 13.0 / 12.0 * part_a * part_a + 0.25 * part_b * part_b
    part_a = step_three - step_two
    part_b = step_two + step_three
    smooth_two = 13.0 / 12.0 * part_a * part_a + 0.25 * part_b * part_b
    part_a = step_four - step_three
    part_b = step_four - 3.0 * step_three
    smooth_three = 13.0 / 12.0 * part_a * part_a + 0.25 * part_b * part_b
    denom_one = 1e-06 + smooth_one
    denom_two = 1e-06 + smooth_two
    denom_three = 1e-06 + smooth_three
    square_one = denom_one * denom_one
    square_two = denom_two * denom_two
    square_three = denom_three * denom_three
    weight_one = square_two * square_three
    weight_two = 6.0 * (square_one * square_three)
    weight_three = 3.0 * (square_one * square_two)
    return third + (weight_one * cand_one + weight_two * cand_two + weight_three * cand_three) / (
        6.0 * (weight_one + weight_two + weight_three)
    )


def upwind(values, slope):
    diffs = [values[k + 1] - values[k] for k in range(6)]
    ahead = slope < 0.0
    chosen = [jnp.where(ahead, diffs[k], diffs[5 - k]) for k in range(5)]
    return slope * weno(*chosen)


SUB = 8
HALO = 3


def stage_kernel(scale_level, scale_step, rows_block, first):
    def kernel(*refs):
        if first:
            low_ref, main_ref, high_ref, wide_ref, ls_ref = refs[:5]
            out_ref, top_ref, bottom_ref, edge_ref, sx_ref, sy_ref, sz_ref = refs[5:12]
            p_ref, e_ref, sems = refs[12:]
            rest = (out_ref, top_ref, bottom_ref, p_ref, sems)
        else:
            low_ref, main_ref, high_ref, edge_ref, sx_ref, sy_ref, sz_ref, ls_ref = refs[:8]
            rest = refs[8:]
            out_ref = rest[0]
            p_ref, sems = rest[-2:]
        rows = main_ref.shape[0]
        rows_y = out_ref.shape[1]
        rows_z = out_ref.shape[2]
        block = pl.program_id(0)
        last = pl.num_programs(0) - 1
        inner = pl.ds(SUB, rows_y)

        @pl.when(block == 0)
        def _():
            copy = pltpu.make_async_copy(main_ref, p_ref.at[pl.ds(HALO, rows), inner, :], sems.at[0])
            copy.start()
            zeros = jnp.zeros((SUB, rows_z), jnp.float32)

            def clear(x, carry):
                p_ref[x, pl.ds(0, SUB), :] = zeros
                p_ref[x, pl.ds(SUB + rows_y, SUB), :] = zeros
                return carry

            lax.fori_loop(0, rows + 2 * HALO, clear, 0)
            p_ref[pl.ds(0, HALO), inner, :] = low_ref[...]
            p_ref[pl.ds(HALO + rows, HALO), inner, :] = high_ref[...]
            if first:
                spread = pltpu.make_async_copy(
                    wide_ref, e_ref.at[pl.ds(0, rows + 2), inner, :], sems.at[1]
                )
                spread.start()

                def clear_edge(x, carry):
                    e_ref[x, pl.ds(0, SUB), :] = zeros
                    e_ref[x, pl.ds(SUB + rows_y, SUB), :] = zeros
                    return carry

                lax.fori_loop(0, rows + 2, clear_edge, 0)
                spread.wait()
            copy.wait()

        lane = lax.broadcasted_iota(jnp.int32, (SUB, rows_z), 1)

        def along_z(tile, step):
            moved = pltpu.roll(tile, (-step) % rows_z, 1)
            keep = lane < rows_z - step if step > 0 else lane >= -step
            return jnp.where(keep, moved, 0.0)

        def row(r, carry):
            centre_row = block * rows_block + r + HALO
            for chunk in range(rows_y // SUB):
                top = SUB + chunk * SUB

                def at(step_x, step_y):
                    return p_ref[centre_row + step_x, pl.ds(top + step_y, SUB), :]

                centre = at(0, 0)
                line_x = [at(k, 0) for k in range(-HALO, HALO + 1)]
                line_y = [at(0, k) for k in range(-HALO, HALO + 1)]
                line_z = [along_z(centre, k) for k in range(-HALO, HALO + 1)]
                here = pl.ds(chunk * SUB, SUB)
                if first:
                    edge_row = block * rows_block + r + 1

                    def near(step_x, step_y):
                        return e_ref[edge_row + step_x, pl.ds(top + step_y, SUB), :]

                    edge_here = near(0, 0)
                    slope_x = (near(1, 0) - near(-1, 0)) * 0.5
                    slope_y = (near(0, 1) - near(0, -1)) * 0.5
                    slope_z = (along_z(edge_here, 1) - along_z(edge_here, -1)) * 0.5
                    edge_ref[r, here, :] = edge_here
                    sx_ref[r, here, :] = slope_x
                    sy_ref[r, here, :] = slope_y
                    sz_ref[r, here, :] = slope_z
                else:
                    edge_here = edge_ref[r, here, :]
                    slope_x = sx_ref[r, here, :]
                    slope_y = sy_ref[r, here, :]
                    slope_z = sz_ref[r, here, :]
                flow_x = upwind(line_x, slope_x)
                flow_y = upwind(line_y, slope_y)
                flow_z = upwind(line_z, slope_z)
                up_x = line_x[HALO + 1]
                down_x = line_x[HALO - 1]
                up_y = line_y[HALO + 1]
                down_y = line_y[HALO - 1]
                up_z = line_z[HALO + 1]
                down_z = line_z[HALO - 1]
                first_x = up_x - down_x
                first_y = up_y - down_y
                first_z = up_z - down_z
                second_xx = up_x - 2.0 * centre + down_x
                second_yy = up_y - 2.0 * centre + down_y
                second_zz = up_z - 2.0 * centre + down_z
                mixed_xy = at(1, 1) - at(1, -1) - at(-1, 1) + at(-1, -1)
                mixed_xz = along_z(first_x, 1) - along_z(first_x, -1)
                mixed_yz = along_z(first_y, 1) - along_z(first_y, -1)
                square_x = first_x * first_x
                square_y = first_y * first_y
                square_z = first_z * first_z
                numerator = (
                    second_xx * (square_y + square_z)
                    + second_yy * (square_x + square_z)
                    + second_zz * (square_x + square_y)
                )
                numerator = numerator - 0.5 * (
                    first_x * first_y * mixed_xy
                    + first_x * first_z * mixed_xz
                    + first_y * first_z * mixed_yz
                )
                curvature = numerator / (square_x + square_y + square_z + 4.0)
                rate = edge_here * curvature + (flow_x + flow_y + flow_z)
                moved = centre + 0.1 * rate
                if scale_level is None:
                    out_ref[r, here, :] = moved
                else:
                    out_ref[r, here, :] = scale_level * ls_ref[r, here, :] + scale_step * moved
            return carry

        lax.fori_loop(0, rows_block, row, 0)
        if len(rest) > 3:
            top_ref, bottom_ref = rest[1], rest[2]

            @pl.when(block == 0)
            def _():
                top_ref[...] = out_ref[pl.ds(0, HALO)]

            @pl.when(block == last)
            def _():
                bottom_ref[...] = out_ref[pl.ds(rows_block - HALO, HALO)]

    return kernel


def stage(low, field, high, edge, slope, level_set, scale_level, scale_step, sides):
    rows, rows_y, rows_z = level_set.shape
    rows_block = SUB if rows % SUB == 0 else rows
    raw = pl.BlockSpec(memory_space=pl.ANY)
    part = pl.BlockSpec((rows_block, rows_y, rows_z), lambda i: (i, 0, 0))
    side = pl.BlockSpec((HALO, rows_y, rows_z), lambda i: (0, 0, 0))
    result = jax.ShapeDtypeStruct(level_set.shape, level_set.dtype)
    edge_rows = jax.ShapeDtypeStruct((HALO, rows_y, rows_z), level_set.dtype)
    first = slope is None
    scratch = [pltpu.VMEM((rows + 2 * HALO, rows_y + 2 * SUB, rows_z), jnp.float32)]
    if first:
        scratch.append(pltpu.VMEM((rows + 2, rows_y + 2 * SUB, rows_z), jnp.float32))
        in_specs = [side, raw, side, raw, part]
        operands = (low, field, high, edge, level_set)
        out_specs = [part, side, side, part, part, part, part]
        out_shape = [result, edge_rows, edge_rows, result, result, result, result]
    else:
        in_specs = [side, raw, side, part, part, part, part, part]
        operands = (low, field, high, edge, slope[0], slope[1], slope[2], level_set)
        out_specs = [part, side, side] if sides else part
        out_shape = [result, edge_rows, edge_rows] if sides else result
    return pl.pallas_call(
        stage_kernel(scale_level, scale_step, rows_block, first),
        grid=(rows // rows_block,),
        in_specs=in_specs,
        out_specs=out_specs,
        out_shape=out_shape,
        scratch_shapes=scratch + [pltpu.SemaphoreType.DMA((2,))],
        compiler_params=pltpu.CompilerParams(dimension_semantics=("arbitrary",)),
    )(*operands)


def shards(volume, level_set):
    rows, rows_y, rows_z = volume.shape
    exact = lax.Precision.HIGHEST
    halo = min(rows, RADIUS + 2)
    low = shifted(volume[rows - halo :], "gx", 1)
    high = shifted(volume[:halo], "gx", -1)
    extended = jnp.concatenate([low, volume, high], axis=0)
    wide = rows + 4
    blurred = jnp.dot(
        band(wide, extended.shape[0], halo - 2),
        extended.reshape(extended.shape[0], rows_y * rows_z),
        precision=exact,
    )
    blurred = jnp.dot(
        blurred.reshape(wide * rows_y, rows_z), band(rows_z, rows_z, 0).T, precision=exact
    ).reshape(wide, rows_y, rows_z)
    blurred = jnp.einsum("yv,xvz->xyz", band(rows_y, rows_y, 0), blurred, precision=exact)
    positions = lax.axis_index("gx") * rows - 2 + jnp.arange(wide, dtype=jnp.int32)
    inside = (positions >= 0) & (positions < rows * lax.axis_size("gx"))
    blurred = jnp.where(inside[:, None, None], blurred, 0.0)
    edge_wide = edge_from(blurred)
    edge_wide = jnp.where(inside[1:-1, None, None], edge_wide, 0.0)

    def step(field, top, bottom, scale_level, scale_step, sides=True):
        low = shifted(bottom, "gx", 1)
        high = shifted(top, "gx", -1)
        return stage(low, field, high, edge, slope, level_set, scale_level, scale_step, sides)

    low = shifted(level_set[rows - HALO :], "gx", 1)
    high = shifted(level_set[:HALO], "gx", -1)
    section_one, top, bottom, edge, *slope = stage(
        low, level_set, high, edge_wide, None, level_set, None, None, True
    )
    section_two, top, bottom = step(section_one, top, bottom, 0.75, 0.25)
    advanced = step(section_two, top, bottom, 1.0 / 3.0, 2.0 / 3.0, sides=False)
    return (edge, advanced)


def solution(mesh):
    return jax.shard_map(
        shards,
        mesh=mesh,
        in_specs=(P(("grp", "gx"), None, None), P(("grp", "gx"), None, None)),
        out_specs=(P(("grp", "gx"), None, None), P(("grp", "gx"), None, None)),
        check_vma=False,
    )
```

```python
import math

import numpy as np

import jax
import jax.numpy as jnp
from jax import lax
from jax.experimental import pallas as pl
from jax.experimental.pallas import tpu as pltpu
from jax.sharding import PartitionSpec as P

RADIUS = 12


def shifted(block, axis, distance):
    devices = range(lax.axis_size(axis))
    route = [(i - distance, i) for i in devices if i - distance in devices]
    return lax.ppermute(block, axis, route)


def extended_2(block, sides, width):
    for axis, dim in sides:
        count = lax.axis_size(axis)
        forward = [(i, i + 1) for i in range(count - 1)]
        backward = [(target, source) for source, target in forward]
        low = lax.ppermute(
            lax.slice_in_dim(block, block.shape[dim] - width, None, axis=dim), axis, forward
        )
        high = lax.ppermute(lax.slice_in_dim(block, 0, width, axis=dim), axis, backward)
        block = jnp.concatenate([low, block, high], axis=dim)
    return block


def blur_taps():
    raw = [math.exp(-(offset * offset) / 18.0) for offset in range(-RADIUS, RADIUS + 1)]
    total = sum(raw)
    return [value / total for value in raw]


def band(rows, cols, shift):
    taps = blur_taps()
    table = np.zeros((rows, cols), np.float32)
    for i in range(rows):
        for k in range(-RADIUS, RADIUS + 1):
            j = i + shift + k
            if 0 <= j < cols:
                table[i, j] = taps[k + RADIUS]
    return jnp.asarray(table)


def pad_axis(array, axis, width):
    widths = [(0, 0), (0, 0), (0, 0)]
    widths[axis] = (width, width)
    return jnp.pad(array, widths)


def blur_padded(padded, axis, count):
    taps = blur_taps()
    result = taps[0] * lax.slice_in_dim(padded, 0, count, axis=axis)
    for offset in range(1, len(taps)):
        result = result + taps[offset] * lax.slice_in_dim(padded, offset, offset + count, axis=axis)
    return result


def central_grads(padded):
    inner = padded[1:-1]
    side = jnp.pad(inner, ((0, 0), (1, 1), (1, 1)))
    grad_x = (padded[2:] - padded[:-2]) * 0.5
    grad_y = (side[:, 2:, 1:-1] - side[:, :-2, 1:-1]) * 0.5
    grad_z = (side[:, 1:-1, 2:] - side[:, 1:-1, :-2]) * 0.5
    return (grad_x, grad_y, grad_z)


def edge_from(padded):
    grad_x, grad_y, grad_z = central_grads(padded)
    return 1.0 / (1.0 + 6000.0 * (grad_x * grad_x + grad_y * grad_y + grad_z * grad_z))


def weno(first, second, third, fourth, fifth):
    step_one = second - first
    step_two = third - second
    step_three = fourth - third
    step_four = fifth - fourth
    cand_one = 5.0 * step_two - 2.0 * step_one
    cand_two = step_two + 2.0 * step_three
    cand_three = 4.0 * step_three - step_four
    part_a = step_two - step_one
    part_b = 3.0 * step_two - step_one
    smooth_one = 13.0 / 12.0 * part_a * part_a + 0.25 * part_b * part_b
    part_a = step_three - step_two
    part_b = step_two + step_three
    smooth_two = 13.0 / 12.0 * part_a * part_a + 0.25 * part_b * part_b
    part_a = step_four - step_three
    part_b = step_four - 3.0 * step_three
    smooth_three = 13.0 / 12.0 * part_a * part_a + 0.25 * part_b * part_b
    denom_one = 1e-06 + smooth_one
    denom_two = 1e-06 + smooth_two
    denom_three = 1e-06 + smooth_three
    square_one = denom_one * denom_one
    square_two = denom_two * denom_two
    square_three = denom_three * denom_three
    weight_one = square_two * square_three
    weight_two = 6.0 * (square_one * square_three)
    weight_three = 3.0 * (square_one * square_two)
    return third + (weight_one * cand_one + weight_two * cand_two + weight_three * cand_three) / (
        6.0 * (weight_one + weight_two + weight_three)
    )


def upwind(values, slope):
    diffs = [values[k + 1] - values[k] for k in range(6)]
    ahead = slope < 0.0
    chosen = [jnp.where(ahead, diffs[k], diffs[5 - k]) for k in range(5)]
    return slope * weno(*chosen)


SUB = 8
HALO = 3


def stage_kernel(scale_level, scale_step, rows_block, first):
    def kernel(*refs):
        if first:
            low_ref, main_ref, high_ref, wide_ref, ls_ref = refs[:5]
            out_ref, top_ref, bottom_ref, edge_ref, sx_ref, sy_ref, sz_ref = refs[5:12]
            p_ref, e_ref, sems = refs[12:]
            rest = (out_ref, top_ref, bottom_ref, p_ref, sems)
        else:
            low_ref, main_ref, high_ref, edge_ref, sx_ref, sy_ref, sz_ref, ls_ref = refs[:8]
            rest = refs[8:]
            out_ref = rest[0]
            p_ref, sems = rest[-2:]
        rows = main_ref.shape[0]
        rows_y = out_ref.shape[1]
        rows_z = out_ref.shape[2]
        block = pl.program_id(0)
        last = pl.num_programs(0) - 1
        inner = pl.ds(SUB, rows_y)

        blocks = rows // rows_block

        def piece(k):
            return pltpu.make_async_copy(
                main_ref.at[pl.ds(k * rows_block, rows_block)],
                p_ref.at[pl.ds(HALO + k * rows_block, rows_block), inner, :],
                sems.at[k],
            )

        @pl.when(block == 0)
        def _():
            for k in range(blocks):
                piece(k).start()
            zeros = jnp.zeros((SUB, rows_z), jnp.float32)

            def clear(x, carry):
                p_ref[x, pl.ds(0, SUB), :] = zeros
                p_ref[x, pl.ds(SUB + rows_y, SUB), :] = zeros
                return carry

            lax.fori_loop(0, rows + 2 * HALO, clear, 0)
            p_ref[pl.ds(0, HALO), inner, :] = low_ref[...]
            p_ref[pl.ds(HALO + rows, HALO), inner, :] = high_ref[...]
            if first:
                spread = pltpu.make_async_copy(
                    wide_ref, e_ref.at[pl.ds(0, rows + 2), inner, :], sems.at[blocks]
                )
                spread.start()

                def clear_edge(x, carry):
                    e_ref[x, pl.ds(0, SUB), :] = zeros
                    e_ref[x, pl.ds(SUB + rows_y, SUB), :] = zeros
                    return carry

                lax.fori_loop(0, rows + 2, clear_edge, 0)
                spread.wait()
            for k in range(min(blocks, 2)):
                piece(k).wait()

        @pl.when((block >= 1) & (block + 1 < blocks))
        def _():
            piece(block + 1).wait()

        lane = lax.broadcasted_iota(jnp.int32, (SUB, rows_z), 1)

        def along_z(tile, step):
            moved = pltpu.roll(tile, (-step) % rows_z, 1)
            keep = lane < rows_z - step if step > 0 else lane >= -step
            return jnp.where(keep, moved, 0.0)

        def row(r, carry):
            centre_row = block * rows_block + r + HALO
            for chunk in range(rows_y // SUB):
                top = SUB + chunk * SUB

                def at(step_x, step_y):
                    return p_ref[centre_row + step_x, pl.ds(top + step_y, SUB), :]

                centre = at(0, 0)
                line_x = [at(k, 0) for k in range(-HALO, HALO + 1)]
                line_y = [at(0, k) for k in range(-HALO, HALO + 1)]
                line_z = [along_z(centre, k) for k in range(-HALO, HALO + 1)]
                here = pl.ds(chunk * SUB, SUB)
                if first:
                    edge_row = block * rows_block + r + 1

                    def near(step_x, step_y):
                        return e_ref[edge_row + step_x, pl.ds(top + step_y, SUB), :]

                    edge_here = near(0, 0)
                    slope_x = (near(1, 0) - near(-1, 0)) * 0.5
                    slope_y = (near(0, 1) - near(0, -1)) * 0.5
                    slope_z = (along_z(edge_here, 1) - along_z(edge_here, -1)) * 0.5
                    edge_ref[r, here, :] = edge_here
                    sx_ref[r, here, :] = slope_x
                    sy_ref[r, here, :] = slope_y
                    sz_ref[r, here, :] = slope_z
                else:
                    edge_here = edge_ref[r, here, :]
                    slope_x = sx_ref[r, here, :]
                    slope_y = sy_ref[r, here, :]
                    slope_z = sz_ref[r, here, :]
                flow_x = upwind(line_x, slope_x)
                flow_y = upwind(line_y, slope_y)
                flow_z = upwind(line_z, slope_z)
                up_x = line_x[HALO + 1]
                down_x = line_x[HALO - 1]
                up_y = line_y[HALO + 1]
                down_y = line_y[HALO - 1]
                up_z = line_z[HALO + 1]
                down_z = line_z[HALO - 1]
                first_x = up_x - down_x
                first_y = up_y - down_y
                first_z = up_z - down_z
                second_xx = up_x - 2.0 * centre + down_x
                second_yy = up_y - 2.0 * centre + down_y
                second_zz = up_z - 2.0 * centre + down_z
                mixed_xy = at(1, 1) - at(1, -1) - at(-1, 1) + at(-1, -1)
                mixed_xz = along_z(first_x, 1) - along_z(first_x, -1)
                mixed_yz = along_z(first_y, 1) - along_z(first_y, -1)
                square_x = first_x * first_x
                square_y = first_y * first_y
                square_z = first_z * first_z
                numerator = (
                    second_xx * (square_y + square_z)
                    + second_yy * (square_x + square_z)
                    + second_zz * (square_x + square_y)
                )
                numerator = numerator - 0.5 * (
                    first_x * first_y * mixed_xy
                    + first_x * first_z * mixed_xz
                    + first_y * first_z * mixed_yz
                )
                curvature = numerator / (square_x + square_y + square_z + 4.0)
                rate = edge_here * curvature + (flow_x + flow_y + flow_z)
                moved = centre + 0.1 * rate
                if scale_level is None:
                    out_ref[r, here, :] = moved
                else:
                    out_ref[r, here, :] = scale_level * ls_ref[r, here, :] + scale_step * moved
            return carry

        lax.fori_loop(0, rows_block, row, 0)
        if len(rest) > 3:
            top_ref, bottom_ref = rest[1], rest[2]

            @pl.when(block == 0)
            def _():
                top_ref[...] = out_ref[pl.ds(0, HALO)]

            @pl.when(block == last)
            def _():
                bottom_ref[...] = out_ref[pl.ds(rows_block - HALO, HALO)]

    return kernel


def stage(low, field, high, edge, slope, level_set, scale_level, scale_step, sides):
    rows, rows_y, rows_z = level_set.shape
    rows_block = SUB if rows % SUB == 0 else rows
    raw = pl.BlockSpec(memory_space=pl.ANY)
    part = pl.BlockSpec((rows_block, rows_y, rows_z), lambda i: (i, 0, 0))
    side = pl.BlockSpec((HALO, rows_y, rows_z), lambda i: (0, 0, 0))
    result = jax.ShapeDtypeStruct(level_set.shape, level_set.dtype)
    edge_rows = jax.ShapeDtypeStruct((HALO, rows_y, rows_z), level_set.dtype)
    first = slope is None
    scratch = [pltpu.VMEM((rows + 2 * HALO, rows_y + 2 * SUB, rows_z), jnp.float32)]
    if first:
        scratch.append(pltpu.VMEM((rows + 2, rows_y + 2 * SUB, rows_z), jnp.float32))
        in_specs = [side, raw, side, raw, part]
        operands = (low, field, high, edge, level_set)
        out_specs = [part, side, side, part, part, part, part]
        out_shape = [result, edge_rows, edge_rows, result, result, result, result]
    else:
        in_specs = [side, raw, side, part, part, part, part, part]
        operands = (low, field, high, edge, slope[0], slope[1], slope[2], level_set)
        out_specs = [part, side, side] if sides else part
        out_shape = [result, edge_rows, edge_rows] if sides else result
    return pl.pallas_call(
        stage_kernel(scale_level, scale_step, rows_block, first),
        grid=(rows // rows_block,),
        in_specs=in_specs,
        out_specs=out_specs,
        out_shape=out_shape,
        scratch_shapes=scratch + [pltpu.SemaphoreType.DMA((rows // rows_block + 1,))],
        compiler_params=pltpu.CompilerParams(dimension_semantics=("arbitrary",)),
    )(*operands)


def shards(volume, level_set):
    rows, rows_y, rows_z = volume.shape
    exact = lax.Precision.HIGHEST
    halo = min(rows, RADIUS + 2)
    low = shifted(volume[rows - halo :], "gx", 1)
    high = shifted(volume[:halo], "gx", -1)
    extended = jnp.concatenate([low, volume, high], axis=0)
    wide = rows + 4
    blurred = jnp.dot(
        band(wide, extended.shape[0], halo - 2),
        extended.reshape(extended.shape[0], rows_y * rows_z),
        precision=exact,
    )
    blurred = jnp.dot(
        blurred.reshape(wide * rows_y, rows_z), band(rows_z, rows_z, 0).T, precision=exact
    ).reshape(wide, rows_y, rows_z)
    blurred = jnp.einsum("yv,xvz->xyz", band(rows_y, rows_y, 0), blurred, precision=exact)
    positions = lax.axis_index("gx") * rows - 2 + jnp.arange(wide, dtype=jnp.int32)
    inside = (positions >= 0) & (positions < rows * lax.axis_size("gx"))
    blurred = jnp.where(inside[:, None, None], blurred, 0.0)
    edge_wide = edge_from(blurred)
    edge_wide = jnp.where(inside[1:-1, None, None], edge_wide, 0.0)

    def step(field, top, bottom, scale_level, scale_step, sides=True):
        low = shifted(bottom, "gx", 1)
        high = shifted(top, "gx", -1)
        return stage(low, field, high, edge, slope, level_set, scale_level, scale_step, sides)

    low = shifted(level_set[rows - HALO :], "gx", 1)
    high = shifted(level_set[:HALO], "gx", -1)
    section_one, top, bottom, edge, *slope = stage(
        low, level_set, high, edge_wide, None, level_set, None, None, True
    )
    section_two, top, bottom = step(section_one, top, bottom, 0.75, 0.25)
    advanced = step(section_two, top, bottom, 1.0 / 3.0, 2.0 / 3.0, sides=False)
    return (edge, advanced)


def solution(mesh):
    return jax.shard_map(
        shards,
        mesh=mesh,
        in_specs=(P(("grp", "gx"), None, None), P(("grp", "gx"), None, None)),
        out_specs=(P(("grp", "gx"), None, None), P(("grp", "gx"), None, None)),
        check_vma=False,
    )
```

```python
import math

import numpy as np

import jax
import jax.numpy as jnp
from jax import lax
from jax.experimental import pallas as pl
from jax.experimental.pallas import tpu as pltpu
from jax.sharding import PartitionSpec as P

RADIUS = 12


def shifted(block, axis, distance):
    devices = range(lax.axis_size(axis))
    route = [(i - distance, i) for i in devices if i - distance in devices]
    return lax.ppermute(block, axis, route)


def extended_2(block, sides, width):
    for axis, dim in sides:
        count = lax.axis_size(axis)
        forward = [(i, i + 1) for i in range(count - 1)]
        backward = [(target, source) for source, target in forward]
        low = lax.ppermute(
            lax.slice_in_dim(block, block.shape[dim] - width, None, axis=dim), axis, forward
        )
        high = lax.ppermute(lax.slice_in_dim(block, 0, width, axis=dim), axis, backward)
        block = jnp.concatenate([low, block, high], axis=dim)
    return block


def blur_taps():
    raw = [math.exp(-(offset * offset) / 18.0) for offset in range(-RADIUS, RADIUS + 1)]
    total = sum(raw)
    return [value / total for value in raw]


def band(rows, cols, shift):
    taps = blur_taps()
    table = np.zeros((rows, cols), np.float32)
    for i in range(rows):
        for k in range(-RADIUS, RADIUS + 1):
            j = i + shift + k
            if 0 <= j < cols:
                table[i, j] = taps[k + RADIUS]
    return jnp.asarray(table)


def pad_axis(array, axis, width):
    widths = [(0, 0), (0, 0), (0, 0)]
    widths[axis] = (width, width)
    return jnp.pad(array, widths)


def blur_padded(padded, axis, count):
    taps = blur_taps()
    result = taps[0] * lax.slice_in_dim(padded, 0, count, axis=axis)
    for offset in range(1, len(taps)):
        result = result + taps[offset] * lax.slice_in_dim(padded, offset, offset + count, axis=axis)
    return result


def central_grads(padded):
    inner = padded[1:-1]
    side = jnp.pad(inner, ((0, 0), (1, 1), (1, 1)))
    grad_x = (padded[2:] - padded[:-2]) * 0.5
    grad_y = (side[:, 2:, 1:-1] - side[:, :-2, 1:-1]) * 0.5
    grad_z = (side[:, 1:-1, 2:] - side[:, 1:-1, :-2]) * 0.5
    return (grad_x, grad_y, grad_z)


def edge_from(padded):
    grad_x, grad_y, grad_z = central_grads(padded)
    return 1.0 / (1.0 + 6000.0 * (grad_x * grad_x + grad_y * grad_y + grad_z * grad_z))


def weno(first, second, third, fourth, fifth):
    step_one = second - first
    step_two = third - second
    step_three = fourth - third
    step_four = fifth - fourth
    cand_one = 5.0 * step_two - 2.0 * step_one
    cand_two = step_two + 2.0 * step_three
    cand_three = 4.0 * step_three - step_four
    part_a = step_two - step_one
    part_b = 3.0 * step_two - step_one
    smooth_one = 13.0 / 12.0 * part_a * part_a + 0.25 * part_b * part_b
    part_a = step_three - step_two
    part_b = step_two + step_three
    smooth_two = 13.0 / 12.0 * part_a * part_a + 0.25 * part_b * part_b
    part_a = step_four - step_three
    part_b = step_four - 3.0 * step_three
    smooth_three = 13.0 / 12.0 * part_a * part_a + 0.25 * part_b * part_b
    denom_one = 1e-06 + smooth_one
    denom_two = 1e-06 + smooth_two
    denom_three = 1e-06 + smooth_three
    square_one = denom_one * denom_one
    square_two = denom_two * denom_two
    square_three = denom_three * denom_three
    weight_one = square_two * square_three
    weight_two = 6.0 * (square_one * square_three)
    weight_three = 3.0 * (square_one * square_two)
    return third + (weight_one * cand_one + weight_two * cand_two + weight_three * cand_three) / (
        6.0 * (weight_one + weight_two + weight_three)
    )


def upwind(values, slope):
    diffs = [values[k + 1] - values[k] for k in range(6)]
    ahead = slope < 0.0
    chosen = [jnp.where(ahead, diffs[k], diffs[5 - k]) for k in range(5)]
    return slope * weno(*chosen)


SUB = 8
HALO = 3


def stage_kernel(scale_level, scale_step, rows_block, first):
    def kernel(*refs):
        if first:
            low_ref, main_ref, high_ref, wide_ref, ls_ref = refs[:5]
            out_ref, top_ref, bottom_ref, edge_ref, sx_ref, sy_ref, sz_ref = refs[5:12]
            p_ref, e_ref, sems = refs[12:]
            rest = (out_ref, top_ref, bottom_ref, p_ref, sems)
        else:
            low_ref, main_ref, high_ref, edge_ref, sx_ref, sy_ref, sz_ref, ls_ref = refs[:8]
            rest = refs[8:]
            out_ref = rest[0]
            p_ref, sems = rest[-2:]
        rows = main_ref.shape[0]
        rows_y = out_ref.shape[1]
        rows_z = out_ref.shape[2]
        block = pl.program_id(0)
        last = pl.num_programs(0) - 1
        inner = pl.ds(SUB, rows_y)

        blocks = rows // rows_block

        def piece(k):
            return pltpu.make_async_copy(
                main_ref.at[pl.ds(k * rows_block, rows_block)],
                p_ref.at[pl.ds(HALO + k * rows_block, rows_block), inner, :],
                sems.at[k],
            )

        @pl.when(block == 0)
        def _():
            for k in range(blocks):
                piece(k).start()
            zeros = jnp.zeros((SUB, rows_z), jnp.float32)

            def clear(x, carry):
                p_ref[x, pl.ds(0, SUB), :] = zeros
                p_ref[x, pl.ds(SUB + rows_y, SUB), :] = zeros
                return carry

            lax.fori_loop(0, rows + 2 * HALO, clear, 0)
            p_ref[pl.ds(0, HALO), inner, :] = low_ref[...]
            p_ref[pl.ds(HALO + rows, HALO), inner, :] = high_ref[...]
            if first:
                spread = pltpu.make_async_copy(
                    wide_ref, e_ref.at[pl.ds(0, rows + 2), inner, :], sems.at[blocks]
                )
                spread.start()

                def clear_edge(x, carry):
                    e_ref[x, pl.ds(0, SUB), :] = zeros
                    e_ref[x, pl.ds(SUB + rows_y, SUB), :] = zeros
                    return carry

                lax.fori_loop(0, rows + 2, clear_edge, 0)
                spread.wait()
            for k in range(min(blocks, 2)):
                piece(k).wait()

        @pl.when((block >= 1) & (block + 1 < blocks))
        def _():
            piece(block + 1).wait()

        lane = lax.broadcasted_iota(jnp.int32, (SUB, rows_z), 1)

        def along_z(tile, step):
            moved = pltpu.roll(tile, (-step) % rows_z, 1)
            keep = lane < rows_z - step if step > 0 else lane >= -step
            return jnp.where(keep, moved, 0.0)

        def row(r, carry):
            centre_row = block * rows_block + r + HALO
            for chunk in range(rows_y // SUB):
                top = SUB + chunk * SUB

                def at(step_x, step_y):
                    return p_ref[centre_row + step_x, pl.ds(top + step_y, SUB), :]

                centre = at(0, 0)
                line_x = [at(k, 0) for k in range(-HALO, HALO + 1)]
                line_y = [at(0, k) for k in range(-HALO, HALO + 1)]
                line_z = [along_z(centre, k) for k in range(-HALO, HALO + 1)]
                here = pl.ds(chunk * SUB, SUB)
                if first:
                    edge_row = block * rows_block + r + 1

                    def near(step_x, step_y):
                        return e_ref[edge_row + step_x, pl.ds(top + step_y, SUB), :]

                    edge_here = near(0, 0)
                    slope_x = (near(1, 0) - near(-1, 0)) * 0.5
                    slope_y = (near(0, 1) - near(0, -1)) * 0.5
                    slope_z = (along_z(edge_here, 1) - along_z(edge_here, -1)) * 0.5
                    edge_ref[r, here, :] = edge_here
                    sx_ref[r, here, :] = slope_x
                    sy_ref[r, here, :] = slope_y
                    sz_ref[r, here, :] = slope_z
                else:
                    edge_here = edge_ref[r, here, :]
                    slope_x = sx_ref[r, here, :]
                    slope_y = sy_ref[r, here, :]
                    slope_z = sz_ref[r, here, :]
                flow_x = upwind(line_x, slope_x)
                flow_y = upwind(line_y, slope_y)
                flow_z = upwind(line_z, slope_z)
                up_x = line_x[HALO + 1]
                down_x = line_x[HALO - 1]
                up_y = line_y[HALO + 1]
                down_y = line_y[HALO - 1]
                up_z = line_z[HALO + 1]
                down_z = line_z[HALO - 1]
                first_x = up_x - down_x
                first_y = up_y - down_y
                first_z = up_z - down_z
                second_xx = up_x - 2.0 * centre + down_x
                second_yy = up_y - 2.0 * centre + down_y
                second_zz = up_z - 2.0 * centre + down_z
                mixed_xy = at(1, 1) - at(1, -1) - at(-1, 1) + at(-1, -1)
                mixed_xz = along_z(first_x, 1) - along_z(first_x, -1)
                mixed_yz = along_z(first_y, 1) - along_z(first_y, -1)
                square_x = first_x * first_x
                square_y = first_y * first_y
                square_z = first_z * first_z
                numerator = (
                    second_xx * (square_y + square_z)
                    + second_yy * (square_x + square_z)
                    + second_zz * (square_x + square_y)
                )
                numerator = numerator - 0.5 * (
                    first_x * first_y * mixed_xy
                    + first_x * first_z * mixed_xz
                    + first_y * first_z * mixed_yz
                )
                curvature = numerator / (square_x + square_y + square_z + 4.0)
                rate = edge_here * curvature + (flow_x + flow_y + flow_z)
                moved = centre + 0.1 * rate
                if scale_level is None:
                    out_ref[r, here, :] = moved
                else:
                    out_ref[r, here, :] = scale_level * ls_ref[r, here, :] + scale_step * moved
            return carry

        lax.fori_loop(0, rows_block, row, 0)
        if len(rest) > 3:
            top_ref, bottom_ref = rest[1], rest[2]

            @pl.when(block == 0)
            def _():
                top_ref[...] = out_ref[pl.ds(0, HALO)]

            @pl.when(block == last)
            def _():
                bottom_ref[...] = out_ref[pl.ds(rows_block - HALO, HALO)]

    return kernel


def stage(low, field, high, edge, slope, level_set, scale_level, scale_step, sides):
    rows, rows_y, rows_z = level_set.shape
    rows_block = SUB if rows % SUB == 0 else rows
    raw = pl.BlockSpec(memory_space=pl.ANY)
    part = pl.BlockSpec((rows_block, rows_y, rows_z), lambda i: (i, 0, 0))
    side = pl.BlockSpec((HALO, rows_y, rows_z), lambda i: (0, 0, 0))
    result = jax.ShapeDtypeStruct(level_set.shape, level_set.dtype)
    edge_rows = jax.ShapeDtypeStruct((HALO, rows_y, rows_z), level_set.dtype)
    first = slope is None
    scratch = [pltpu.VMEM((rows + 2 * HALO, rows_y + 2 * SUB, rows_z), jnp.float32)]
    if first:
        scratch.append(pltpu.VMEM((rows + 2, rows_y + 2 * SUB, rows_z), jnp.float32))
        in_specs = [side, raw, side, raw, part]
        operands = (low, field, high, edge, level_set)
        out_specs = [part, side, side, part, part, part, part]
        out_shape = [result, edge_rows, edge_rows, result, result, result, result]
    else:
        in_specs = [side, raw, side, part, part, part, part, part]
        operands = (low, field, high, edge, slope[0], slope[1], slope[2], level_set)
        out_specs = [part, side, side] if sides else part
        out_shape = [result, edge_rows, edge_rows] if sides else result
    return pl.pallas_call(
        stage_kernel(scale_level, scale_step, rows_block, first),
        grid=(rows // rows_block,),
        in_specs=in_specs,
        out_specs=out_specs,
        out_shape=out_shape,
        scratch_shapes=scratch + [pltpu.SemaphoreType.DMA((rows // rows_block + 1,))],
        compiler_params=pltpu.CompilerParams(dimension_semantics=("arbitrary",)),
    )(*operands)


def ends_kernel(count):
    def kernel(volume_ref, bottom_ref, top_ref, sems):
        rows = volume_ref.shape[0]
        copies = [
            pltpu.make_async_copy(volume_ref.at[pl.ds(rows - count, count)], bottom_ref, sems.at[0]),
            pltpu.make_async_copy(volume_ref.at[pl.ds(0, count)], top_ref, sems.at[1]),
        ]
        for copy in copies:
            copy.start()
        for copy in copies:
            copy.wait()

    return kernel


def ends(volume, count):
    shape = jax.ShapeDtypeStruct((count,) + volume.shape[1:], volume.dtype)
    raw = pl.BlockSpec(memory_space=pl.ANY)
    return pl.pallas_call(
        ends_kernel(count),
        in_specs=[raw],
        out_specs=[raw, raw],
        out_shape=[shape, shape],
        scratch_shapes=[pltpu.SemaphoreType.DMA((2,))],
    )(volume)


def shards(volume, level_set):
    rows, rows_y, rows_z = volume.shape
    exact = lax.Precision.HIGHEST
    halo = min(rows, RADIUS + 2)
    bottom_rows, top_rows = ends(volume, halo)
    low = shifted(bottom_rows, "gx", 1)
    high = shifted(top_rows, "gx", -1)
    extended = jnp.concatenate([low, volume, high], axis=0)
    wide = rows + 4
    blurred = jnp.dot(
        band(wide, extended.shape[0], halo - 2),
        extended.reshape(extended.shape[0], rows_y * rows_z),
        precision=exact,
    )
    blurred = jnp.dot(
        blurred.reshape(wide * rows_y, rows_z), band(rows_z, rows_z, 0).T, precision=exact
    ).reshape(wide, rows_y, rows_z)
    blurred = jnp.einsum("yv,xvz->xyz", band(rows_y, rows_y, 0), blurred, precision=exact)
    positions = lax.axis_index("gx") * rows - 2 + jnp.arange(wide, dtype=jnp.int32)
    inside = (positions >= 0) & (positions < rows * lax.axis_size("gx"))
    blurred = jnp.where(inside[:, None, None], blurred, 0.0)
    edge_wide = edge_from(blurred)
    edge_wide = jnp.where(inside[1:-1, None, None], edge_wide, 0.0)

    def step(field, top, bottom, scale_level, scale_step, sides=True):
        low = shifted(bottom, "gx", 1)
        high = shifted(top, "gx", -1)
        return stage(low, field, high, edge, slope, level_set, scale_level, scale_step, sides)

    low = shifted(level_set[rows - HALO :], "gx", 1)
    high = shifted(level_set[:HALO], "gx", -1)
    section_one, top, bottom, edge, *slope = stage(
        low, level_set, high, edge_wide, None, level_set, None, None, True
    )
    section_two, top, bottom = step(section_one, top, bottom, 0.75, 0.25)
    advanced = step(section_two, top, bottom, 1.0 / 3.0, 2.0 / 3.0, sides=False)
    return (edge, advanced)


def solution(mesh):
    return jax.shard_map(
        shards,
        mesh=mesh,
        in_specs=(P(("grp", "gx"), None, None), P(("grp", "gx"), None, None)),
        out_specs=(P(("grp", "gx"), None, None), P(("grp", "gx"), None, None)),
        check_vma=False,
    )
```

```python
import math

import numpy as np

import jax
import jax.numpy as jnp
from jax import lax
from jax.experimental import pallas as pl
from jax.experimental.pallas import tpu as pltpu
from jax.sharding import PartitionSpec as P

RADIUS = 12


def shifted(block, axis, distance):
    devices = range(lax.axis_size(axis))
    route = [(i - distance, i) for i in devices if i - distance in devices]
    return lax.ppermute(block, axis, route)


def extended_2(block, sides, width):
    for axis, dim in sides:
        count = lax.axis_size(axis)
        forward = [(i, i + 1) for i in range(count - 1)]
        backward = [(target, source) for source, target in forward]
        low = lax.ppermute(
            lax.slice_in_dim(block, block.shape[dim] - width, None, axis=dim), axis, forward
        )
        high = lax.ppermute(lax.slice_in_dim(block, 0, width, axis=dim), axis, backward)
        block = jnp.concatenate([low, block, high], axis=dim)
    return block


def blur_taps():
    raw = [math.exp(-(offset * offset) / 18.0) for offset in range(-RADIUS, RADIUS + 1)]
    total = sum(raw)
    return [value / total for value in raw]


def band(rows, cols, shift):
    taps = blur_taps()
    table = np.zeros((rows, cols), np.float32)
    for i in range(rows):
        for k in range(-RADIUS, RADIUS + 1):
            j = i + shift + k
            if 0 <= j < cols:
                table[i, j] = taps[k + RADIUS]
    return jnp.asarray(table)


def pad_axis(array, axis, width):
    widths = [(0, 0), (0, 0), (0, 0)]
    widths[axis] = (width, width)
    return jnp.pad(array, widths)


def blur_padded(padded, axis, count):
    taps = blur_taps()
    result = taps[0] * lax.slice_in_dim(padded, 0, count, axis=axis)
    for offset in range(1, len(taps)):
        result = result + taps[offset] * lax.slice_in_dim(padded, offset, offset + count, axis=axis)
    return result


def central_grads(padded):
    inner = padded[1:-1]
    side = jnp.pad(inner, ((0, 0), (1, 1), (1, 1)))
    grad_x = (padded[2:] - padded[:-2]) * 0.5
    grad_y = (side[:, 2:, 1:-1] - side[:, :-2, 1:-1]) * 0.5
    grad_z = (side[:, 1:-1, 2:] - side[:, 1:-1, :-2]) * 0.5
    return (grad_x, grad_y, grad_z)


def edge_from(padded):
    grad_x, grad_y, grad_z = central_grads(padded)
    return 1.0 / (1.0 + 6000.0 * (grad_x * grad_x + grad_y * grad_y + grad_z * grad_z))


def weno(first, second, third, fourth, fifth):
    step_one = second - first
    step_two = third - second
    step_three = fourth - third
    step_four = fifth - fourth
    cand_one = 5.0 * step_two - 2.0 * step_one
    cand_two = step_two + 2.0 * step_three
    cand_three = 4.0 * step_three - step_four
    part_a = step_two - step_one
    part_b = 3.0 * step_two - step_one
    smooth_one = 13.0 / 12.0 * part_a * part_a + 0.25 * part_b * part_b
    part_a = step_three - step_two
    part_b = step_two + step_three
    smooth_two = 13.0 / 12.0 * part_a * part_a + 0.25 * part_b * part_b
    part_a = step_four - step_three
    part_b = step_four - 3.0 * step_three
    smooth_three = 13.0 / 12.0 * part_a * part_a + 0.25 * part_b * part_b
    denom_one = 1e-06 + smooth_one
    denom_two = 1e-06 + smooth_two
    denom_three = 1e-06 + smooth_three
    square_one = denom_one * denom_one
    square_two = denom_two * denom_two
    square_three = denom_three * denom_three
    weight_one = square_two * square_three
    weight_two = 6.0 * (square_one * square_three)
    weight_three = 3.0 * (square_one * square_two)
    return third + (weight_one * cand_one + weight_two * cand_two + weight_three * cand_three) / (
        6.0 * (weight_one + weight_two + weight_three)
    )


def upwind(values, slope):
    diffs = [values[k + 1] - values[k] for k in range(6)]
    ahead = slope < 0.0
    chosen = [jnp.where(ahead, diffs[k], diffs[5 - k]) for k in range(5)]
    return slope * weno(*chosen)


SUB = 8
HALO = 3


def stage_kernel(scale_level, scale_step, rows_block, first):
    def kernel(*refs):
        if first:
            low_ref, main_ref, high_ref, wide_ref, ls_ref = refs[:5]
            out_ref, top_ref, bottom_ref, edge_ref, sx_ref, sy_ref, sz_ref = refs[5:12]
            p_ref, e_ref, sems = refs[12:]
            rest = (out_ref, top_ref, bottom_ref, p_ref, sems)
        else:
            low_ref, main_ref, high_ref, edge_ref, sx_ref, sy_ref, sz_ref, ls_ref = refs[:8]
            rest = refs[8:]
            out_ref = rest[0]
            p_ref, sems = rest[-2:]
        rows = main_ref.shape[0]
        rows_y = out_ref.shape[1]
        rows_z = out_ref.shape[2]
        block = pl.program_id(0)
        last = pl.num_programs(0) - 1
        inner = pl.ds(SUB, rows_y)

        blocks = rows // rows_block

        def piece(k):
            return pltpu.make_async_copy(
                main_ref.at[pl.ds(k * rows_block, rows_block)],
                p_ref.at[pl.ds(HALO + k * rows_block, rows_block), inner, :],
                sems.at[k],
            )

        @pl.when(block == 0)
        def _():
            for k in range(blocks):
                piece(k).start()
            zeros = jnp.zeros((SUB, rows_z), jnp.float32)

            def clear(x, carry):
                p_ref[x, pl.ds(0, SUB), :] = zeros
                p_ref[x, pl.ds(SUB + rows_y, SUB), :] = zeros
                return carry

            lax.fori_loop(0, rows + 2 * HALO, clear, 0)
            p_ref[pl.ds(0, HALO), inner, :] = low_ref[...]
            p_ref[pl.ds(HALO + rows, HALO), inner, :] = high_ref[...]
            if first:
                spread = pltpu.make_async_copy(
                    wide_ref, e_ref.at[pl.ds(0, rows + 2), inner, :], sems.at[blocks]
                )
                spread.start()

                def clear_edge(x, carry):
                    e_ref[x, pl.ds(0, SUB), :] = zeros
                    e_ref[x, pl.ds(SUB + rows_y, SUB), :] = zeros
                    return carry

                lax.fori_loop(0, rows + 2, clear_edge, 0)
                spread.wait()
            for k in range(min(blocks, 2)):
                piece(k).wait()

        @pl.when((block >= 1) & (block + 1 < blocks))
        def _():
            piece(block + 1).wait()

        lane = lax.broadcasted_iota(jnp.int32, (SUB, rows_z), 1)

        def along_z(tile, step):
            moved = pltpu.roll(tile, (-step) % rows_z, 1)
            keep = lane < rows_z - step if step > 0 else lane >= -step
            return jnp.where(keep, moved, 0.0)

        def row(r, carry):
            centre_row = block * rows_block + r + HALO
            for chunk in range(rows_y // SUB):
                top = SUB + chunk * SUB

                def at(step_x, step_y):
                    return p_ref[centre_row + step_x, pl.ds(top + step_y, SUB), :]

                centre = at(0, 0)
                line_x = [at(k, 0) for k in range(-HALO, HALO + 1)]
                line_y = [at(0, k) for k in range(-HALO, HALO + 1)]
                line_z = [along_z(centre, k) for k in range(-HALO, HALO + 1)]
                here = pl.ds(chunk * SUB, SUB)
                if first:
                    edge_row = block * rows_block + r + 1

                    def near(step_x, step_y):
                        return e_ref[edge_row + step_x, pl.ds(top + step_y, SUB), :]

                    edge_here = near(0, 0)
                    slope_x = (near(1, 0) - near(-1, 0)) * 0.5
                    slope_y = (near(0, 1) - near(0, -1)) * 0.5
                    slope_z = (along_z(edge_here, 1) - along_z(edge_here, -1)) * 0.5
                    edge_ref[r, here, :] = edge_here
                    sx_ref[r, here, :] = slope_x
                    sy_ref[r, here, :] = slope_y
                    sz_ref[r, here, :] = slope_z
                else:
                    edge_here = edge_ref[r, here, :]
                    slope_x = sx_ref[r, here, :]
                    slope_y = sy_ref[r, here, :]
                    slope_z = sz_ref[r, here, :]
                flow_x = upwind(line_x, slope_x)
                flow_y = upwind(line_y, slope_y)
                flow_z = upwind(line_z, slope_z)
                up_x = line_x[HALO + 1]
                down_x = line_x[HALO - 1]
                up_y = line_y[HALO + 1]
                down_y = line_y[HALO - 1]
                up_z = line_z[HALO + 1]
                down_z = line_z[HALO - 1]
                first_x = up_x - down_x
                first_y = up_y - down_y
                first_z = up_z - down_z
                second_xx = up_x - 2.0 * centre + down_x
                second_yy = up_y - 2.0 * centre + down_y
                second_zz = up_z - 2.0 * centre + down_z
                mixed_xy = at(1, 1) - at(1, -1) - at(-1, 1) + at(-1, -1)
                mixed_xz = along_z(first_x, 1) - along_z(first_x, -1)
                mixed_yz = along_z(first_y, 1) - along_z(first_y, -1)
                square_x = first_x * first_x
                square_y = first_y * first_y
                square_z = first_z * first_z
                numerator = (
                    second_xx * (square_y + square_z)
                    + second_yy * (square_x + square_z)
                    + second_zz * (square_x + square_y)
                )
                numerator = numerator - 0.5 * (
                    first_x * first_y * mixed_xy
                    + first_x * first_z * mixed_xz
                    + first_y * first_z * mixed_yz
                )
                curvature = numerator / (square_x + square_y + square_z + 4.0)
                rate = edge_here * curvature + (flow_x + flow_y + flow_z)
                moved = centre + 0.1 * rate
                if scale_level is None:
                    out_ref[r, here, :] = moved
                else:
                    out_ref[r, here, :] = scale_level * ls_ref[r, here, :] + scale_step * moved
            return carry

        lax.fori_loop(0, rows_block, row, 0)
        if len(rest) > 3:
            top_ref, bottom_ref = rest[1], rest[2]

            @pl.when(block == 0)
            def _():
                top_ref[...] = out_ref[pl.ds(0, HALO)]

            @pl.when(block == last)
            def _():
                bottom_ref[...] = out_ref[pl.ds(rows_block - HALO, HALO)]

    return kernel


def stage(low, field, high, edge, slope, level_set, scale_level, scale_step, sides):
    rows, rows_y, rows_z = level_set.shape
    rows_block = SUB if rows % SUB == 0 else rows
    raw = pl.BlockSpec(memory_space=pl.ANY)
    part = pl.BlockSpec((rows_block, rows_y, rows_z), lambda i: (i, 0, 0))
    side = pl.BlockSpec((HALO, rows_y, rows_z), lambda i: (0, 0, 0))
    result = jax.ShapeDtypeStruct(level_set.shape, level_set.dtype)
    edge_rows = jax.ShapeDtypeStruct((HALO, rows_y, rows_z), level_set.dtype)
    first = slope is None
    scratch = [pltpu.VMEM((rows + 2 * HALO, rows_y + 2 * SUB, rows_z), jnp.float32)]
    if first:
        scratch.append(pltpu.VMEM((rows + 2, rows_y + 2 * SUB, rows_z), jnp.float32))
        in_specs = [side, raw, side, raw, part]
        operands = (low, field, high, edge, level_set)
        out_specs = [part, side, side, part, part, part, part]
        out_shape = [result, edge_rows, edge_rows, result, result, result, result]
    else:
        in_specs = [side, raw, side, part, part, part, part, part]
        operands = (low, field, high, edge, slope[0], slope[1], slope[2], level_set)
        out_specs = [part, side, side] if sides else part
        out_shape = [result, edge_rows, edge_rows] if sides else result
    return pl.pallas_call(
        stage_kernel(scale_level, scale_step, rows_block, first),
        grid=(rows // rows_block,),
        in_specs=in_specs,
        out_specs=out_specs,
        out_shape=out_shape,
        scratch_shapes=scratch + [pltpu.SemaphoreType.DMA((rows // rows_block + 1,))],
        compiler_params=pltpu.CompilerParams(
            dimension_semantics=("arbitrary",)
        ),
    )(*operands)


def shards(volume, level_set):
    rows, rows_y, rows_z = volume.shape
    exact = lax.Precision.HIGHEST
    halo = min(rows, RADIUS + 2)
    low = shifted(volume[rows - halo :], "gx", 1)
    high = shifted(volume[:halo], "gx", -1)
    def across(block):
        count = block.shape[0]
        flat = jnp.dot(
            block.reshape(count * rows_y, rows_z), band(rows_z, rows_z, 0).T, precision=exact
        ).reshape(count, rows_y, rows_z)
        return jnp.einsum("yv,xvz->xyz", band(rows_y, rows_y, 0), flat, precision=exact)

    own = across(volume)
    extended = jnp.concatenate([across(low), own, across(high)], axis=0)
    wide = rows + 4
    blurred = jnp.dot(
        band(wide, extended.shape[0], halo - 2),
        extended.reshape(extended.shape[0], rows_y * rows_z),
        precision=exact,
    ).reshape(wide, rows_y, rows_z)
    positions = lax.axis_index("gx") * rows - 2 + jnp.arange(wide, dtype=jnp.int32)
    inside = (positions >= 0) & (positions < rows * lax.axis_size("gx"))
    blurred = jnp.where(inside[:, None, None], blurred, 0.0)
    edge_wide = edge_from(blurred)
    edge_wide = jnp.where(inside[1:-1, None, None], edge_wide, 0.0)

    def step(field, top, bottom, scale_level, scale_step, sides=True):
        low = shifted(bottom, "gx", 1)
        high = shifted(top, "gx", -1)
        return stage(low, field, high, edge, slope, level_set, scale_level, scale_step, sides)

    low = shifted(level_set[rows - HALO :], "gx", 1)
    high = shifted(level_set[:HALO], "gx", -1)
    section_one, top, bottom, edge, *slope = stage(
        low, level_set, high, edge_wide, None, level_set, None, None, True
    )
    section_two, top, bottom = step(section_one, top, bottom, 0.75, 0.25)
    advanced = step(section_two, top, bottom, 1.0 / 3.0, 2.0 / 3.0, sides=False)
    return (edge, advanced)


def solution(mesh):
    return jax.shard_map(
        shards,
        mesh=mesh,
        in_specs=(P(("grp", "gx"), None, None), P(("grp", "gx"), None, None)),
        out_specs=(P(("grp", "gx"), None, None), P(("grp", "gx"), None, None)),
        check_vma=False,
    )
```

```python
import math

import numpy as np

import jax
import jax.numpy as jnp
from jax import lax
from jax.experimental import pallas as pl
from jax.experimental.pallas import tpu as pltpu
from jax.sharding import PartitionSpec as P

RADIUS = 12


def shifted(block, axis, distance):
    devices = range(lax.axis_size(axis))
    route = [(i - distance, i) for i in devices if i - distance in devices]
    return lax.ppermute(block, axis, route)


def extended_2(block, sides, width):
    for axis, dim in sides:
        count = lax.axis_size(axis)
        forward = [(i, i + 1) for i in range(count - 1)]
        backward = [(target, source) for source, target in forward]
        low = lax.ppermute(
            lax.slice_in_dim(block, block.shape[dim] - width, None, axis=dim), axis, forward
        )
        high = lax.ppermute(lax.slice_in_dim(block, 0, width, axis=dim), axis, backward)
        block = jnp.concatenate([low, block, high], axis=dim)
    return block


def blur_taps():
    raw = [math.exp(-(offset * offset) / 18.0) for offset in range(-RADIUS, RADIUS + 1)]
    total = sum(raw)
    return [value / total for value in raw]


def band(rows, cols, shift):
    taps = blur_taps()
    table = np.zeros((rows, cols), np.float32)
    for i in range(rows):
        for k in range(-RADIUS, RADIUS + 1):
            j = i + shift + k
            if 0 <= j < cols:
                table[i, j] = taps[k + RADIUS]
    return jnp.asarray(table)


def pad_axis(array, axis, width):
    widths = [(0, 0), (0, 0), (0, 0)]
    widths[axis] = (width, width)
    return jnp.pad(array, widths)


def blur_padded(padded, axis, count):
    taps = blur_taps()
    result = taps[0] * lax.slice_in_dim(padded, 0, count, axis=axis)
    for offset in range(1, len(taps)):
        result = result + taps[offset] * lax.slice_in_dim(padded, offset, offset + count, axis=axis)
    return result


def central_grads(padded):
    inner = padded[1:-1]
    side = jnp.pad(inner, ((0, 0), (1, 1), (1, 1)))
    grad_x = (padded[2:] - padded[:-2]) * 0.5
    grad_y = (side[:, 2:, 1:-1] - side[:, :-2, 1:-1]) * 0.5
    grad_z = (side[:, 1:-1, 2:] - side[:, 1:-1, :-2]) * 0.5
    return (grad_x, grad_y, grad_z)


def edge_from(padded):
    grad_x, grad_y, grad_z = central_grads(padded)
    return 1.0 / (1.0 + 6000.0 * (grad_x * grad_x + grad_y * grad_y + grad_z * grad_z))


def weno(first, second, third, fourth, fifth):
    step_one = second - first
    step_two = third - second
    step_three = fourth - third
    step_four = fifth - fourth
    cand_one = 5.0 * step_two - 2.0 * step_one
    cand_two = step_two + 2.0 * step_three
    cand_three = 4.0 * step_three - step_four
    part_a = step_two - step_one
    part_b = 3.0 * step_two - step_one
    smooth_one = 13.0 / 12.0 * part_a * part_a + 0.25 * part_b * part_b
    part_a = step_three - step_two
    part_b = step_two + step_three
    smooth_two = 13.0 / 12.0 * part_a * part_a + 0.25 * part_b * part_b
    part_a = step_four - step_three
    part_b = step_four - 3.0 * step_three
    smooth_three = 13.0 / 12.0 * part_a * part_a + 0.25 * part_b * part_b
    denom_one = 1e-06 + smooth_one
    denom_two = 1e-06 + smooth_two
    denom_three = 1e-06 + smooth_three
    square_one = denom_one * denom_one
    square_two = denom_two * denom_two
    square_three = denom_three * denom_three
    weight_one = square_two * square_three
    weight_two = 6.0 * (square_one * square_three)
    weight_three = 3.0 * (square_one * square_two)
    return third + (weight_one * cand_one + weight_two * cand_two + weight_three * cand_three) / (
        6.0 * (weight_one + weight_two + weight_three)
    )


def upwind(values, slope):
    diffs = [values[k + 1] - values[k] for k in range(6)]
    ahead = slope < 0.0
    chosen = [jnp.where(ahead, diffs[k], diffs[5 - k]) for k in range(5)]
    return slope * weno(*chosen)


SUB = 8
HALO = 3


def stage_kernel(scale_level, scale_step, rows_block, first):
    def kernel(*refs):
        if first:
            low_ref, main_ref, high_ref, wide_ref, ls_ref = refs[:5]
            out_ref, top_ref, bottom_ref, edge_ref, sx_ref, sy_ref, sz_ref = refs[5:12]
            p_ref, e_ref, sems = refs[12:]
            rest = (out_ref, top_ref, bottom_ref, p_ref, sems)
        else:
            low_ref, main_ref, high_ref, edge_ref, sx_ref, sy_ref, sz_ref, ls_ref = refs[:8]
            rest = refs[8:]
            out_ref = rest[0]
            p_ref, sems = rest[-2:]
        rows = main_ref.shape[0]
        rows_y = out_ref.shape[1]
        rows_z = out_ref.shape[2]
        block = pl.program_id(0)
        last = pl.num_programs(0) - 1
        inner = pl.ds(SUB, rows_y)

        blocks = rows // rows_block

        def piece(k):
            return pltpu.make_async_copy(
                main_ref.at[pl.ds(k * rows_block, rows_block)],
                p_ref.at[pl.ds(HALO + k * rows_block, rows_block), inner, :],
                sems.at[k],
            )

        def spread(k):
            count = rows_block
            if isinstance(k, int) and k == blocks:
                count = 2
            return pltpu.make_async_copy(
                wide_ref.at[pl.ds(k * rows_block, count)],
                e_ref.at[pl.ds(k * rows_block, count), inner, :],
                sems.at[blocks + k],
            )

        @pl.when(block == 0)
        def _():
            for k in range(blocks):
                piece(k).start()
            zeros = jnp.zeros((SUB, rows_z), jnp.float32)

            def clear(x, carry):
                p_ref[x, pl.ds(0, SUB), :] = zeros
                p_ref[x, pl.ds(SUB + rows_y, SUB), :] = zeros
                return carry

            lax.fori_loop(0, rows + 2 * HALO, clear, 0)
            p_ref[pl.ds(0, HALO), inner, :] = low_ref[...]
            p_ref[pl.ds(HALO + rows, HALO), inner, :] = high_ref[...]
            if first:
                for k in range(blocks + 1):
                    spread(k).start()

                def clear_edge(x, carry):
                    e_ref[x, pl.ds(0, SUB), :] = zeros
                    e_ref[x, pl.ds(SUB + rows_y, SUB), :] = zeros
                    return carry

                lax.fori_loop(0, rows + 2, clear_edge, 0)
                for k in range(2):
                    spread(k).wait()
            for k in range(min(blocks, 2)):
                piece(k).wait()

        @pl.when((block >= 1) & (block + 1 < blocks))
        def _():
            piece(block + 1).wait()

        if first:

            @pl.when((block >= 1) & (block + 1 < blocks))
            def _():
                spread(block + 1).wait()

            @pl.when((block >= 1) & (block + 1 == blocks))
            def _():
                spread(blocks).wait()

        lane = lax.broadcasted_iota(jnp.int32, (SUB, rows_z), 1)

        def along_z(tile, step):
            moved = pltpu.roll(tile, (-step) % rows_z, 1)
            keep = lane < rows_z - step if step > 0 else lane >= -step
            return jnp.where(keep, moved, 0.0)

        def row(r, carry):
            centre_row = block * rows_block + r + HALO
            for chunk in range(rows_y // SUB):
                top = SUB + chunk * SUB

                def at(step_x, step_y):
                    return p_ref[centre_row + step_x, pl.ds(top + step_y, SUB), :]

                centre = at(0, 0)
                line_x = [at(k, 0) for k in range(-HALO, HALO + 1)]
                line_y = [at(0, k) for k in range(-HALO, HALO + 1)]
                line_z = [along_z(centre, k) for k in range(-HALO, HALO + 1)]
                here = pl.ds(chunk * SUB, SUB)
                if first:
                    edge_row = block * rows_block + r + 1

                    def near(step_x, step_y):
                        return e_ref[edge_row + step_x, pl.ds(top + step_y, SUB), :]

                    edge_here = near(0, 0)
                    slope_x = (near(1, 0) - near(-1, 0)) * 0.5
                    slope_y = (near(0, 1) - near(0, -1)) * 0.5
                    slope_z = (along_z(edge_here, 1) - along_z(edge_here, -1)) * 0.5
                    edge_ref[r, here, :] = edge_here
                    sx_ref[r, here, :] = slope_x
                    sy_ref[r, here, :] = slope_y
                    sz_ref[r, here, :] = slope_z
                else:
                    edge_here = edge_ref[r, here, :]
                    slope_x = sx_ref[r, here, :]
                    slope_y = sy_ref[r, here, :]
                    slope_z = sz_ref[r, here, :]
                flow_x = upwind(line_x, slope_x)
                flow_y = upwind(line_y, slope_y)
                flow_z = upwind(line_z, slope_z)
                up_x = line_x[HALO + 1]
                down_x = line_x[HALO - 1]
                up_y = line_y[HALO + 1]
                down_y = line_y[HALO - 1]
                up_z = line_z[HALO + 1]
                down_z = line_z[HALO - 1]
                first_x = up_x - down_x
                first_y = up_y - down_y
                first_z = up_z - down_z
                second_xx = up_x - 2.0 * centre + down_x
                second_yy = up_y - 2.0 * centre + down_y
                second_zz = up_z - 2.0 * centre + down_z
                mixed_xy = at(1, 1) - at(1, -1) - at(-1, 1) + at(-1, -1)
                mixed_xz = along_z(first_x, 1) - along_z(first_x, -1)
                mixed_yz = along_z(first_y, 1) - along_z(first_y, -1)
                square_x = first_x * first_x
                square_y = first_y * first_y
                square_z = first_z * first_z
                numerator = (
                    second_xx * (square_y + square_z)
                    + second_yy * (square_x + square_z)
                    + second_zz * (square_x + square_y)
                )
                numerator = numerator - 0.5 * (
                    first_x * first_y * mixed_xy
                    + first_x * first_z * mixed_xz
                    + first_y * first_z * mixed_yz
                )
                curvature = numerator / (square_x + square_y + square_z + 4.0)
                rate = edge_here * curvature + (flow_x + flow_y + flow_z)
                moved = centre + 0.1 * rate
                if scale_level is None:
                    out_ref[r, here, :] = moved
                else:
                    out_ref[r, here, :] = scale_level * ls_ref[r, here, :] + scale_step * moved
            return carry

        lax.fori_loop(0, rows_block, row, 0)
        if len(rest) > 3:
            top_ref, bottom_ref = rest[1], rest[2]

            @pl.when(block == 0)
            def _():
                top_ref[...] = out_ref[pl.ds(0, HALO)]

            @pl.when(block == last)
            def _():
                bottom_ref[...] = out_ref[pl.ds(rows_block - HALO, HALO)]

    return kernel


def stage(low, field, high, edge, slope, level_set, scale_level, scale_step, sides):
    rows, rows_y, rows_z = level_set.shape
    rows_block = SUB if rows % SUB == 0 else rows
    raw = pl.BlockSpec(memory_space=pl.ANY)
    part = pl.BlockSpec((rows_block, rows_y, rows_z), lambda i: (i, 0, 0))
    side = pl.BlockSpec((HALO, rows_y, rows_z), lambda i: (0, 0, 0))
    result = jax.ShapeDtypeStruct(level_set.shape, level_set.dtype)
    edge_rows = jax.ShapeDtypeStruct((HALO, rows_y, rows_z), level_set.dtype)
    first = slope is None
    scratch = [pltpu.VMEM((rows + 2 * HALO, rows_y + 2 * SUB, rows_z), jnp.float32)]
    if first:
        scratch.append(pltpu.VMEM((rows + 2, rows_y + 2 * SUB, rows_z), jnp.float32))
        in_specs = [side, raw, side, raw, part]
        operands = (low, field, high, edge, level_set)
        out_specs = [part, side, side, part, part, part, part]
        out_shape = [result, edge_rows, edge_rows, result, result, result, result]
    else:
        in_specs = [side, raw, side, part, part, part, part, part]
        operands = (low, field, high, edge, slope[0], slope[1], slope[2], level_set)
        out_specs = [part, side, side] if sides else part
        out_shape = [result, edge_rows, edge_rows] if sides else result
    return pl.pallas_call(
        stage_kernel(scale_level, scale_step, rows_block, first),
        grid=(rows // rows_block,),
        in_specs=in_specs,
        out_specs=out_specs,
        out_shape=out_shape,
        scratch_shapes=scratch + [pltpu.SemaphoreType.DMA((2 * (rows // rows_block) + 1,))],
        compiler_params=pltpu.CompilerParams(
            dimension_semantics=("arbitrary",)
        ),
    )(*operands)


def shards(volume, level_set):
    rows, rows_y, rows_z = volume.shape
    exact = lax.Precision.HIGHEST
    halo = min(rows, RADIUS + 2)
    low = shifted(volume[rows - halo :], "gx", 1)
    high = shifted(volume[:halo], "gx", -1)
    extended = jnp.concatenate([low, volume, high], axis=0)
    wide = rows + 4
    blurred = jnp.dot(
        band(wide, extended.shape[0], halo - 2),
        extended.reshape(extended.shape[0], rows_y * rows_z),
        precision=exact,
    )
    blurred = jnp.dot(
        blurred.reshape(wide * rows_y, rows_z), band(rows_z, rows_z, 0).T, precision=exact
    ).reshape(wide, rows_y, rows_z)
    blurred = jnp.einsum("yv,xvz->xyz", band(rows_y, rows_y, 0), blurred, precision=exact)
    positions = lax.axis_index("gx") * rows - 2 + jnp.arange(wide, dtype=jnp.int32)
    inside = (positions >= 0) & (positions < rows * lax.axis_size("gx"))
    blurred = jnp.where(inside[:, None, None], blurred, 0.0)
    edge_wide = edge_from(blurred)
    edge_wide = jnp.where(inside[1:-1, None, None], edge_wide, 0.0)

    def step(field, top, bottom, scale_level, scale_step, sides=True):
        low = shifted(bottom, "gx", 1)
        high = shifted(top, "gx", -1)
        return stage(low, field, high, edge, slope, level_set, scale_level, scale_step, sides)

    low = shifted(level_set[rows - HALO :], "gx", 1)
    high = shifted(level_set[:HALO], "gx", -1)
    section_one, top, bottom, edge, *slope = stage(
        low, level_set, high, edge_wide, None, level_set, None, None, True
    )
    section_two, top, bottom = step(section_one, top, bottom, 0.75, 0.25)
    advanced = step(section_two, top, bottom, 1.0 / 3.0, 2.0 / 3.0, sides=False)
    return (edge, advanced)


def solution(mesh):
    return jax.shard_map(
        shards,
        mesh=mesh,
        in_specs=(P(("grp", "gx"), None, None), P(("grp", "gx"), None, None)),
        out_specs=(P(("grp", "gx"), None, None), P(("grp", "gx"), None, None)),
        check_vma=False,
    )
```
